128 devices in a mesh: head: 8 (over y, core), blk: 16 (over x, z).
Axes of the slice: x: 4, y: 4, z: 4, core: 2. Of those that a mesh axis runs over, the one named last changes fastest.
Arguments:
- states: bfloat16 [16384, 4096], P('blk', 'head'), may hold values from -6 to 6
- qkv_weight: bfloat16 [3, 4096, 4096], P(None, None, 'head'), may hold values from -1 to 1
- norm_gains: bfloat16 [2, 4096], P(None, 'head'), may hold values from 0.5 to 2
- kv_cache: bfloat16 [2, 640, 64, 4096], P(None, 'blk', None, 'head'), may hold values from -300 to 300
- cached_len: int32 [8], replicated, may hold values from 1 to 4096, as said below
- old_table: int32 [8, 64], replicated, may hold values from -1 to 639, as said below
- new_table: int32 [8, 32], replicated, may hold values from 0 to 639, as said below
Outputs:
- attended: bfloat16 [16384, 4096], P('blk', 'head')
- updated_cache: bfloat16 [2, 640, 64, 4096], P(None, 'blk', None, 'head')
The draws below stay inside these ranges and needn't reach their ends.
Inputs may be any that keep to these rules, and one draw needn't show every extreme that they name: `cached_len`: one request has exactly 4096 cached tokens. old_table[r, b] is d * 40 plus a local slot for the blocks b of request r below the ceiling of cached_len[r] / 64, and -1 beyond; block b of request r lies on blk index d = (o + b) mod 16, where o is the index of its block 0. New block j of request r lies on blk index (p + j // 2) mod 16, where p is the index of its block 0; no slot appears twice in old_table and new_table together.
All inputs are finite; a program needn't handle non-finite values.
Results may differ from the reference program's by a relative error of at most 0.014.
The reference program's roundings to bfloat16 on the way count: a program that leaves them out, or rounds other values in their place, can miss the bound.
Values may be sent and summed in bfloat16 or wider, within the bound.
No kernel may reach another device: no remote copies, remote signals or barrier semaphores. Data moves between devices by JAX's collectives and lax.ppermute only.
A program may use at most 192 MiB of HBM per device.

```python
import math
import jax
import jax.numpy as jnp
from jax import lax

D = 4096
HEADS = 32
HS = 128
TOK_DEV = 1024
REQS = 8
BT = 64
SLOTS = 40
LONG_DEV = 4
BLOCKS_DEV = 12
TOKENS = 16384
NEWR = 2048
GROUP = 2
MAXB = 64
NEWB = 32
POOL = 640
N_BLK = 16


def layout(key):
    base_key = jax.random.fold_in(key, 11)
    key_list = jax.random.split(base_key, 6)
    request_ids = jnp.arange(REQS, dtype=jnp.int32)
    longest = jax.random.randint(key_list[0], (), 0, REQS)
    shares = jax.random.randint(key_list[1], (REQS,), 4, 13)
    shares = jnp.where(request_ids == longest, 0, shares)
    spare_blocks = (BLOCKS_DEV - LONG_DEV) * N_BLK - (REQS - 1)
    portion = spare_blocks * shares // jnp.sum(shares)
    leftover = spare_blocks - jnp.sum(portion)
    receiver = jnp.where(longest == 0, 1, 0)
    portion = portion + jnp.where(request_ids == receiver, leftover, 0)
    block_count = jnp.where(request_ids == longest, MAXB, portion + 1)
    trims = jax.random.randint(key_list[2], (REQS,), 0, BT)
    trims = jnp.where(request_ids == longest, 0, trims)
    cached = block_count * BT - trims
    old_home = jax.random.randint(key_list[3], (REQS,), 0, N_BLK)
    new_home = jax.random.randint(key_list[4], (REQS,), 0, N_BLK)
    slot_scores = jax.random.randint(key_list[5], (N_BLK, SLOTS), 0, 1 << 20) * SLOTS + jnp.arange(SLOTS, dtype=jnp.int32)[None, :]
    slot_order = jnp.argsort(slot_scores, axis=1).astype(jnp.int32)
    devices = jnp.arange(N_BLK, dtype=jnp.int32)
    distance = (devices[None, :] - old_home[:, None]) % N_BLK
    old_counts = (block_count[:, None] - distance + N_BLK - 1) // N_BLK
    old_before = jnp.cumsum(old_counts, axis=0) - old_counts
    old_total = jnp.sum(old_counts, axis=0)
    new_distance = (devices[None, :] - new_home[:, None]) % N_BLK
    new_counts = jnp.where(new_distance < NEWB // 2, 2, 0)
    new_before = jnp.cumsum(new_counts, axis=0) - new_counts
    block_ids = jnp.arange(MAXB, dtype=jnp.int32)
    old_device = (old_home[:, None] + block_ids[None, :]) % N_BLK
    old_rank = old_before[request_ids[:, None], old_device] + block_ids[None, :] // N_BLK
    old_rank = jnp.clip(old_rank, 0, SLOTS - 1)
    old_slot = old_device * SLOTS + slot_order[old_device, old_rank]
    old_table = jnp.where(block_ids[None, :] < block_count[:, None], old_slot, -1).astype(jnp.int32)
    new_ids = jnp.arange(NEWB, dtype=jnp.int32)
    new_device = (new_home[:, None] + new_ids[None, :] // 2) % N_BLK
    new_rank = old_total[new_device] + new_before[request_ids[:, None], new_device] + new_ids[None, :] % 2
    new_table = (new_device * SLOTS + slot_order[new_device, new_rank]).astype(jnp.int32)
    return (cached.astype(jnp.int32), old_table, new_table)


def draw_cached_len(key, part):
    return layout(key)[0]


def draw_old_table(key, part):
    return layout(key)[1]


def draw_new_table(key, part):
    return layout(key)[2]


def draw_qkv_weight(key, part):
    columns = jnp.arange(D, dtype=jnp.int32) // HS
    level = columns.astype(jnp.float32) / (HEADS - 1)
    raw_values = jnp.clip(jax.random.normal(key, (3, D, D), jnp.float32), -6.0, 6.0)
    growth = 3.0 ** (0.5 * level)
    return (raw_values * growth[None, None, :] * D ** (-0.5)).astype(jnp.bfloat16)


def draw_kv_cache(key, part):
    return jnp.clip(jax.random.normal(key, (2, POOL, BT, D), jnp.float32), -6.0, 6.0).astype(jnp.bfloat16)


def steps_of(own_key, shape, pieces, least, largest):
    gain, own = 1.0, jax.random.fold_in(own_key, 6)
    for position, parts in pieces:
        heights = jnp.exp(jax.random.uniform(jax.random.fold_in(own, position), (parts,), jnp.float32, least / len(pieces), largest / len(pieces)))
        gain = gain * jnp.repeat(heights, shape[position] // parts).reshape([-1 if axis == position else 1 for axis in range(len(shape))])
    return gain


def normal_values(key, shape, width, reach, shards=(), kind=jnp.bfloat16):
    level = steps_of(key, shape, shards, -0.22, 0.18) if shards else 1.0
    drawn = jax.random.normal(key, shape, jnp.float32) * width * level
    return jnp.minimum(jnp.maximum(drawn, -reach), reach).astype(kind)


def setup_inputs(seed: int = 0) -> dict:
    streams_of = jax.random.split(jax.random.key(seed), 8)
    return {
        "states": normal_values(streams_of[0], (TOKENS, D), 1.0, 6.0, ((0, 16), (1, 8))),
        "qkv_weight": draw_qkv_weight(jax.random.fold_in(streams_of[7], 71), 0),
        "norm_gains": jnp.clip(jnp.exp(math.log(2.0) - 1.3862944 * jax.random.uniform(streams_of[2], (2, D), jnp.float32) ** steps_of(streams_of[2], (2, D), ((1, 8),), -0.2, 0.2)), 0.5, 2.0).astype(jnp.bfloat16),
        "kv_cache": draw_kv_cache(jax.random.fold_in(streams_of[7], 71), 0),
        "cached_len": draw_cached_len(jax.random.fold_in(streams_of[7], 71), 0),
        "old_table": draw_old_table(jax.random.fold_in(streams_of[7], 71), 0),
        "new_table": draw_new_table(jax.random.fold_in(streams_of[7], 71), 0),
    }


rope_base = 500000.0
norm_eps = 1e-06

def rotate(values, positions, head_size):
    half_size = head_size // 2
    frequency = rope_base ** (-jnp.arange(half_size, dtype=jnp.float32) * 2.0 / head_size)
    angles = positions.astype(jnp.float32)[:, None] * frequency[None, :]
    cosine = jnp.cos(angles)[:, None, :]
    sine_part = jnp.sin(angles)[:, None, :]
    first_half = values[..., :half_size]
    second = values[..., half_size:]
    return jnp.concatenate([first_half * cosine - second * sine_part, second * cosine + first_half * sine_part], axis=-1)

def reference(states, qkv_weight, norm_gains, kv_cache, cached_len, old_table, new_table):
    weight_full = qkv_weight.astype(jnp.float32)
    gains = norm_gains.astype(jnp.float32)
    outputs = []
    fresh_list = []
    score_scale = HS ** (-0.5)
    half_rows = TOK_DEV // 2
    for request in range(REQS):
        rows_raw = states[request * NEWR:(request + 1) * NEWR].astype(jnp.float32)
        split_rows = rows_raw.reshape(GROUP, 2, half_rows, D)
        rows_in = jnp.concatenate([split_rows[:, 0], split_rows[:, 1][::-1]], axis=0).reshape(NEWR, D)
        projected = jnp.einsum('tc,jcw->tjw', rows_in, weight_full)
        queries = projected[:, 0]
        key_new = projected[:, 1]
        value_new = projected[:, 2]
        queries = queries * lax.rsqrt(lax.optimization_barrier(jnp.mean(queries * queries, axis=1, keepdims=True)) + norm_eps) * gains[0]
        key_new = key_new * lax.rsqrt(lax.optimization_barrier(jnp.mean(key_new * key_new, axis=1, keepdims=True)) + norm_eps) * gains[1]
        positions = cached_len[request] + jnp.arange(NEWR, dtype=jnp.int32)
        queries = rotate(queries.reshape(NEWR, HEADS, HS), positions, HS).reshape(NEWR, D).astype(jnp.bfloat16)
        key_new = rotate(key_new.reshape(NEWR, HEADS, HS), positions, HS).reshape(NEWR, D).astype(jnp.bfloat16)
        value_new = value_new.astype(jnp.bfloat16)
        fresh_list.append(jnp.stack([key_new, value_new]))
        safe_slots = jnp.clip(old_table[request], 0, kv_cache.shape[1] - 1).astype(jnp.int32)
        cached = kv_cache[:, safe_slots].reshape(2, MAXB * BT, D)
        key_pos = jnp.arange(MAXB * BT, dtype=jnp.int32)
        cached_mask = jnp.broadcast_to(key_pos[None, :] < cached_len[request], (NEWR, MAXB * BT))
        token_ids = jnp.arange(NEWR, dtype=jnp.int32)
        causal = token_ids[None, :] <= token_ids[:, None]
        full_mask = jnp.concatenate([cached_mask, causal], axis=1)
        all_keys = jnp.concatenate([cached[0], key_new.astype(cached.dtype)], axis=0)
        all_values = jnp.concatenate([cached[1], value_new.astype(cached.dtype)], axis=0)

        def one_head(head_index):
            q_head = lax.dynamic_slice_in_dim(queries, head_index * HS, HS, 1).astype(jnp.float32)
            k_head = lax.dynamic_slice_in_dim(all_keys, head_index * HS, HS, 1).astype(jnp.float32)
            v_head = lax.dynamic_slice_in_dim(all_values, head_index * HS, HS, 1).astype(jnp.float32)
            scores = jnp.einsum('qd,kd->qk', q_head, k_head) * score_scale
            scores = jnp.where(full_mask, scores, -jnp.inf)
            row_max = lax.optimization_barrier(jnp.max(scores, axis=1, keepdims=True))
            weights = jnp.exp(scores - row_max)
            probabilities = (weights / lax.optimization_barrier(jnp.sum(weights, axis=1, keepdims=True))).astype(jnp.bfloat16)
            return jnp.dot(probabilities, v_head.astype(jnp.bfloat16), preferred_element_type=jnp.float32).astype(jnp.bfloat16)
        heads_out = lax.map(one_head, jnp.arange(HEADS, dtype=jnp.int32))
        token_major = jnp.transpose(heads_out, (1, 0, 2)).reshape(2 * GROUP, half_rows, D)
        back_rows = jnp.stack([token_major[:GROUP], token_major[GROUP:][::-1]], axis=1)
        outputs.append(back_rows.reshape(NEWR, D))
    attended = jnp.concatenate(outputs, axis=0)
    fresh_all = jnp.stack(fresh_list, axis=1).reshape(2, REQS * NEWB, BT, D).astype(kv_cache.dtype)
    updated_cache = kv_cache.at[:, new_table.reshape(-1).astype(jnp.int32)].set(fresh_all)
    return (attended, updated_cache)
```

```python
import functools

import jax
import jax.numpy as jnp
from jax import lax
from jax.experimental import pallas as pl
from jax.experimental.pallas import tpu as pltpu
from jax.sharding import PartitionSpec as P

D = 4096
HS = 128


rope_base = 500000.0
norm_eps = 1e-06
score_scale = HS ** (-0.5)


def swapped(block, axis, apart):
    count = lax.axis_size(axis)
    route = []
    for low in range(count):
        high = low | 1 << apart
        if high != low and high < count:
            route += [(low, high), (high, low)]
    return lax.ppermute(block, axis, route)


def rotate(values, positions, head_size):
    half_size = head_size // 2
    frequency = rope_base ** (-jnp.arange(half_size, dtype=jnp.float32) * 2.0 / head_size)
    angles = positions.astype(jnp.float32)[:, None] * frequency[None, :]
    cosine = jnp.cos(angles)[:, None, :]
    sine_part = jnp.sin(angles)[:, None, :]
    first_half = values[..., :half_size]
    second = values[..., half_size:]
    return jnp.concatenate(
        [first_half * cosine - second * sine_part, second * cosine + first_half * sine_part],
        axis=-1,
    )


def online_update(s, v, m_sc, l_sc, acc_sc):
    m_prev = m_sc[...]
    m_cur = jnp.max(s, axis=1, keepdims=True)
    m_next = jnp.maximum(m_prev, m_cur)
    alpha = jnp.exp(m_prev - m_next)
    p = jnp.exp(s - m_next[:, :1])
    l_sc[...] = alpha * l_sc[...] + jnp.sum(p, axis=1, keepdims=True)
    pv = jnp.dot(p.astype(jnp.bfloat16), v, preferred_element_type=jnp.float32)
    acc_sc[...] = acc_sc[...] * alpha + pv
    m_sc[...] = m_next


def scores_of(q, k):
    return (
        lax.dot_general(q, k, (((1,), (1,)), ((), ())), preferred_element_type=jnp.float32)
        * score_scale
    )


def new_kernel(meta_ref, q_ref, k_ref, v_ref, acc_out, m_out, l_out, m_sc, l_sc, acc_sc):
    qi = pl.program_id(1)
    kj = pl.program_id(2)
    member = meta_ref[0]
    q_chunk = jnp.where(qi == 0, member, 3 - member)
    k_chunk = jnp.where(kj == 0, 0, jnp.where(kj == 1, 3, kj - 1))

    @pl.when(kj == 0)
    def _():
        m_sc[...] = jnp.full(m_sc.shape, -jnp.inf, jnp.float32)
        l_sc[...] = jnp.zeros(l_sc.shape, jnp.float32)
        acc_sc[...] = jnp.zeros(acc_sc.shape, jnp.float32)

    @pl.when(k_chunk <= q_chunk)
    def _():
        s = scores_of(q_ref[...], k_ref[...])
        rows = lax.broadcasted_iota(jnp.int32, s.shape, 0)
        cols = lax.broadcasted_iota(jnp.int32, s.shape, 1)
        visible = (k_chunk < q_chunk) | (cols <= rows)
        s = jnp.where(visible, s, -jnp.inf)
        online_update(s, v_ref[...], m_sc, l_sc, acc_sc)

    @pl.when(kj == pl.num_programs(2) - 1)
    def _():
        acc_out[...] = acc_sc[...]
        m_out[...] = m_sc[...]
        l_out[...] = l_sc[...]


def cached_kernel(meta_ref, q_ref, k_ref, v_ref, acc_in, m_in, l_in, o_ref, m_sc, l_sc, acc_sc,
                  *, groups, per_half, block_len):
    c = pl.program_id(1)
    half = pl.program_id(2)
    length = meta_ref[1]
    first = meta_ref[2]
    tile = per_half * block_len

    @pl.when((c == 0) & (half == 0))
    def _():
        m_sc[...] = m_in[...]
        l_sc[...] = l_in[...]
        acc_sc[...] = acc_in[...]

    @pl.when(c * groups * block_len < length)
    def _():
        k = k_ref[...].reshape(tile, HS)
        v = v_ref[...].reshape(tile, HS)
        s = scores_of(q_ref[...], k)
        cols = lax.broadcasted_iota(jnp.int32, (1, tile), 1)
        src = half * per_half + cols // block_len
        block = (src - first + groups) % groups + groups * c
        visible = block * block_len + cols % block_len < length
        s = jnp.where(visible, s, -jnp.inf)
        online_update(s, v, m_sc, l_sc, acc_sc)

    @pl.when((c == pl.num_programs(1) - 1) & (half == pl.num_programs(2) - 1))
    def _():
        o_ref[...] = (acc_sc[...] / l_sc[...]).astype(o_ref.dtype)


def new_attention(meta, queries, keys, values):
    tok_rows, width = queries.shape
    heads = width // HS
    q_rows = tok_rows // 2
    key_rows = keys.shape[0]
    k_tiles = key_rows // q_rows
    state = jax.ShapeDtypeStruct((tok_rows, width), jnp.float32)
    state_spec = pl.BlockSpec((q_rows, HS), lambda h, i, j, meta: (i, h))
    flops = 2 * 2 * tok_rows * key_rows * width
    return pl.pallas_call(
        new_kernel,
        out_shape=(state, state, state),
        grid_spec=pltpu.PrefetchScalarGridSpec(
            num_scalar_prefetch=1,
            grid=(heads, 2, k_tiles),
            in_specs=[
                pl.BlockSpec((q_rows, HS), lambda h, i, j, meta: (i, h)),
                pl.BlockSpec((q_rows, HS), lambda h, i, j, meta: (j, h)),
                pl.BlockSpec((q_rows, HS), lambda h, i, j, meta: (j, h)),
            ],
            out_specs=[state_spec, state_spec, state_spec],
            scratch_shapes=[
                pltpu.VMEM((q_rows, HS), jnp.float32),
                pltpu.VMEM((q_rows, HS), jnp.float32),
                pltpu.VMEM((q_rows, HS), jnp.float32),
            ],
        ),
        compiler_params=pltpu.CompilerParams(
            dimension_semantics=("arbitrary", "arbitrary", "arbitrary")
        ),
        cost_estimate=pl.CostEstimate(
            flops=flops // 2,
            transcendentals=tok_rows * key_rows * heads // 2,
            bytes_accessed=2 * tok_rows * width * 2 + 2 * 2 * key_rows * width + 3 * 4 * tok_rows * width,
        ),
    )(meta, queries, keys, values)


def cached_attention(meta, queries, received, acc, m, l):
    tok_rows, width = queries.shape
    heads = width // HS
    groups, _, per_dev, block_len, _ = received.shape
    per_half = groups // 2

    def kv_map(index):
        def index_map(h, c, half, meta):
            last = (meta[1] + groups * block_len - 1) // (groups * block_len) - 1
            skip = c > last
            return (
                jnp.where(skip, 1, half),
                index,
                jnp.where(skip, last, c),
                0,
                h,
            )

        return index_map

    kv_block = (per_half, None, None, block_len, HS)
    state_spec = pl.BlockSpec((tok_rows, HS), lambda h, c, half, meta: (0, h))
    keys_total = groups * per_dev * block_len
    return pl.pallas_call(
        functools.partial(
            cached_kernel, groups=groups, per_half=per_half, block_len=block_len
        ),
        out_shape=jax.ShapeDtypeStruct((tok_rows, width), jnp.bfloat16),
        grid_spec=pltpu.PrefetchScalarGridSpec(
            num_scalar_prefetch=1,
            grid=(heads, per_dev, 2),
            in_specs=[
                pl.BlockSpec((tok_rows, HS), lambda h, c, half, meta: (0, h)),
                pl.BlockSpec(kv_block, kv_map(0)),
                pl.BlockSpec(kv_block, kv_map(1)),
                state_spec,
                state_spec,
                state_spec,
            ],
            out_specs=pl.BlockSpec((tok_rows, HS), lambda h, c, half, meta: (0, h)),
            scratch_shapes=[
                pltpu.VMEM((tok_rows, HS), jnp.float32),
                pltpu.VMEM((tok_rows, HS), jnp.float32),
                pltpu.VMEM((tok_rows, HS), jnp.float32),
            ],
        ),
        compiler_params=pltpu.CompilerParams(
            dimension_semantics=("arbitrary", "arbitrary", "arbitrary")
        ),
        cost_estimate=pl.CostEstimate(
            flops=2 * 2 * tok_rows * keys_total * width // 2,
            transcendentals=tok_rows * keys_total * heads // 2,
            bytes_accessed=2 * keys_total * width + 2 * tok_rows * width * 2 + 3 * 4 * tok_rows * width,
        ),
    )(meta, queries, received, received, acc, m, l)


def body(states, qkv_weight, norm_gains, kv_cache, cached_len, old_table, new_table):
    tok_rows = states.shape[0]
    half_rows = tok_rows // 2
    local_width = qkv_weight.shape[2]
    local_heads = local_width // HS
    groups = lax.axis_size("blk")
    slot_count = kv_cache.shape[1]
    block_len = kv_cache.shape[2]
    requests = cached_len.shape[0]
    group_size = groups // requests
    per_dev = old_table.shape[1] // groups
    my_index = lax.axis_index("blk")
    request = my_index // group_size
    member = my_index % group_size
    late_block = 2 * group_size - 1 - member
    targets = jnp.arange(groups, dtype=jnp.int32)
    kv_flat = kv_cache.reshape(2 * slot_count, block_len, local_width)

    lengths_blocks = jnp.sum((old_table >= 0).astype(jnp.int32), axis=1)
    first_dev = old_table[:, 0] // slot_count
    target_req = targets // group_size
    c_index = jnp.arange(per_dev, dtype=jnp.int32)
    block_index = ((my_index - first_dev[target_req]) % groups)[:, None] + groups * c_index[None, :]
    slot_index = (
        old_table[target_req[:, None], jnp.clip(block_index, 0, old_table.shape[1] - 1)]
        - my_index * slot_count
    )
    slot_index = jnp.clip(slot_index, 0, slot_count - 1)
    kv_ids = jnp.arange(2, dtype=jnp.int32)
    out_ids = kv_ids[None, :, None] * slot_count + slot_index[:, None, :]
    outgoing = jnp.take(kv_flat, out_ids.reshape(-1), axis=0).reshape(
        groups, 2, per_dev, block_len, local_width
    )
    received = lax.all_to_all(outgoing, "blk", split_axis=0, concat_axis=0, tiled=True)

    projected = jnp.einsum(
        "tc,jcw->tjw",
        lax.all_gather(states, "head", axis=1, tiled=True),
        qkv_weight,
        preferred_element_type=jnp.float32,
    )
    queries = projected[:, 0]
    key_new = projected[:, 1]
    value_new = projected[:, 2]
    query_sq, key_sq = lax.psum(
        (jnp.sum(queries * queries, axis=1), jnp.sum(key_new * key_new, axis=1)), "head"
    )
    gains = norm_gains.astype(jnp.float32)
    queries = queries * lax.rsqrt(query_sq / D + norm_eps)[:, None] * gains[0]
    key_new = key_new * lax.rsqrt(key_sq / D + norm_eps)[:, None] * gains[1]
    half_ids = jnp.arange(half_rows, dtype=jnp.int32)
    token_offset = jnp.concatenate(
        [member * half_rows + half_ids, late_block * half_rows + half_ids]
    )
    positions = cached_len[request] + token_offset
    queries = (
        rotate(queries.reshape(tok_rows, local_heads, HS), positions, HS)
        .reshape(tok_rows, local_width)
        .astype(jnp.bfloat16)
    )
    key_new = (
        rotate(key_new.reshape(tok_rows, local_heads, HS), positions, HS)
        .reshape(tok_rows, local_width)
        .astype(jnp.bfloat16)
    )
    value_new = value_new.astype(jnp.bfloat16)
    fresh_kv = jnp.stack([key_new, value_new])

    blocks_dev = tok_rows // block_len
    half_blocks = blocks_dev // 2
    new_count = new_table.shape[1]
    fresh_flat = fresh_kv.reshape(2 * blocks_dev, block_len, local_width)
    pair_index = jnp.arange(2, dtype=jnp.int32)
    new_home = new_table[:, 0] // slot_count
    wanted_out = 2 * ((targets - new_home[request]) % groups)[:, None] + pair_index[None, :]
    out_half = wanted_out // half_blocks
    local_index = jnp.where(
        out_half == member,
        wanted_out - member * half_blocks,
        wanted_out - late_block * half_blocks + half_blocks,
    )
    local_index = jnp.clip(local_index, 0, blocks_dev - 1)
    pick_ids = kv_ids[None, :, None] * blocks_dev + local_index[:, None, :]
    picked = jnp.take(fresh_flat, pick_ids.reshape(-1), axis=0).reshape(
        groups, 2, 2, block_len, local_width
    )
    arrived = lax.all_to_all(picked, "blk", split_axis=0, concat_axis=0, tiled=True)
    source_req = targets // group_size
    source_member = targets % group_size
    source_late = 2 * group_size - 1 - source_member
    wanted_in = 2 * ((my_index - new_home[source_req]) % groups)[:, None] + pair_index[None, :]
    in_half = wanted_in // half_blocks
    valid_in = (in_half == source_member[:, None]) | (in_half == source_late[:, None])
    target_slot = (
        new_table[source_req[:, None], jnp.clip(wanted_in, 0, new_count - 1)]
        - my_index * slot_count
    )
    target_ids = kv_ids[None, :, None] * slot_count + target_slot[:, None, :]
    target_ids = jnp.where(valid_in[:, None, :], target_ids, 2 * slot_count)
    updated_cache = (
        kv_flat.at[target_ids.reshape(-1)]
        .set(arrived.reshape(groups * 4, block_len, local_width), mode="drop")
        .reshape(kv_cache.shape)
    )

    collected = fresh_kv
    partner_new = swapped(collected, "blk", 0)
    lower_new = member // 2**0 % 2 == 0
    collected = jnp.where(
        lower_new,
        jnp.concatenate([collected, partner_new], axis=1),
        jnp.concatenate([partner_new, collected], axis=1),
    )
    meta = jnp.stack([member, cached_len[request], first_dev[request], 0]).astype(jnp.int32)
    acc, m, l = new_attention(meta, queries, collected[0], collected[1])
    attended = cached_attention(meta, queries, received, acc, m, l)
    return (attended, updated_cache)


def solution(mesh):
    return jax.shard_map(
        body,
        mesh=mesh,
        in_specs=(
            P("blk", "head"),
            P(None, None, "head"),
            P(None, "head"),
            P(None, "blk", None, "head"),
            P(),
            P(),
            P(),
        ),
        out_specs=(P("blk", "head"), P(None, "blk", None, "head")),
        check_vma=False,
    )
```

```python
import functools

import jax
import jax.numpy as jnp
from jax import lax
from jax.experimental import pallas as pl
from jax.experimental.pallas import tpu as pltpu
from jax.sharding import PartitionSpec as P


D = 4096
HS = 128


rope_base = 500000.0
norm_eps = 1e-06
score_scale = HS ** (-0.5)


def swapped(block, axis, apart):
    count = lax.axis_size(axis)
    route = []
    for low in range(count):
        high = low | 1 << apart
        if high != low and high < count:
            route += [(low, high), (high, low)]
    return lax.ppermute(block, axis, route)


def rotate(values, positions, head_size):
    half_size = head_size // 2
    frequency = rope_base ** (-jnp.arange(half_size, dtype=jnp.float32) * 2.0 / head_size)
    angles = positions.astype(jnp.float32)[:, None] * frequency[None, :]
    cosine = jnp.cos(angles)[:, None, :]
    sine_part = jnp.sin(angles)[:, None, :]
    first_half = values[..., :half_size]
    second = values[..., half_size:]
    return jnp.concatenate(
        [first_half * cosine - second * sine_part, second * cosine + first_half * sine_part],
        axis=-1,
    )


def online_update(s, v, m_sc, l_sc, acc_sc):
    m_prev = m_sc[...]
    m_cur = jnp.max(s, axis=1, keepdims=True) * score_scale
    m_next = jnp.maximum(m_prev, m_cur)
    alpha = jnp.exp(m_prev - m_next)
    p = jnp.exp(s * score_scale - m_next[:, :1])
    l_sc[...] = alpha * l_sc[...] + jnp.sum(p, axis=1, keepdims=True)
    pv = jnp.dot(p.astype(jnp.bfloat16), v, preferred_element_type=jnp.float32)
    acc_sc[...] = acc_sc[...] * alpha + pv
    m_sc[...] = m_next


def scores_of(q, k):
    return lax.dot_general(q, k, (((1,), (1,)), ((), ())), preferred_element_type=jnp.float32)


def new_kernel(meta_ref, q_ref, k_ref, v_ref, acc_out, m_out, l_out, m_sc, l_sc, acc_sc):
    qi = pl.program_id(1)
    kj = pl.program_id(2)
    member = meta_ref[0]
    q_chunk = jnp.where(qi == 0, member, 3 - member)
    k_chunk = jnp.where(kj == 0, 0, jnp.where(kj == 1, 3, kj - 1))

    @pl.when(kj == 0)
    def _():
        m_sc[...] = jnp.full(m_sc.shape, -jnp.inf, jnp.float32)
        l_sc[...] = jnp.zeros(l_sc.shape, jnp.float32)
        acc_sc[...] = jnp.zeros(acc_sc.shape, jnp.float32)

    @pl.when(k_chunk < q_chunk)
    def _():
        s = scores_of(q_ref[...], k_ref[...])
        online_update(s, v_ref[...], m_sc, l_sc, acc_sc)

    @pl.when(k_chunk == q_chunk)
    def _():
        s = scores_of(q_ref[...], k_ref[...])
        rows = lax.broadcasted_iota(jnp.int32, s.shape, 0)
        cols = lax.broadcasted_iota(jnp.int32, s.shape, 1)
        s = jnp.where(cols <= rows, s, -jnp.inf)
        online_update(s, v_ref[...], m_sc, l_sc, acc_sc)

    @pl.when(kj == pl.num_programs(2) - 1)
    def _():
        acc_out[...] = acc_sc[...]
        m_out[...] = m_sc[...]
        l_out[...] = l_sc[...]


def cached_kernel(meta_ref, q_ref, k_ref, v_ref, acc_in, m_in, l_in, o_ref, m_sc, l_sc, acc_sc,
                  *, groups, per_half, block_len):
    c = pl.program_id(1)
    half = pl.program_id(2)
    length = meta_ref[1]
    first = meta_ref[2]
    tile = per_half * block_len

    @pl.when((c == 0) & (half == 0))
    def _():
        m_sc[...] = m_in[...]
        l_sc[...] = l_in[...]
        acc_sc[...] = acc_in[...]

    @pl.when((c + 1) * groups * block_len <= length)
    def _():
        k = k_ref[...].reshape(tile, HS)
        v = v_ref[...].reshape(tile, HS)
        s = scores_of(q_ref[...], k)
        online_update(s, v, m_sc, l_sc, acc_sc)

    @pl.when((c * groups * block_len < length) & ((c + 1) * groups * block_len > length))
    def _():
        k = k_ref[...].reshape(tile, HS)
        v = v_ref[...].reshape(tile, HS)
        s = scores_of(q_ref[...], k)
        cols = lax.broadcasted_iota(jnp.int32, (1, tile), 1)
        src = half * per_half + cols // block_len
        block = (src - first + groups) % groups + groups * c
        visible = block * block_len + cols % block_len < length
        s = jnp.where(visible, s, -jnp.inf)
        online_update(s, v, m_sc, l_sc, acc_sc)

    @pl.when((c == pl.num_programs(1) - 1) & (half == pl.num_programs(2) - 1))
    def _():
        o_ref[...] = (acc_sc[...] / l_sc[...]).astype(o_ref.dtype)


def new_attention(meta, queries, keys, values):
    tok_rows, width = queries.shape
    heads = width // HS
    q_rows = tok_rows // 2
    key_rows = keys.shape[0]
    k_tiles = key_rows // q_rows
    state = jax.ShapeDtypeStruct((tok_rows, width), jnp.float32)
    state_spec = pl.BlockSpec((q_rows, HS), lambda h, i, j, meta: (i, h))
    flops = 2 * 2 * tok_rows * key_rows * width
    return pl.pallas_call(
        new_kernel,
        out_shape=(state, state, state),
        grid_spec=pltpu.PrefetchScalarGridSpec(
            num_scalar_prefetch=1,
            grid=(heads, 2, k_tiles),
            in_specs=[
                pl.BlockSpec((q_rows, HS), lambda h, i, j, meta: (i, h)),
                pl.BlockSpec((q_rows, HS), lambda h, i, j, meta: (j, h)),
                pl.BlockSpec((q_rows, HS), lambda h, i, j, meta: (j, h)),
            ],
            out_specs=[state_spec, state_spec, state_spec],
            scratch_shapes=[
                pltpu.VMEM((q_rows, HS), jnp.float32),
                pltpu.VMEM((q_rows, HS), jnp.float32),
                pltpu.VMEM((q_rows, HS), jnp.float32),
            ],
        ),
        compiler_params=pltpu.CompilerParams(
            dimension_semantics=("arbitrary", "arbitrary", "arbitrary")
        ),
        cost_estimate=pl.CostEstimate(
            flops=flops // 2,
            transcendentals=tok_rows * key_rows * heads // 2,
            bytes_accessed=2 * tok_rows * width * 2 + 2 * 2 * key_rows * width + 3 * 4 * tok_rows * width,
        ),
    )(meta, queries, keys, values)


def cached_attention(meta, queries, received, acc, m, l):
    tok_rows, width = queries.shape
    heads = width // HS
    groups, _, per_dev, block_len, _ = received.shape
    per_half = groups // 2

    def kv_map(index):
        def index_map(h, c, half, meta):
            last = (meta[1] + groups * block_len - 1) // (groups * block_len) - 1
            skip = c > last
            return (
                jnp.where(skip, 1, half),
                index,
                jnp.where(skip, last, c),
                0,
                h,
            )

        return index_map

    kv_block = (per_half, None, None, block_len, HS)
    state_spec = pl.BlockSpec((tok_rows, HS), lambda h, c, half, meta: (0, h))
    keys_total = groups * per_dev * block_len
    return pl.pallas_call(
        functools.partial(
            cached_kernel, groups=groups, per_half=per_half, block_len=block_len
        ),
        out_shape=jax.ShapeDtypeStruct((tok_rows, width), jnp.bfloat16),
        grid_spec=pltpu.PrefetchScalarGridSpec(
            num_scalar_prefetch=1,
            grid=(heads, per_dev, 2),
            in_specs=[
                pl.BlockSpec((tok_rows, HS), lambda h, c, half, meta: (0, h)),
                pl.BlockSpec(kv_block, kv_map(0)),
                pl.BlockSpec(kv_block, kv_map(1)),
                state_spec,
                state_spec,
                state_spec,
            ],
            out_specs=pl.BlockSpec((tok_rows, HS), lambda h, c, half, meta: (0, h)),
            scratch_shapes=[
                pltpu.VMEM((tok_rows, HS), jnp.float32),
                pltpu.VMEM((tok_rows, HS), jnp.float32),
                pltpu.VMEM((tok_rows, HS), jnp.float32),
            ],
        ),
        compiler_params=pltpu.CompilerParams(
            dimension_semantics=("arbitrary", "arbitrary", "arbitrary")
        ),
        cost_estimate=pl.CostEstimate(
            flops=2 * 2 * tok_rows * keys_total * width // 2,
            transcendentals=tok_rows * keys_total * heads // 2,
            bytes_accessed=2 * keys_total * width + 2 * tok_rows * width * 2 + 3 * 4 * tok_rows * width,
        ),
    )(meta, queries, received, received, acc, m, l)


def body(states, qkv_weight, norm_gains, kv_cache, cached_len, old_table, new_table):
    tok_rows = states.shape[0]
    half_rows = tok_rows // 2
    local_width = qkv_weight.shape[2]
    local_heads = local_width // HS
    groups = lax.axis_size("blk")
    slot_count = kv_cache.shape[1]
    block_len = kv_cache.shape[2]
    requests = cached_len.shape[0]
    group_size = groups // requests
    per_dev = old_table.shape[1] // groups
    my_index = lax.axis_index("blk")
    request = my_index // group_size
    member = my_index % group_size
    late_block = 2 * group_size - 1 - member
    targets = jnp.arange(groups, dtype=jnp.int32)
    kv_flat = kv_cache.reshape(2 * slot_count, block_len, local_width)

    lengths_blocks = jnp.sum((old_table >= 0).astype(jnp.int32), axis=1)
    first_dev = old_table[:, 0] // slot_count
    target_req = targets // group_size
    c_index = jnp.arange(per_dev, dtype=jnp.int32)
    block_index = ((my_index - first_dev[target_req]) % groups)[:, None] + groups * c_index[None, :]
    slot_index = (
        old_table[target_req[:, None], jnp.clip(block_index, 0, old_table.shape[1] - 1)]
        - my_index * slot_count
    )
    slot_index = jnp.clip(slot_index, 0, slot_count - 1)
    kv_ids = jnp.arange(2, dtype=jnp.int32)
    out_ids = kv_ids[None, :, None] * slot_count + slot_index[:, None, :]
    outgoing = jnp.take(kv_flat, out_ids.reshape(-1), axis=0, mode="clip").reshape(
        groups, 2, per_dev, block_len, local_width
    )
    received = lax.all_to_all(outgoing, "blk", split_axis=0, concat_axis=0, tiled=True)

    projected = jnp.einsum(
        "tc,jcw->tjw",
        lax.all_gather(states, "head", axis=1, tiled=True),
        qkv_weight,
        preferred_element_type=jnp.float32,
    )
    queries = projected[:, 0]
    key_new = projected[:, 1]
    value_new = projected[:, 2]
    query_sq, key_sq = lax.psum(
        (jnp.sum(queries * queries, axis=1), jnp.sum(key_new * key_new, axis=1)), "head"
    )
    gains = norm_gains.astype(jnp.float32)
    queries = queries * lax.rsqrt(query_sq / D + norm_eps)[:, None] * gains[0]
    key_new = key_new * lax.rsqrt(key_sq / D + norm_eps)[:, None] * gains[1]
    half_ids = jnp.arange(half_rows, dtype=jnp.int32)
    token_offset = jnp.concatenate(
        [member * half_rows + half_ids, late_block * half_rows + half_ids]
    )
    positions = cached_len[request] + token_offset
    queries = (
        rotate(queries.reshape(tok_rows, local_heads, HS), positions, HS)
        .reshape(tok_rows, local_width)
        .astype(jnp.bfloat16)
    )
    key_new = (
        rotate(key_new.reshape(tok_rows, local_heads, HS), positions, HS)
        .reshape(tok_rows, local_width)
        .astype(jnp.bfloat16)
    )
    value_new = value_new.astype(jnp.bfloat16)
    fresh_kv = jnp.stack([key_new, value_new])

    blocks_dev = tok_rows // block_len
    half_blocks = blocks_dev // 2
    new_count = new_table.shape[1]
    fresh_flat = fresh_kv.reshape(2 * blocks_dev, block_len, local_width)
    pair_index = jnp.arange(2, dtype=jnp.int32)
    new_home = new_table[:, 0] // slot_count
    wanted_out = 2 * ((targets - new_home[request]) % groups)[:, None] + pair_index[None, :]
    out_half = wanted_out // half_blocks
    local_index = jnp.where(
        out_half == member,
        wanted_out - member * half_blocks,
        wanted_out - late_block * half_blocks + half_blocks,
    )
    local_index = jnp.clip(local_index, 0, blocks_dev - 1)
    pick_ids = kv_ids[None, :, None] * blocks_dev + local_index[:, None, :]
    picked = jnp.take(fresh_flat, pick_ids.reshape(-1), axis=0, mode="clip").reshape(
        groups, 2, 2, block_len, local_width
    )
    arrived = lax.all_to_all(picked, "blk", split_axis=0, concat_axis=0, tiled=True)
    source_req = targets // group_size
    source_member = targets % group_size
    source_late = 2 * group_size - 1 - source_member
    wanted_in = 2 * ((my_index - new_home[source_req]) % groups)[:, None] + pair_index[None, :]
    in_half = wanted_in // half_blocks
    valid_in = (in_half == source_member[:, None]) | (in_half == source_late[:, None])
    target_slot = (
        new_table[source_req[:, None], jnp.clip(wanted_in, 0, new_count - 1)]
        - my_index * slot_count
    )
    target_ids = kv_ids[None, :, None] * slot_count + target_slot[:, None, :]
    target_ids = jnp.where(valid_in[:, None, :], target_ids, 2 * slot_count)
    updated_cache = (
        kv_flat.at[target_ids.reshape(-1)]
        .set(arrived.reshape(groups * 4, block_len, local_width), mode="drop")
        .reshape(kv_cache.shape)
    )

    collected = fresh_kv
    partner_new = swapped(collected, "blk", 0)
    lower_new = member // 2**0 % 2 == 0
    collected = jnp.where(
        lower_new,
        jnp.concatenate([collected, partner_new], axis=1),
        jnp.concatenate([partner_new, collected], axis=1),
    )
    meta = jnp.stack([member, cached_len[request], first_dev[request], 0]).astype(jnp.int32)
    acc, m, l = new_attention(meta, queries, collected[0], collected[1])
    attended = cached_attention(meta, queries, received, acc, m, l)
    return (attended, updated_cache)


def solution(mesh):
    return jax.shard_map(
        body,
        mesh=mesh,
        in_specs=(
            P("blk", "head"),
            P(None, None, "head"),
            P(None, "head"),
            P(None, "blk", None, "head"),
            P(),
            P(),
            P(),
        ),
        out_specs=(P("blk", "head"), P(None, "blk", None, "head")),
        check_vma=False,
    )
```

```python
import functools

import jax
import jax.numpy as jnp
from jax import lax
from jax.experimental import pallas as pl
from jax.experimental.pallas import tpu as pltpu
from jax.sharding import PartitionSpec as P


D = 4096
HS = 128


rope_base = 500000.0
norm_eps = 1e-06
score_scale = HS ** (-0.5)


def rotate(values, positions, head_size):
    half_size = head_size // 2
    frequency = rope_base ** (-jnp.arange(half_size, dtype=jnp.float32) * 2.0 / head_size)
    angles = positions.astype(jnp.float32)[:, None] * frequency[None, :]
    cosine = jnp.cos(angles)[:, None, :]
    sine_part = jnp.sin(angles)[:, None, :]
    first_half = values[..., :half_size]
    second = values[..., half_size:]
    return jnp.concatenate(
        [first_half * cosine - second * sine_part, second * cosine + first_half * sine_part],
        axis=-1,
    )


def online_update(s, v, m_sc, l_sc, acc_sc):
    m_prev = m_sc[...]
    m_cur = jnp.max(s, axis=1, keepdims=True) * score_scale
    m_next = jnp.maximum(m_prev, m_cur)
    alpha = jnp.exp(m_prev - m_next)
    p = jnp.exp(s * score_scale - m_next[:, :1])
    l_sc[...] = alpha * l_sc[...] + jnp.sum(p, axis=1, keepdims=True)
    pv = jnp.dot(p.astype(jnp.bfloat16), v, preferred_element_type=jnp.float32)
    acc_sc[...] = acc_sc[...] * alpha + pv
    m_sc[...] = m_next


def scores_of(q, k):
    return lax.dot_general(q, k, (((1,), (1,)), ((), ())), preferred_element_type=jnp.float32)


def new_kernel(meta_ref, q_ref, k_ref, v_ref, *rest, partner):
    if partner:
        acc_in, m_in, l_in, acc_out, m_out, l_out, m_sc, l_sc, acc_sc = rest
    else:
        acc_out, m_out, l_out, m_sc, l_sc, acc_sc = rest
    qi = pl.program_id(1)
    kj = pl.program_id(2)
    member = meta_ref[0]
    q_chunk = jnp.where(qi == 0, member, 3 - member)
    if partner:
        k_chunk = jnp.where(kj == 0, 1 - member, 2 + member)
    else:
        k_chunk = jnp.where(kj == 0, member, 3 - member)

    @pl.when(kj == 0)
    def _():
        if partner:
            m_sc[...] = m_in[...]
            l_sc[...] = l_in[...]
            acc_sc[...] = acc_in[...]
        else:
            m_sc[...] = jnp.full(m_sc.shape, -jnp.inf, jnp.float32)
            l_sc[...] = jnp.zeros(l_sc.shape, jnp.float32)
            acc_sc[...] = jnp.zeros(acc_sc.shape, jnp.float32)

    @pl.when(k_chunk < q_chunk)
    def _():
        s = scores_of(q_ref[...], k_ref[...])
        online_update(s, v_ref[...], m_sc, l_sc, acc_sc)

    @pl.when(k_chunk == q_chunk)
    def _():
        s = scores_of(q_ref[...], k_ref[...])
        rows = lax.broadcasted_iota(jnp.int32, s.shape, 0)
        cols = lax.broadcasted_iota(jnp.int32, s.shape, 1)
        s = jnp.where(cols <= rows, s, -jnp.inf)
        online_update(s, v_ref[...], m_sc, l_sc, acc_sc)

    @pl.when(kj == pl.num_programs(2) - 1)
    def _():
        acc_out[...] = acc_sc[...]
        m_out[...] = m_sc[...]
        l_out[...] = l_sc[...]


def cached_kernel(meta_ref, q_ref, k_ref, v_ref, acc_in, m_in, l_in, o_ref, m_sc, l_sc, acc_sc,
                  *, groups, per_half, block_len):
    c = pl.program_id(1)
    half = pl.program_id(2)
    length = meta_ref[1]
    first = meta_ref[2]
    tile = per_half * block_len

    @pl.when((c == 0) & (half == 0))
    def _():
        m_sc[...] = m_in[...]
        l_sc[...] = l_in[...]
        acc_sc[...] = acc_in[...]

    @pl.when((c + 1) * groups * block_len <= length)
    def _():
        k = k_ref[...].reshape(tile, HS)
        v = v_ref[...].reshape(tile, HS)
        s = scores_of(q_ref[...], k)
        online_update(s, v, m_sc, l_sc, acc_sc)

    @pl.when((c * groups * block_len < length) & ((c + 1) * groups * block_len > length))
    def _():
        k = k_ref[...].reshape(tile, HS)
        v = v_ref[...].reshape(tile, HS)
        s = scores_of(q_ref[...], k)
        cols = lax.broadcasted_iota(jnp.int32, (1, tile), 1)
        src = half * per_half + cols // block_len
        block = (src - first + groups) % groups + groups * c
        visible = block * block_len + cols % block_len < length
        s = jnp.where(visible, s, -jnp.inf)
        online_update(s, v, m_sc, l_sc, acc_sc)

    @pl.when((c == pl.num_programs(1) - 1) & (half == pl.num_programs(2) - 1))
    def _():
        o_ref[...] = (acc_sc[...] / l_sc[...]).astype(o_ref.dtype)


def new_attention(meta, queries, keys, values, state=None):
    tok_rows, width = queries.shape
    heads = width // HS
    q_rows = tok_rows // 2
    key_rows = keys.shape[0]
    k_tiles = key_rows // q_rows
    partner = state is not None
    shape = jax.ShapeDtypeStruct((tok_rows, width), jnp.float32)
    state_spec = pl.BlockSpec((q_rows, HS), lambda h, i, j, meta: (i, h))
    in_specs = [
        pl.BlockSpec((q_rows, HS), lambda h, i, j, meta: (i, h)),
        pl.BlockSpec((q_rows, HS), lambda h, i, j, meta: (j, h)),
        pl.BlockSpec((q_rows, HS), lambda h, i, j, meta: (j, h)),
    ]
    operands = [meta, queries, keys, values]
    if partner:
        in_specs += [state_spec] * 3
        operands += list(state)
    return pl.pallas_call(
        functools.partial(new_kernel, partner=partner),
        out_shape=(shape, shape, shape),
        grid_spec=pltpu.PrefetchScalarGridSpec(
            num_scalar_prefetch=1,
            grid=(heads, 2, k_tiles),
            in_specs=in_specs,
            out_specs=[state_spec, state_spec, state_spec],
            scratch_shapes=[
                pltpu.VMEM((q_rows, HS), jnp.float32),
                pltpu.VMEM((q_rows, HS), jnp.float32),
                pltpu.VMEM((q_rows, HS), jnp.float32),
            ],
        ),
        compiler_params=pltpu.CompilerParams(
            dimension_semantics=("arbitrary", "arbitrary", "arbitrary")
        ),
        cost_estimate=pl.CostEstimate(
            flops=2 * 2 * tok_rows * key_rows * width * 3 // 4,
            transcendentals=tok_rows * key_rows * heads * 3 // 4,
            bytes_accessed=2 * tok_rows * width + 2 * 2 * key_rows * width + 6 * 4 * tok_rows * width,
        ),
    )(*operands)


def cached_attention(meta, queries, received, acc, m, l):
    tok_rows, width = queries.shape
    heads = width // HS
    groups, _, per_dev, block_len, _ = received.shape
    per_half = groups // 2

    def kv_map(index):
        def index_map(h, c, half, meta):
            last = (meta[1] + groups * block_len - 1) // (groups * block_len) - 1
            skip = c > last
            return (
                jnp.where(skip, 1, half),
                index,
                jnp.where(skip, last, c),
                0,
                h,
            )

        return index_map

    kv_block = (per_half, None, None, block_len, HS)
    state_spec = pl.BlockSpec((tok_rows, HS), lambda h, c, half, meta: (0, h))
    keys_total = groups * per_dev * block_len
    return pl.pallas_call(
        functools.partial(
            cached_kernel, groups=groups, per_half=per_half, block_len=block_len
        ),
        out_shape=jax.ShapeDtypeStruct((tok_rows, width), jnp.bfloat16),
        grid_spec=pltpu.PrefetchScalarGridSpec(
            num_scalar_prefetch=1,
            grid=(heads, per_dev, 2),
            in_specs=[
                pl.BlockSpec((tok_rows, HS), lambda h, c, half, meta: (0, h)),
                pl.BlockSpec(kv_block, kv_map(0)),
                pl.BlockSpec(kv_block, kv_map(1)),
                state_spec,
                state_spec,
                state_spec,
            ],
            out_specs=pl.BlockSpec((tok_rows, HS), lambda h, c, half, meta: (0, h)),
            scratch_shapes=[
                pltpu.VMEM((tok_rows, HS), jnp.float32),
                pltpu.VMEM((tok_rows, HS), jnp.float32),
                pltpu.VMEM((tok_rows, HS), jnp.float32),
            ],
        ),
        compiler_params=pltpu.CompilerParams(
            dimension_semantics=("arbitrary", "arbitrary", "arbitrary")
        ),
        cost_estimate=pl.CostEstimate(
            flops=2 * 2 * tok_rows * keys_total * width // 2,
            transcendentals=tok_rows * keys_total * heads // 2,
            bytes_accessed=2 * keys_total * width + 2 * tok_rows * width * 2 + 3 * 4 * tok_rows * width,
        ),
    )(meta, queries, received, received, acc, m, l)


def body(states, qkv_weight, norm_gains, kv_cache, cached_len, old_table, new_table):
    tok_rows = states.shape[0]
    half_rows = tok_rows // 2
    local_width = qkv_weight.shape[2]
    local_heads = local_width // HS
    pair = lax.axis_size("bp")
    groups = lax.axis_size("bx") * pair
    slot_count = kv_cache.shape[1]
    block_len = kv_cache.shape[2]
    per_dev = old_table.shape[1] // groups
    request = lax.axis_index("bx")
    member = lax.axis_index("bp")
    my_index = request * pair + member
    late_block = 2 * pair - 1 - member
    targets = jnp.arange(groups, dtype=jnp.int32)
    kv_ids = jnp.arange(2, dtype=jnp.int32)
    kv_flat = kv_cache.reshape(2 * slot_count, block_len, local_width)

    first_dev = old_table[:, 0] // slot_count
    target_req = targets // pair
    c_index = jnp.arange(per_dev, dtype=jnp.int32)
    block_index = ((my_index - first_dev[target_req]) % groups)[:, None] + groups * c_index[None, :]
    slot_index = (
        old_table[target_req[:, None], jnp.clip(block_index, 0, old_table.shape[1] - 1)]
        - my_index * slot_count
    )
    slot_index = jnp.clip(slot_index, 0, slot_count - 1)
    out_ids = kv_ids[None, :, None] * slot_count + slot_index[:, None, :]
    outgoing = jnp.take(kv_flat, out_ids.reshape(-1), axis=0, mode="clip").reshape(
        groups, 2, per_dev, block_len, local_width
    )
    received = lax.all_to_all(
        outgoing, ("bx", "bp"), split_axis=0, concat_axis=0, tiled=True
    )

    projected = jnp.einsum(
        "tc,jcw->tjw",
        lax.all_gather(states, "head", axis=1, tiled=True),
        qkv_weight,
        preferred_element_type=jnp.float32,
    )
    queries = projected[:, 0]
    key_new = projected[:, 1]
    value_new = projected[:, 2]
    query_sq, key_sq = lax.psum(
        (jnp.sum(queries * queries, axis=1), jnp.sum(key_new * key_new, axis=1)), "head"
    )
    gains = norm_gains.astype(jnp.float32)
    queries = queries * lax.rsqrt(query_sq / D + norm_eps)[:, None] * gains[0]
    key_new = key_new * lax.rsqrt(key_sq / D + norm_eps)[:, None] * gains[1]
    half_ids = jnp.arange(half_rows, dtype=jnp.int32)
    token_offset = jnp.concatenate(
        [member * half_rows + half_ids, late_block * half_rows + half_ids]
    )
    positions = cached_len[request] + token_offset
    queries = (
        rotate(queries.reshape(tok_rows, local_heads, HS), positions, HS)
        .reshape(tok_rows, local_width)
        .astype(jnp.bfloat16)
    )
    key_new = (
        rotate(key_new.reshape(tok_rows, local_heads, HS), positions, HS)
        .reshape(tok_rows, local_width)
        .astype(jnp.bfloat16)
    )
    value_new = value_new.astype(jnp.bfloat16)
    fresh_kv = jnp.stack([key_new, value_new])
    meta = jnp.stack([member, cached_len[request], first_dev[request], 0]).astype(jnp.int32)

    partner_new = lax.ppermute(fresh_kv, "bp", [(0, 1), (1, 0)])
    state = new_attention(meta, queries, fresh_kv[0], fresh_kv[1])

    blocks_dev = tok_rows // block_len
    chunk_blocks = blocks_dev // 2
    collected = jnp.where(
        member == 0,
        jnp.concatenate([fresh_kv, partner_new], axis=1),
        jnp.concatenate([partner_new, fresh_kv], axis=1),
    )
    new_blocks = 2 * blocks_dev
    collected_flat = collected.reshape(2 * new_blocks, block_len, local_width)
    chunk_place = jnp.array([0, 2, 3, 1], dtype=jnp.int32)
    new_home = new_table[:, 0] // slot_count
    pair_index = jnp.arange(2, dtype=jnp.int32)
    reqs = jnp.arange(groups // pair, dtype=jnp.int32)
    dest = reqs * pair + member
    wanted_out = 2 * ((dest - new_home[request]) % groups)[:, None] + pair_index[None, :]
    place = chunk_place[wanted_out // chunk_blocks] * chunk_blocks + wanted_out % chunk_blocks
    pick_ids = kv_ids[None, :, None] * new_blocks + place[:, None, :]
    picked = jnp.take(collected_flat, pick_ids.reshape(-1), axis=0, mode="clip").reshape(
        groups // pair, 2, 2, block_len, local_width
    )
    arrived = lax.all_to_all(picked, "bx", split_axis=0, concat_axis=0, tiled=True)
    wanted_in = 2 * ((my_index - new_home) % groups)[:, None] + pair_index[None, :]
    target_slot = (
        new_table[reqs[:, None], jnp.clip(wanted_in, 0, new_table.shape[1] - 1)]
        - my_index * slot_count
    )
    target_ids = kv_ids[None, :, None] * slot_count + target_slot[:, None, :]
    updated_cache = (
        kv_flat.at[target_ids.reshape(-1)]
        .set(arrived.reshape(-1, block_len, local_width), mode="drop")
        .reshape(kv_cache.shape)
    )

    state = new_attention(meta, queries, partner_new[0], partner_new[1], state)
    attended = cached_attention(meta, queries, received, *state)
    return (attended, updated_cache)


def solution(mesh):
    heads, groups = mesh.devices.shape
    split = jax.sharding.Mesh(mesh.devices.reshape(heads, groups // 2, 2), ("head", "bx", "bp"))
    blk = ("bx", "bp")
    return jax.shard_map(
        body,
        mesh=split,
        in_specs=(
            P(blk, "head"),
            P(None, None, "head"),
            P(None, "head"),
            P(None, blk, None, "head"),
            P(),
            P(),
            P(),
        ),
        out_specs=(P(blk, "head"), P(None, blk, None, "head")),
        check_vma=False,
    )
```

```python
import functools

import jax
import jax.numpy as jnp
from jax import lax
from jax.experimental import pallas as pl
from jax.experimental.pallas import tpu as pltpu
from jax.sharding import PartitionSpec as P


D = 4096
HS = 128


rope_base = 500000.0
norm_eps = 1e-06
score_scale = HS ** (-0.5)


def rotate(values, positions, head_size):
    half_size = head_size // 2
    frequency = rope_base ** (-jnp.arange(half_size, dtype=jnp.float32) * 2.0 / head_size)
    angles = positions.astype(jnp.float32)[:, None] * frequency[None, :]
    cosine = jnp.cos(angles)[:, None, :]
    sine_part = jnp.sin(angles)[:, None, :]
    first_half = values[..., :half_size]
    second = values[..., half_size:]
    return jnp.concatenate(
        [first_half * cosine - second * sine_part, second * cosine + first_half * sine_part],
        axis=-1,
    )


def online_update(s, v, m_sc, l_sc, acc_sc):
    m_prev = m_sc[...]
    m_cur = jnp.max(s, axis=1, keepdims=True) * score_scale
    m_next = jnp.maximum(m_prev, m_cur)
    alpha = jnp.exp(m_prev - m_next)
    p = jnp.exp(s * score_scale - m_next[:, :1])
    l_sc[...] = alpha * l_sc[...] + jnp.sum(p, axis=1, keepdims=True)
    pv = jnp.dot(p.astype(jnp.bfloat16), v, preferred_element_type=jnp.float32)
    acc_sc[...] = acc_sc[...] * alpha + pv
    m_sc[...] = m_next


def scores_of(q, k):
    return lax.dot_general(q, k, (((1,), (1,)), ((), ())), preferred_element_type=jnp.float32)


def new_kernel(meta_ref, q_ref, k_ref, v_ref, *rest, partner):
    if partner:
        acc_in, m_in, l_in, acc_out, m_out, l_out, m_sc, l_sc, acc_sc = rest
    else:
        acc_out, m_out, l_out, m_sc, l_sc, acc_sc = rest
    qi = pl.program_id(1)
    kj = pl.program_id(2)
    member = meta_ref[0]
    q_chunk = jnp.where(qi == 0, member, 3 - member)
    if partner:
        k_chunk = jnp.where(kj == 0, 1 - member, 2 + member)
    else:
        k_chunk = jnp.where(kj == 0, member, 3 - member)

    @pl.when(kj == 0)
    def _():
        if partner:
            m_sc[...] = m_in[...]
            l_sc[...] = l_in[...]
            acc_sc[...] = acc_in[...]
        else:
            m_sc[...] = jnp.full(m_sc.shape, -jnp.inf, jnp.float32)
            l_sc[...] = jnp.zeros(l_sc.shape, jnp.float32)
            acc_sc[...] = jnp.zeros(acc_sc.shape, jnp.float32)

    @pl.when(k_chunk < q_chunk)
    def _():
        s = scores_of(q_ref[...], k_ref[...])
        online_update(s, v_ref[...], m_sc, l_sc, acc_sc)

    @pl.when(k_chunk == q_chunk)
    def _():
        s = scores_of(q_ref[...], k_ref[...])
        rows = lax.broadcasted_iota(jnp.int32, s.shape, 0)
        cols = lax.broadcasted_iota(jnp.int32, s.shape, 1)
        s = jnp.where(cols <= rows, s, -jnp.inf)
        online_update(s, v_ref[...], m_sc, l_sc, acc_sc)

    @pl.when(kj == pl.num_programs(2) - 1)
    def _():
        acc_out[...] = acc_sc[...]
        m_out[...] = m_sc[...]
        l_out[...] = l_sc[...]


def cached_kernel(meta_ref, q_ref, k_ref, v_ref, acc_in, m_in, l_in, *rest,
                  groups, per_half, block_len, level0, final):
    if final:
        o_ref, m_sc, l_sc, acc_sc = rest
    else:
        acc_out, m_out, l_out, m_sc, l_sc, acc_sc = rest
    c = pl.program_id(1) + level0
    half = pl.program_id(2)
    length = meta_ref[1]
    first = meta_ref[2]
    tile = per_half * block_len

    @pl.when((pl.program_id(1) == 0) & (half == 0))
    def _():
        m_sc[...] = m_in[...]
        l_sc[...] = l_in[...]
        acc_sc[...] = acc_in[...]

    @pl.when((c + 1) * groups * block_len <= length)
    def _():
        k = k_ref[...].reshape(tile, HS)
        v = v_ref[...].reshape(tile, HS)
        s = scores_of(q_ref[...], k)
        online_update(s, v, m_sc, l_sc, acc_sc)

    @pl.when((c * groups * block_len < length) & ((c + 1) * groups * block_len > length))
    def _():
        k = k_ref[...].reshape(tile, HS)
        v = v_ref[...].reshape(tile, HS)
        s = scores_of(q_ref[...], k)
        cols = lax.broadcasted_iota(jnp.int32, (1, tile), 1)
        src = half * per_half + cols // block_len
        block = (src - first + groups) % groups + groups * c
        visible = block * block_len + cols % block_len < length
        s = jnp.where(visible, s, -jnp.inf)
        online_update(s, v, m_sc, l_sc, acc_sc)

    @pl.when((pl.program_id(1) == pl.num_programs(1) - 1) & (half == pl.num_programs(2) - 1))
    def _():
        if final:
            o_ref[...] = (acc_sc[...] / l_sc[...]).astype(o_ref.dtype)
        else:
            acc_out[...] = acc_sc[...]
            m_out[...] = m_sc[...]
            l_out[...] = l_sc[...]


def new_attention(meta, queries, keys, values, state=None):
    tok_rows, width = queries.shape
    heads = width // HS
    q_rows = tok_rows // 2
    key_rows = keys.shape[0]
    k_tiles = key_rows // q_rows
    partner = state is not None
    shape = jax.ShapeDtypeStruct((tok_rows, width), jnp.float32)
    state_spec = pl.BlockSpec((q_rows, HS), lambda h, i, j, meta: (i, h))
    in_specs = [
        pl.BlockSpec((q_rows, HS), lambda h, i, j, meta: (i, h)),
        pl.BlockSpec((q_rows, HS), lambda h, i, j, meta: (j, h)),
        pl.BlockSpec((q_rows, HS), lambda h, i, j, meta: (j, h)),
    ]
    operands = [meta, queries, keys, values]
    if partner:
        in_specs += [state_spec] * 3
        operands += list(state)
    return pl.pallas_call(
        functools.partial(new_kernel, partner=partner),
        out_shape=(shape, shape, shape),
        grid_spec=pltpu.PrefetchScalarGridSpec(
            num_scalar_prefetch=1,
            grid=(heads, 2, k_tiles),
            in_specs=in_specs,
            out_specs=[state_spec, state_spec, state_spec],
            scratch_shapes=[
                pltpu.VMEM((q_rows, HS), jnp.float32),
                pltpu.VMEM((q_rows, HS), jnp.float32),
                pltpu.VMEM((q_rows, HS), jnp.float32),
            ],
        ),
        compiler_params=pltpu.CompilerParams(
            dimension_semantics=("arbitrary", "arbitrary", "arbitrary")
        ),
        cost_estimate=pl.CostEstimate(
            flops=2 * 2 * tok_rows * key_rows * width * 3 // 4,
            transcendentals=tok_rows * key_rows * heads * 3 // 4,
            bytes_accessed=2 * tok_rows * width + 2 * 2 * key_rows * width + 6 * 4 * tok_rows * width,
        ),
    )(*operands)


def cached_attention(meta, queries, received, acc, m, l, level0, final):
    tok_rows, width = queries.shape
    heads = width // HS
    groups, _, levels, block_len, _ = received.shape
    per_half = groups // 2

    def kv_map(index):
        def index_map(h, c, half, meta):
            last = (meta[1] + groups * block_len - 1) // (groups * block_len) - 1 - level0
            skip = c > last
            return (
                jnp.where(skip, 1, half),
                index,
                jnp.where(skip, jnp.clip(last, 0, levels - 1), c),
                0,
                h,
            )

        return index_map

    kv_block = (per_half, None, None, block_len, HS)
    state_spec = pl.BlockSpec((tok_rows, HS), lambda h, c, half, meta: (0, h))
    keys_total = groups * levels * block_len
    if final:
        out_shape = jax.ShapeDtypeStruct((tok_rows, width), jnp.bfloat16)
        out_specs = state_spec
    else:
        state = jax.ShapeDtypeStruct((tok_rows, width), jnp.float32)
        out_shape = (state, state, state)
        out_specs = [state_spec, state_spec, state_spec]
    return pl.pallas_call(
        functools.partial(
            cached_kernel, groups=groups, per_half=per_half, block_len=block_len,
            level0=level0, final=final,
        ),
        out_shape=out_shape,
        grid_spec=pltpu.PrefetchScalarGridSpec(
            num_scalar_prefetch=1,
            grid=(heads, levels, 2),
            in_specs=[
                pl.BlockSpec((tok_rows, HS), lambda h, c, half, meta: (0, h)),
                pl.BlockSpec(kv_block, kv_map(0)),
                pl.BlockSpec(kv_block, kv_map(1)),
                state_spec,
                state_spec,
                state_spec,
            ],
            out_specs=out_specs,
            scratch_shapes=[
                pltpu.VMEM((tok_rows, HS), jnp.float32),
                pltpu.VMEM((tok_rows, HS), jnp.float32),
                pltpu.VMEM((tok_rows, HS), jnp.float32),
            ],
        ),
        compiler_params=pltpu.CompilerParams(
            dimension_semantics=("arbitrary", "arbitrary", "arbitrary")
        ),
        cost_estimate=pl.CostEstimate(
            flops=2 * 2 * tok_rows * keys_total * width // 2,
            transcendentals=tok_rows * keys_total * heads // 2,
            bytes_accessed=2 * keys_total * width + 2 * tok_rows * width * 2 + 6 * 4 * tok_rows * width,
        ),
    )(meta, queries, received, received, acc, m, l)


def body(states, qkv_weight, norm_gains, kv_cache, cached_len, old_table, new_table):
    tok_rows = states.shape[0]
    half_rows = tok_rows // 2
    local_width = qkv_weight.shape[2]
    local_heads = local_width // HS
    pair = lax.axis_size("bp")
    groups = lax.axis_size("bx") * pair
    slot_count = kv_cache.shape[1]
    block_len = kv_cache.shape[2]
    per_dev = old_table.shape[1] // groups
    request = lax.axis_index("bx")
    member = lax.axis_index("bp")
    my_index = request * pair + member
    late_block = 2 * pair - 1 - member
    targets = jnp.arange(groups, dtype=jnp.int32)
    kv_ids = jnp.arange(2, dtype=jnp.int32)
    kv_flat = kv_cache.reshape(2 * slot_count, block_len, local_width)

    first_dev = old_table[:, 0] // slot_count
    target_req = targets // pair
    c_index = jnp.arange(per_dev, dtype=jnp.int32)
    block_index = ((my_index - first_dev[target_req]) % groups)[:, None] + groups * c_index[None, :]
    slot_index = (
        old_table[target_req[:, None], jnp.clip(block_index, 0, old_table.shape[1] - 1)]
        - my_index * slot_count
    )
    slot_index = jnp.clip(slot_index, 0, slot_count - 1)
    out_ids = kv_ids[None, :, None] * slot_count + slot_index[:, None, :]
    low_levels = per_dev // 2

    def cached_part(ids):
        outgoing = jnp.take(kv_flat, ids.reshape(-1), axis=0, mode="clip").reshape(
            groups, 2, ids.shape[2], block_len, local_width
        )
        return lax.all_to_all(outgoing, ("bx", "bp"), split_axis=0, concat_axis=0, tiled=True)

    received_lo = cached_part(out_ids[:, :, :low_levels])
    received_hi = cached_part(out_ids[:, :, low_levels:])

    gathered = lax.all_gather(states, "head", axis=1, tiled=True)
    projected = jnp.einsum("tc,jcw->tjw", gathered, qkv_weight, preferred_element_type=jnp.float32)
    queries = projected[:, 0]
    key_new = projected[:, 1]
    value_new = projected[:, 2]
    query_sq, key_sq = lax.psum(
        (jnp.sum(queries * queries, axis=1), jnp.sum(key_new * key_new, axis=1)), "head"
    )
    gains = norm_gains.astype(jnp.float32)
    queries = queries * lax.rsqrt(query_sq / D + norm_eps)[:, None] * gains[0]
    key_new = key_new * lax.rsqrt(key_sq / D + norm_eps)[:, None] * gains[1]
    half_ids = jnp.arange(half_rows, dtype=jnp.int32)
    token_offset = jnp.concatenate(
        [member * half_rows + half_ids, late_block * half_rows + half_ids]
    )
    positions = cached_len[request] + token_offset
    queries = (
        rotate(queries.reshape(tok_rows, local_heads, HS), positions, HS)
        .reshape(tok_rows, local_width)
        .astype(jnp.bfloat16)
    )
    key_new = (
        rotate(key_new.reshape(tok_rows, local_heads, HS), positions, HS)
        .reshape(tok_rows, local_width)
        .astype(jnp.bfloat16)
    )
    value_new = value_new.astype(jnp.bfloat16)
    fresh_kv = jnp.stack([key_new, value_new])
    meta = jnp.stack([member, cached_len[request], first_dev[request], 0]).astype(jnp.int32)

    partner_new = lax.ppermute(fresh_kv, "bp", [(0, 1), (1, 0)])
    state = new_attention(meta, queries, fresh_kv[0], fresh_kv[1])

    blocks_dev = tok_rows // block_len
    chunk_blocks = blocks_dev // 2
    collected = jnp.where(
        member == 0,
        jnp.concatenate([fresh_kv, partner_new], axis=1),
        jnp.concatenate([partner_new, fresh_kv], axis=1),
    )
    new_blocks = 2 * blocks_dev
    collected_flat = collected.reshape(2 * new_blocks, block_len, local_width)
    chunk_place = jnp.array([0, 2, 3, 1], dtype=jnp.int32)
    new_home = new_table[:, 0] // slot_count
    pair_index = jnp.arange(2, dtype=jnp.int32)
    reqs = jnp.arange(groups // pair, dtype=jnp.int32)
    dest = reqs * pair + member
    wanted_out = 2 * ((dest - new_home[request]) % groups)[:, None] + pair_index[None, :]
    place = chunk_place[wanted_out // chunk_blocks] * chunk_blocks + wanted_out % chunk_blocks
    pick_ids = kv_ids[None, :, None] * new_blocks + place[:, None, :]
    picked = jnp.take(collected_flat, pick_ids.reshape(-1), axis=0, mode="clip").reshape(
        groups // pair, 2, 2, block_len, local_width
    )
    arrived = lax.all_to_all(picked, "bx", split_axis=0, concat_axis=0, tiled=True)
    wanted_in = 2 * ((my_index - new_home) % groups)[:, None] + pair_index[None, :]
    target_slot = (
        new_table[reqs[:, None], jnp.clip(wanted_in, 0, new_table.shape[1] - 1)]
        - my_index * slot_count
    )
    target_ids = kv_ids[None, :, None] * slot_count + target_slot[:, None, :]
    updated_cache = (
        kv_flat.at[target_ids.reshape(-1)]
        .set(arrived.reshape(-1, block_len, local_width), mode="drop")
        .reshape(kv_cache.shape)
    )

    state = new_attention(meta, queries, partner_new[0], partner_new[1], state)
    state = cached_attention(meta, queries, received_lo, *state, 0, False)
    attended = cached_attention(meta, queries, received_hi, *state, low_levels, True)
    return (attended, updated_cache)


def solution(mesh):
    heads, groups = mesh.devices.shape
    split = jax.sharding.Mesh(mesh.devices.reshape(heads, groups // 2, 2), ("head", "bx", "bp"))
    blk = ("bx", "bp")
    return jax.shard_map(
        body,
        mesh=split,
        in_specs=(
            P(blk, "head"),
            P(None, None, "head"),
            P(None, "head"),
            P(None, blk, None, "head"),
            P(),
            P(),
            P(),
        ),
        out_specs=(P(blk, "head"), P(None, blk, None, "head")),
        check_vma=False,
    )
```

```python
import functools

import jax
import jax.numpy as jnp
from jax import lax
from jax.experimental import pallas as pl
from jax.experimental.pallas import tpu as pltpu
from jax.sharding import PartitionSpec as P


D = 4096
HS = 128


rope_base = 500000.0
norm_eps = 1e-06
score_scale = HS ** (-0.5)


def rotate(values, positions, head_size):
    half_size = head_size // 2
    frequency = rope_base ** (-jnp.arange(half_size, dtype=jnp.float32) * 2.0 / head_size)
    angles = positions.astype(jnp.float32)[:, None] * frequency[None, :]
    cosine = jnp.cos(angles)[:, None, :]
    sine_part = jnp.sin(angles)[:, None, :]
    first_half = values[..., :half_size]
    second = values[..., half_size:]
    return jnp.concatenate(
        [first_half * cosine - second * sine_part, second * cosine + first_half * sine_part],
        axis=-1,
    )


def online_update(s, v, m_sc, l_sc, acc_sc):
    m_prev = m_sc[...]
    m_cur = jnp.max(s, axis=1, keepdims=True) * score_scale
    m_next = jnp.maximum(m_prev, m_cur)
    alpha = jnp.exp(m_prev - m_next)
    p = jnp.exp(s * score_scale - m_next[:, :1])
    l_sc[...] = alpha * l_sc[...] + jnp.sum(p, axis=1, keepdims=True)
    pv = jnp.dot(p.astype(jnp.bfloat16), v, preferred_element_type=jnp.float32)
    acc_sc[...] = acc_sc[...] * alpha + pv
    m_sc[...] = m_next


def scores_of(q, k):
    return lax.dot_general(q, k, (((1,), (1,)), ((), ())), preferred_element_type=jnp.float32)


def new_kernel(meta_ref, q_ref, k_ref, v_ref, *rest, partner):
    if partner:
        acc_in, m_in, l_in, acc_out, m_out, l_out, m_sc, l_sc, acc_sc = rest
    else:
        acc_out, m_out, l_out, m_sc, l_sc, acc_sc = rest
    qi = pl.program_id(1)
    kj = pl.program_id(2)
    member = meta_ref[0]
    q_chunk = jnp.where(qi == 0, member, 3 - member)
    if partner:
        k_chunk = jnp.where(kj == 0, 1 - member, 2 + member)
    else:
        k_chunk = jnp.where(kj == 0, member, 3 - member)

    @pl.when(kj == 0)
    def _():
        if partner:
            m_sc[...] = m_in[...]
            l_sc[...] = l_in[...]
            acc_sc[...] = acc_in[...]
        else:
            m_sc[...] = jnp.full(m_sc.shape, -jnp.inf, jnp.float32)
            l_sc[...] = jnp.zeros(l_sc.shape, jnp.float32)
            acc_sc[...] = jnp.zeros(acc_sc.shape, jnp.float32)

    @pl.when(k_chunk < q_chunk)
    def _():
        s = scores_of(q_ref[...], k_ref[...])
        online_update(s, v_ref[...], m_sc, l_sc, acc_sc)

    @pl.when(k_chunk == q_chunk)
    def _():
        s = scores_of(q_ref[...], k_ref[...])
        rows = lax.broadcasted_iota(jnp.int32, s.shape, 0)
        cols = lax.broadcasted_iota(jnp.int32, s.shape, 1)
        s = jnp.where(cols <= rows, s, -jnp.inf)
        online_update(s, v_ref[...], m_sc, l_sc, acc_sc)

    @pl.when(kj == pl.num_programs(2) - 1)
    def _():
        acc_out[...] = acc_sc[...]
        m_out[...] = m_sc[...]
        l_out[...] = l_sc[...]


def cached_kernel(meta_ref, q_ref, k_ref, v_ref, acc_in, m_in, l_in, o_ref, m_sc, l_sc, acc_sc,
                  *, groups, per_half, block_len):
    c = pl.program_id(1)
    half = pl.program_id(2)
    length = meta_ref[1]
    first = meta_ref[2]
    tile = per_half * block_len

    @pl.when((c == 0) & (half == 0))
    def _():
        m_sc[...] = m_in[...]
        l_sc[...] = l_in[...]
        acc_sc[...] = acc_in[...]

    @pl.when((c + 1) * groups * block_len <= length)
    def _():
        k = k_ref[...].reshape(tile, HS)
        v = v_ref[...].reshape(tile, HS)
        s = scores_of(q_ref[...], k)
        online_update(s, v, m_sc, l_sc, acc_sc)

    @pl.when((c * groups * block_len < length) & ((c + 1) * groups * block_len > length))
    def _():
        k = k_ref[...].reshape(tile, HS)
        v = v_ref[...].reshape(tile, HS)
        s = scores_of(q_ref[...], k)
        cols = lax.broadcasted_iota(jnp.int32, (1, tile), 1)
        src = half * per_half + cols // block_len
        block = (src - first + groups) % groups + groups * c
        visible = block * block_len + cols % block_len < length
        s = jnp.where(visible, s, -jnp.inf)
        online_update(s, v, m_sc, l_sc, acc_sc)

    @pl.when((c == pl.num_programs(1) - 1) & (half == pl.num_programs(2) - 1))
    def _():
        o_ref[...] = (acc_sc[...] / l_sc[...]).astype(o_ref.dtype)


def new_attention(meta, queries, keys, values, state=None):
    tok_rows, width = queries.shape
    heads = width // HS
    q_rows = tok_rows // 2
    key_rows = keys.shape[0]
    k_tiles = key_rows // q_rows
    partner = state is not None
    shape = jax.ShapeDtypeStruct((tok_rows, width), jnp.float32)
    state_spec = pl.BlockSpec((q_rows, HS), lambda h, i, j, meta: (i, h))
    in_specs = [
        pl.BlockSpec((q_rows, HS), lambda h, i, j, meta: (i, h)),
        pl.BlockSpec((q_rows, HS), lambda h, i, j, meta: (j, h)),
        pl.BlockSpec((q_rows, HS), lambda h, i, j, meta: (j, h)),
    ]
    operands = [meta, queries, keys, values]
    if partner:
        in_specs += [state_spec] * 3
        operands += list(state)
    return pl.pallas_call(
        functools.partial(new_kernel, partner=partner),
        out_shape=(shape, shape, shape),
        grid_spec=pltpu.PrefetchScalarGridSpec(
            num_scalar_prefetch=1,
            grid=(heads, 2, k_tiles),
            in_specs=in_specs,
            out_specs=[state_spec, state_spec, state_spec],
            scratch_shapes=[
                pltpu.VMEM((q_rows, HS), jnp.float32),
                pltpu.VMEM((q_rows, HS), jnp.float32),
                pltpu.VMEM((q_rows, HS), jnp.float32),
            ],
        ),
        compiler_params=pltpu.CompilerParams(
            dimension_semantics=("arbitrary", "arbitrary", "arbitrary")
        ),
        cost_estimate=pl.CostEstimate(
            flops=2 * 2 * tok_rows * key_rows * width * 3 // 4,
            transcendentals=tok_rows * key_rows * heads * 3 // 4,
            bytes_accessed=2 * tok_rows * width + 2 * 2 * key_rows * width + 6 * 4 * tok_rows * width,
        ),
    )(*operands)


def cached_attention(meta, queries, received, acc, m, l):
    tok_rows, width = queries.shape
    heads = width // HS
    groups, _, per_dev, block_len, _ = received.shape
    per_half = groups // 2

    def kv_map(index):
        def index_map(h, c, half, meta):
            last = (meta[1] + groups * block_len - 1) // (groups * block_len) - 1
            skip = c > last
            return (
                jnp.where(skip, 1, half),
                index,
                jnp.where(skip, last, c),
                0,
                h,
            )

        return index_map

    kv_block = (per_half, None, None, block_len, HS)
    state_spec = pl.BlockSpec((tok_rows, HS), lambda h, c, half, meta: (0, h))
    keys_total = groups * per_dev * block_len
    return pl.pallas_call(
        functools.partial(
            cached_kernel, groups=groups, per_half=per_half, block_len=block_len
        ),
        out_shape=jax.ShapeDtypeStruct((tok_rows, width), jnp.bfloat16),
        grid_spec=pltpu.PrefetchScalarGridSpec(
            num_scalar_prefetch=1,
            grid=(heads, per_dev, 2),
            in_specs=[
                pl.BlockSpec((tok_rows, HS), lambda h, c, half, meta: (0, h)),
                pl.BlockSpec(kv_block, kv_map(0)),
                pl.BlockSpec(kv_block, kv_map(1)),
                state_spec,
                state_spec,
                state_spec,
            ],
            out_specs=pl.BlockSpec((tok_rows, HS), lambda h, c, half, meta: (0, h)),
            scratch_shapes=[
                pltpu.VMEM((tok_rows, HS), jnp.float32),
                pltpu.VMEM((tok_rows, HS), jnp.float32),
                pltpu.VMEM((tok_rows, HS), jnp.float32),
            ],
        ),
        compiler_params=pltpu.CompilerParams(
            dimension_semantics=("arbitrary", "arbitrary", "arbitrary")
        ),
        cost_estimate=pl.CostEstimate(
            flops=2 * 2 * tok_rows * keys_total * width // 2,
            transcendentals=tok_rows * keys_total * heads // 2,
            bytes_accessed=2 * keys_total * width + 2 * tok_rows * width * 2 + 3 * 4 * tok_rows * width,
        ),
    )(meta, queries, received, received, acc, m, l)


def body(states, qkv_weight, norm_gains, kv_cache, cached_len, old_table, new_table):
    tok_rows = states.shape[0]
    half_rows = tok_rows // 2
    local_width = qkv_weight.shape[2]
    local_heads = local_width // HS
    pair = lax.axis_size("bp")
    groups = lax.axis_size("bx") * pair
    slot_count = kv_cache.shape[1]
    block_len = kv_cache.shape[2]
    per_dev = old_table.shape[1] // groups
    request = lax.axis_index("bx")
    member = lax.axis_index("bp")
    my_index = request * pair + member
    late_block = 2 * pair - 1 - member
    targets = jnp.arange(groups, dtype=jnp.int32)
    kv_ids = jnp.arange(2, dtype=jnp.int32)
    kv_flat = kv_cache.reshape(2 * slot_count, block_len, local_width)

    first_dev = old_table[:, 0] // slot_count
    target_req = targets // pair
    c_index = jnp.arange(per_dev, dtype=jnp.int32)
    block_index = ((my_index - first_dev[target_req]) % groups)[:, None] + groups * c_index[None, :]
    slot_index = (
        old_table[target_req[:, None], jnp.clip(block_index, 0, old_table.shape[1] - 1)]
        - my_index * slot_count
    )
    slot_index = jnp.clip(slot_index, 0, slot_count - 1)
    out_ids = kv_ids[None, :, None] * slot_count + slot_index[:, None, :]
    outgoing = jnp.take(kv_flat, out_ids.reshape(-1), axis=0, mode="clip").reshape(
        groups, 2, per_dev, block_len, local_width
    )
    received = lax.all_to_all(
        outgoing, ("bx", "bp"), split_axis=0, concat_axis=0, tiled=True
    )

    projected = jnp.einsum(
        "tc,jcw->tjw",
        lax.all_gather(states, "head", axis=1, tiled=True),
        qkv_weight,
        preferred_element_type=jnp.float32,
    )
    queries = projected[:, 0]
    key_new = projected[:, 1]
    value_new = projected[:, 2]
    query_sq, key_sq = lax.psum(
        (jnp.sum(queries * queries, axis=1), jnp.sum(key_new * key_new, axis=1)), "head"
    )
    gains = norm_gains.astype(jnp.float32)
    queries = queries * lax.rsqrt(query_sq / D + norm_eps)[:, None] * gains[0]
    key_new = key_new * lax.rsqrt(key_sq / D + norm_eps)[:, None] * gains[1]
    half_ids = jnp.arange(half_rows, dtype=jnp.int32)
    token_offset = jnp.concatenate(
        [member * half_rows + half_ids, late_block * half_rows + half_ids]
    )
    positions = cached_len[request] + token_offset
    queries = (
        rotate(queries.reshape(tok_rows, local_heads, HS), positions, HS)
        .reshape(tok_rows, local_width)
        .astype(jnp.bfloat16)
    )
    key_new = (
        rotate(key_new.reshape(tok_rows, local_heads, HS), positions, HS)
        .reshape(tok_rows, local_width)
        .astype(jnp.bfloat16)
    )
    value_new = value_new.astype(jnp.bfloat16)
    fresh_kv = jnp.stack([key_new, value_new])
    meta = jnp.stack([member, cached_len[request], first_dev[request], 0]).astype(jnp.int32)

    collected = lax.all_gather(fresh_kv, "bp", axis=1, tiled=True)
    state = new_attention(meta, queries, fresh_kv[0], fresh_kv[1])
    partner_new = lax.dynamic_slice_in_dim(collected, (1 - member) * tok_rows, tok_rows, axis=1)

    blocks_dev = tok_rows // block_len
    chunk_blocks = blocks_dev // 2
    new_blocks = 2 * blocks_dev
    collected_flat = collected.reshape(2 * new_blocks, block_len, local_width)
    chunk_place = jnp.array([0, 2, 3, 1], dtype=jnp.int32)
    new_home = new_table[:, 0] // slot_count
    pair_index = jnp.arange(2, dtype=jnp.int32)
    reqs = jnp.arange(groups // pair, dtype=jnp.int32)
    dest = reqs * pair + member
    wanted_out = 2 * ((dest - new_home[request]) % groups)[:, None] + pair_index[None, :]
    place = chunk_place[wanted_out // chunk_blocks] * chunk_blocks + wanted_out % chunk_blocks
    pick_ids = kv_ids[None, :, None] * new_blocks + place[:, None, :]
    picked = jnp.take(collected_flat, pick_ids.reshape(-1), axis=0, mode="clip").reshape(
        groups // pair, 2, 2, block_len, local_width
    )
    arrived = lax.all_to_all(picked, "bx", split_axis=0, concat_axis=0, tiled=True)
    wanted_in = 2 * ((my_index - new_home) % groups)[:, None] + pair_index[None, :]
    target_slot = (
        new_table[reqs[:, None], jnp.clip(wanted_in, 0, new_table.shape[1] - 1)]
        - my_index * slot_count
    )
    target_ids = kv_ids[None, :, None] * slot_count + target_slot[:, None, :]
    updated_cache = (
        kv_flat.at[target_ids.reshape(-1)]
        .set(arrived.reshape(-1, block_len, local_width), mode="drop")
        .reshape(kv_cache.shape)
    )

    state = new_attention(meta, queries, partner_new[0], partner_new[1], state)
    attended = cached_attention(meta, queries, received, *state)
    return (attended, updated_cache)


def solution(mesh):
    heads, groups = mesh.devices.shape
    split = jax.sharding.Mesh(mesh.devices.reshape(heads, groups // 2, 2), ("head", "bx", "bp"))
    blk = ("bx", "bp")
    return jax.shard_map(
        body,
        mesh=split,
        in_specs=(
            P(blk, "head"),
            P(None, None, "head"),
            P(None, "head"),
            P(None, blk, None, "head"),
            P(),
            P(),
            P(),
        ),
        out_specs=(P(blk, "head"), P(None, blk, None, "head")),
        check_vma=False,
    )
```

```python
import functools

import jax
import jax.numpy as jnp
from jax import lax
from jax.experimental import pallas as pl
from jax.experimental.pallas import tpu as pltpu
from jax.sharding import PartitionSpec as P


D = 4096
HS = 128


rope_base = 500000.0
norm_eps = 1e-06
score_scale = HS ** (-0.5)
scale2 = score_scale * 1.4426950408889634


def rotate(values, positions, head_size):
    half_size = head_size // 2
    frequency = rope_base ** (-jnp.arange(half_size, dtype=jnp.float32) * 2.0 / head_size)
    angles = positions.astype(jnp.float32)[:, None] * frequency[None, :]
    cosine = jnp.cos(angles)[:, None, :]
    sine_part = jnp.sin(angles)[:, None, :]
    first_half = values[..., :half_size]
    second = values[..., half_size:]
    return jnp.concatenate(
        [first_half * cosine - second * sine_part, second * cosine + first_half * sine_part],
        axis=-1,
    )


def online_update(s, v, m_sc, l_sc, acc_sc):
    m_prev = m_sc[...]
    m_cur = jnp.max(s, axis=1, keepdims=True) * scale2
    m_next = jnp.maximum(m_prev, m_cur)
    alpha = jnp.exp2(m_prev - m_next)
    p = jnp.exp2(s * scale2 - m_next[:, :1])
    l_sc[...] = alpha * l_sc[...] + jnp.sum(p, axis=1, keepdims=True)
    pv = jnp.dot(p.astype(jnp.bfloat16), v, preferred_element_type=jnp.float32)
    acc_sc[...] = acc_sc[...] * alpha + pv
    m_sc[...] = m_next


def scores_of(q, k):
    return lax.dot_general(q, k, (((1,), (1,)), ((), ())), preferred_element_type=jnp.float32)


def new_kernel(meta_ref, q_ref, k_ref, v_ref, *rest, partner):
    if partner:
        acc_in, m_in, l_in, acc_out, m_out, l_out, m_sc, l_sc, acc_sc = rest
    else:
        acc_out, m_out, l_out, m_sc, l_sc, acc_sc = rest
    qi = pl.program_id(1)
    kj = pl.program_id(2)
    member = meta_ref[0]
    q_chunk = jnp.where(qi == 0, member, 3 - member)
    if partner:
        k_chunk = jnp.where(kj == 0, 1 - member, 2 + member)
    else:
        k_chunk = jnp.where(kj == 0, member, 3 - member)

    @pl.when(kj == 0)
    def _():
        if partner:
            m_sc[...] = m_in[...]
            l_sc[...] = l_in[...]
            acc_sc[...] = acc_in[...]
        else:
            m_sc[...] = jnp.full(m_sc.shape, -jnp.inf, jnp.float32)
            l_sc[...] = jnp.zeros(l_sc.shape, jnp.float32)
            acc_sc[...] = jnp.zeros(acc_sc.shape, jnp.float32)

    @pl.when(k_chunk < q_chunk)
    def _():
        s = scores_of(q_ref[...], k_ref[...])
        online_update(s, v_ref[...], m_sc, l_sc, acc_sc)

    @pl.when(k_chunk == q_chunk)
    def _():
        s = scores_of(q_ref[...], k_ref[...])
        rows = lax.broadcasted_iota(jnp.int32, s.shape, 0)
        cols = lax.broadcasted_iota(jnp.int32, s.shape, 1)
        s = jnp.where(cols <= rows, s, -jnp.inf)
        online_update(s, v_ref[...], m_sc, l_sc, acc_sc)

    @pl.when(kj == pl.num_programs(2) - 1)
    def _():
        acc_out[...] = acc_sc[...]
        m_out[...] = m_sc[...]
        l_out[...] = l_sc[...]


def cached_kernel(meta_ref, q_ref, k_ref, v_ref, acc_in, m_in, l_in, o_ref, m_sc, l_sc, acc_sc,
                  *, groups, block_len):
    c = pl.program_id(1)
    length = meta_ref[1]
    first = meta_ref[2]
    tile = groups * block_len

    @pl.when(c == 0)
    def _():
        m_sc[...] = m_in[...]
        l_sc[...] = l_in[...]
        acc_sc[...] = acc_in[...]

    @pl.when((c + 1) * groups * block_len <= length)
    def _():
        k = k_ref[...].reshape(tile, HS)
        v = v_ref[...].reshape(tile, HS)
        s = scores_of(q_ref[...], k)
        online_update(s, v, m_sc, l_sc, acc_sc)

    @pl.when((c * groups * block_len < length) & ((c + 1) * groups * block_len > length))
    def _():
        k = k_ref[...].reshape(tile, HS)
        v = v_ref[...].reshape(tile, HS)
        s = scores_of(q_ref[...], k)
        cols = lax.broadcasted_iota(jnp.int32, (1, tile), 1)
        src = cols // block_len
        block = (src - first + groups) % groups + groups * c
        visible = block * block_len + cols % block_len < length
        s = jnp.where(visible, s, -jnp.inf)
        online_update(s, v, m_sc, l_sc, acc_sc)

    @pl.when(c == pl.num_programs(1) - 1)
    def _():
        o_ref[...] = (acc_sc[...] / l_sc[...]).astype(o_ref.dtype)


def new_attention(meta, queries, keys, values, state=None):
    tok_rows, width = queries.shape
    heads = width // HS
    q_rows = tok_rows // 2
    key_rows = keys.shape[0]
    k_tiles = key_rows // q_rows
    partner = state is not None
    shape = jax.ShapeDtypeStruct((tok_rows, width), jnp.float32)
    state_spec = pl.BlockSpec((q_rows, HS), lambda h, i, j, meta: (i, h))
    in_specs = [
        pl.BlockSpec((q_rows, HS), lambda h, i, j, meta: (i, h)),
        pl.BlockSpec((q_rows, HS), lambda h, i, j, meta: (j, h)),
        pl.BlockSpec((q_rows, HS), lambda h, i, j, meta: (j, h)),
    ]
    operands = [meta, queries, keys, values]
    if partner:
        in_specs += [state_spec] * 3
        operands += list(state)
    return pl.pallas_call(
        functools.partial(new_kernel, partner=partner),
        out_shape=(shape, shape, shape),
        grid_spec=pltpu.PrefetchScalarGridSpec(
            num_scalar_prefetch=1,
            grid=(heads, 2, k_tiles),
            in_specs=in_specs,
            out_specs=[state_spec, state_spec, state_spec],
            scratch_shapes=[
                pltpu.VMEM((q_rows, HS), jnp.float32),
                pltpu.VMEM((q_rows, HS), jnp.float32),
                pltpu.VMEM((q_rows, HS), jnp.float32),
            ],
        ),
        compiler_params=pltpu.CompilerParams(
            dimension_semantics=("arbitrary", "arbitrary", "arbitrary")
        ),
        cost_estimate=pl.CostEstimate(
            flops=2 * 2 * tok_rows * key_rows * width * 3 // 4,
            transcendentals=tok_rows * key_rows * heads * 3 // 4,
            bytes_accessed=2 * tok_rows * width + 2 * 2 * key_rows * width + 6 * 4 * tok_rows * width,
        ),
    )(*operands)


def cached_attention(meta, queries, received, acc, m, l):
    tok_rows, width = queries.shape
    heads = width // HS
    groups, _, per_dev, block_len, _ = received.shape

    def kv_map(index):
        def index_map(h, c, meta):
            last = (meta[1] + groups * block_len - 1) // (groups * block_len) - 1
            return (0, index, jnp.minimum(c, last), 0, h)

        return index_map

    kv_block = (groups, None, None, block_len, HS)
    state_spec = pl.BlockSpec((tok_rows, HS), lambda h, c, meta: (0, h))
    keys_total = groups * per_dev * block_len
    return pl.pallas_call(
        functools.partial(
            cached_kernel, groups=groups, block_len=block_len
        ),
        out_shape=jax.ShapeDtypeStruct((tok_rows, width), jnp.bfloat16),
        grid_spec=pltpu.PrefetchScalarGridSpec(
            num_scalar_prefetch=1,
            grid=(heads, per_dev),
            in_specs=[
                pl.BlockSpec((tok_rows, HS), lambda h, c, meta: (0, h)),
                pl.BlockSpec(kv_block, kv_map(0)),
                pl.BlockSpec(kv_block, kv_map(1)),
                state_spec,
                state_spec,
                state_spec,
            ],
            out_specs=pl.BlockSpec((tok_rows, HS), lambda h, c, meta: (0, h)),
            scratch_shapes=[
                pltpu.VMEM((tok_rows, HS), jnp.float32),
                pltpu.VMEM((tok_rows, HS), jnp.float32),
                pltpu.VMEM((tok_rows, HS), jnp.float32),
            ],
        ),
        compiler_params=pltpu.CompilerParams(dimension_semantics=("arbitrary", "arbitrary")),
        cost_estimate=pl.CostEstimate(
            flops=2 * 2 * tok_rows * keys_total * width // 2,
            transcendentals=tok_rows * keys_total * heads // 2,
            bytes_accessed=2 * keys_total * width + 2 * tok_rows * width * 2 + 3 * 4 * tok_rows * width,
        ),
    )(meta, queries, received, received, acc, m, l)


def body(states, qkv_weight, norm_gains, kv_cache, cached_len, old_table, new_table):
    tok_rows = states.shape[0]
    half_rows = tok_rows // 2
    local_width = qkv_weight.shape[2]
    local_heads = local_width // HS
    pair = lax.axis_size("bp")
    groups = lax.axis_size("bx") * pair
    slot_count = kv_cache.shape[1]
    block_len = kv_cache.shape[2]
    per_dev = old_table.shape[1] // groups
    request = lax.axis_index("bx")
    member = lax.axis_index("bp")
    my_index = request * pair + member
    late_block = 2 * pair - 1 - member
    targets = jnp.arange(groups, dtype=jnp.int32)
    kv_ids = jnp.arange(2, dtype=jnp.int32)
    kv_flat = kv_cache.reshape(2 * slot_count, block_len, local_width)

    first_dev = old_table[:, 0] // slot_count
    target_req = targets // pair
    c_index = jnp.arange(per_dev, dtype=jnp.int32)
    block_index = ((my_index - first_dev[target_req]) % groups)[:, None] + groups * c_index[None, :]
    slot_index = (
        old_table[target_req[:, None], jnp.clip(block_index, 0, old_table.shape[1] - 1)]
        - my_index * slot_count
    )
    slot_index = jnp.clip(slot_index, 0, slot_count - 1)
    out_ids = kv_ids[None, :, None] * slot_count + slot_index[:, None, :]
    outgoing = jnp.take(kv_flat, out_ids.reshape(-1), axis=0, mode="clip").reshape(
        groups, 2, per_dev, block_len, local_width
    )
    received = lax.all_to_all(
        outgoing, ("bx", "bp"), split_axis=0, concat_axis=0, tiled=True
    )

    projected = jnp.einsum(
        "tc,jcw->tjw",
        lax.all_gather(states, "head", axis=1, tiled=True),
        qkv_weight,
        preferred_element_type=jnp.float32,
    )
    queries = projected[:, 0]
    key_new = projected[:, 1]
    value_new = projected[:, 2]
    query_sq, key_sq = lax.psum(
        (jnp.sum(queries * queries, axis=1), jnp.sum(key_new * key_new, axis=1)), "head"
    )
    gains = norm_gains.astype(jnp.float32)
    queries = queries * lax.rsqrt(query_sq / D + norm_eps)[:, None] * gains[0]
    key_new = key_new * lax.rsqrt(key_sq / D + norm_eps)[:, None] * gains[1]
    half_ids = jnp.arange(half_rows, dtype=jnp.int32)
    token_offset = jnp.concatenate(
        [member * half_rows + half_ids, late_block * half_rows + half_ids]
    )
    positions = cached_len[request] + token_offset
    queries = (
        rotate(queries.reshape(tok_rows, local_heads, HS), positions, HS)
        .reshape(tok_rows, local_width)
        .astype(jnp.bfloat16)
    )
    key_new = (
        rotate(key_new.reshape(tok_rows, local_heads, HS), positions, HS)
        .reshape(tok_rows, local_width)
        .astype(jnp.bfloat16)
    )
    value_new = value_new.astype(jnp.bfloat16)
    fresh_kv = jnp.stack([key_new, value_new])
    meta = jnp.stack([member, cached_len[request], first_dev[request], 0]).astype(jnp.int32)

    partner_new = lax.ppermute(fresh_kv, "bp", [(0, 1), (1, 0)])
    state = new_attention(meta, queries, fresh_kv[0], fresh_kv[1])

    blocks_dev = tok_rows // block_len
    chunk_blocks = blocks_dev // 2
    collected = jnp.where(
        member == 0,
        jnp.concatenate([fresh_kv, partner_new], axis=1),
        jnp.concatenate([partner_new, fresh_kv], axis=1),
    )
    new_blocks = 2 * blocks_dev
    collected_flat = collected.reshape(2 * new_blocks, block_len, local_width)
    chunk_place = jnp.array([0, 2, 3, 1], dtype=jnp.int32)
    new_home = new_table[:, 0] // slot_count
    pair_index = jnp.arange(2, dtype=jnp.int32)
    reqs = jnp.arange(groups // pair, dtype=jnp.int32)
    dest = reqs * pair + member
    wanted_out = 2 * ((dest - new_home[request]) % groups)[:, None] + pair_index[None, :]
    place = chunk_place[wanted_out // chunk_blocks] * chunk_blocks + wanted_out % chunk_blocks
    pick_ids = kv_ids[None, :, None] * new_blocks + place[:, None, :]
    picked = jnp.take(collected_flat, pick_ids.reshape(-1), axis=0, mode="clip").reshape(
        groups // pair, 2, 2, block_len, local_width
    )
    arrived = lax.all_to_all(picked, "bx", split_axis=0, concat_axis=0, tiled=True)
    wanted_in = 2 * ((my_index - new_home) % groups)[:, None] + pair_index[None, :]
    target_slot = (
        new_table[reqs[:, None], jnp.clip(wanted_in, 0, new_table.shape[1] - 1)]
        - my_index * slot_count
    )
    target_ids = kv_ids[None, :, None] * slot_count + target_slot[:, None, :]
    updated_cache = (
        kv_flat.at[target_ids.reshape(-1)]
        .set(arrived.reshape(-1, block_len, local_width), mode="drop")
        .reshape(kv_cache.shape)
    )

    state = new_attention(meta, queries, partner_new[0], partner_new[1], state)
    attended = cached_attention(meta, queries, received, *state)
    return (attended, updated_cache)


def solution(mesh):
    heads, groups = mesh.devices.shape
    split = jax.sharding.Mesh(mesh.devices.reshape(heads, groups // 2, 2), ("head", "bx", "bp"))
    blk = ("bx", "bp")
    return jax.shard_map(
        body,
        mesh=split,
        in_specs=(
            P(blk, "head"),
            P(None, None, "head"),
            P(None, "head"),
            P(None, blk, None, "head"),
            P(),
            P(),
            P(),
        ),
        out_specs=(P(blk, "head"), P(None, blk, None, "head")),
        check_vma=False,
    )
```

```python
import functools

import jax
import jax.numpy as jnp
from jax import lax
from jax.experimental import pallas as pl
from jax.experimental.pallas import tpu as pltpu
from jax.sharding import PartitionSpec as P


D = 4096
HS = 128


rope_base = 500000.0
norm_eps = 1e-06
score_scale = HS ** (-0.5)
scale2 = score_scale * 1.4426950408889634


def rotate(values, positions, head_size):
    half_size = head_size // 2
    frequency = rope_base ** (-jnp.arange(half_size, dtype=jnp.float32) * 2.0 / head_size)
    angles = positions.astype(jnp.float32)[:, None] * frequency[None, :]
    cosine = jnp.cos(angles)[:, None, :]
    sine_part = jnp.sin(angles)[:, None, :]
    first_half = values[..., :half_size]
    second = values[..., half_size:]
    return jnp.concatenate(
        [first_half * cosine - second * sine_part, second * cosine + first_half * sine_part],
        axis=-1,
    )


def online_update(s, v, m_sc, l_sc, acc_sc):
    m_prev = m_sc[...]
    m_cur = jnp.max(s, axis=1, keepdims=True) * scale2
    m_next = jnp.maximum(m_prev, m_cur)
    alpha = jnp.exp2(m_prev - m_next)
    p = jnp.exp2(s * scale2 - m_next[:, :1])
    l_sc[...] = alpha * l_sc[...] + jnp.sum(p, axis=1, keepdims=True)
    pv = jnp.dot(p.astype(jnp.bfloat16), v, preferred_element_type=jnp.float32)
    acc_sc[...] = acc_sc[...] * alpha + pv
    m_sc[...] = m_next


def scores_of(q, k):
    return lax.dot_general(q, k, (((1,), (1,)), ((), ())), preferred_element_type=jnp.float32)


def new_kernel(meta_ref, q_ref, k_ref, v_ref, *rest, partner):
    if partner:
        acc_in, m_in, l_in, acc_out, m_out, l_out, m_sc, l_sc, acc_sc = rest
    else:
        acc_out, m_out, l_out, m_sc, l_sc, acc_sc = rest
    qi = pl.program_id(1)
    kj = pl.program_id(2)
    member = meta_ref[0]
    q_chunk = jnp.where(qi == 0, member, 3 - member)
    if partner:
        k_chunk = jnp.where(kj == 0, 1 - member, 2 + member)
    else:
        k_chunk = jnp.where(kj == 0, member, 3 - member)

    @pl.when(kj == 0)
    def _():
        if partner:
            m_sc[...] = m_in[...]
            l_sc[...] = l_in[...]
            acc_sc[...] = acc_in[...]
        else:
            m_sc[...] = jnp.full(m_sc.shape, -jnp.inf, jnp.float32)
            l_sc[...] = jnp.zeros(l_sc.shape, jnp.float32)
            acc_sc[...] = jnp.zeros(acc_sc.shape, jnp.float32)

    @pl.when(k_chunk < q_chunk)
    def _():
        s = scores_of(q_ref[...], k_ref[...])
        online_update(s, v_ref[...], m_sc, l_sc, acc_sc)

    @pl.when(k_chunk == q_chunk)
    def _():
        s = scores_of(q_ref[...], k_ref[...])
        rows = lax.broadcasted_iota(jnp.int32, s.shape, 0)
        cols = lax.broadcasted_iota(jnp.int32, s.shape, 1)
        s = jnp.where(cols <= rows, s, -jnp.inf)
        online_update(s, v_ref[...], m_sc, l_sc, acc_sc)

    @pl.when(kj == pl.num_programs(2) - 1)
    def _():
        acc_out[...] = acc_sc[...]
        m_out[...] = m_sc[...]
        l_out[...] = l_sc[...]


def partner_kernel(meta_ref, q_ref, k_ref, v_ref, acc_in, m_in, l_in, acc_out, m_out, l_out):
    member = meta_ref[0]
    rows = q_ref.shape[0]
    half = rows // 2
    acc_out[...] = acc_in[...]
    m_out[...] = m_in[...]
    l_out[...] = l_in[...]

    @pl.when(member == 0)
    def _():
        s = scores_of(q_ref[pl.ds(half, half), :], k_ref[...])
        online_update(
            s, v_ref[...], m_out.at[pl.ds(half, half)], l_out.at[pl.ds(half, half)],
            acc_out.at[pl.ds(half, half)],
        )

    @pl.when(member != 0)
    def _():
        s = scores_of(q_ref[...], k_ref[pl.ds(0, half), :])
        online_update(s, v_ref[pl.ds(0, half), :], m_out, l_out, acc_out)


def partner_attention(meta, queries, keys, values, state):
    tok_rows, width = queries.shape
    heads = width // HS
    shape = jax.ShapeDtypeStruct((tok_rows, width), jnp.float32)
    spec = pl.BlockSpec((tok_rows, HS), lambda h, meta: (0, h))
    return pl.pallas_call(
        partner_kernel,
        out_shape=(shape, shape, shape),
        grid_spec=pltpu.PrefetchScalarGridSpec(
            num_scalar_prefetch=1,
            grid=(heads,),
            in_specs=[spec] * 6,
            out_specs=[spec] * 3,
        ),
        compiler_params=pltpu.CompilerParams(dimension_semantics=("arbitrary",)),
        cost_estimate=pl.CostEstimate(
            flops=2 * 2 * tok_rows * tok_rows * width // 2,
            transcendentals=tok_rows * tok_rows * heads // 2,
            bytes_accessed=3 * 2 * tok_rows * width + 6 * 4 * tok_rows * width,
        ),
    )(meta, queries, keys, values, *state)


def cached_kernel(meta_ref, q_ref, k_ref, v_ref, acc_in, m_in, l_in, o_ref, m_sc, l_sc, acc_sc,
                  *, groups, block_len):
    c = pl.program_id(1)
    length = meta_ref[1]
    first = meta_ref[2]
    tile = groups * block_len

    @pl.when(c == 0)
    def _():
        m_sc[...] = m_in[...]
        l_sc[...] = l_in[...]
        acc_sc[...] = acc_in[...]

    @pl.when((c + 1) * groups * block_len <= length)
    def _():
        k = k_ref[...].reshape(tile, HS)
        v = v_ref[...].reshape(tile, HS)
        s = scores_of(q_ref[...], k)
        online_update(s, v, m_sc, l_sc, acc_sc)

    @pl.when((c * groups * block_len < length) & ((c + 1) * groups * block_len > length))
    def _():
        k = k_ref[...].reshape(tile, HS)
        v = v_ref[...].reshape(tile, HS)
        s = scores_of(q_ref[...], k)
        cols = lax.broadcasted_iota(jnp.int32, (1, tile), 1)
        src = cols // block_len
        block = (src - first + groups) % groups + groups * c
        visible = block * block_len + cols % block_len < length
        s = jnp.where(visible, s, -jnp.inf)
        online_update(s, v, m_sc, l_sc, acc_sc)

    @pl.when(c == pl.num_programs(1) - 1)
    def _():
        o_ref[...] = (acc_sc[...] / l_sc[...]).astype(o_ref.dtype)


def new_attention(meta, queries, keys, values, state=None):
    tok_rows, width = queries.shape
    heads = width // HS
    q_rows = tok_rows // 2
    key_rows = keys.shape[0]
    k_tiles = key_rows // q_rows
    partner = state is not None
    shape = jax.ShapeDtypeStruct((tok_rows, width), jnp.float32)
    state_spec = pl.BlockSpec((q_rows, HS), lambda h, i, j, meta: (i, h))
    in_specs = [
        pl.BlockSpec((q_rows, HS), lambda h, i, j, meta: (i, h)),
        pl.BlockSpec((q_rows, HS), lambda h, i, j, meta: (j, h)),
        pl.BlockSpec((q_rows, HS), lambda h, i, j, meta: (j, h)),
    ]
    operands = [meta, queries, keys, values]
    if partner:
        in_specs += [state_spec] * 3
        operands += list(state)
    return pl.pallas_call(
        functools.partial(new_kernel, partner=partner),
        out_shape=(shape, shape, shape),
        grid_spec=pltpu.PrefetchScalarGridSpec(
            num_scalar_prefetch=1,
            grid=(heads, 2, k_tiles),
            in_specs=in_specs,
            out_specs=[state_spec, state_spec, state_spec],
            scratch_shapes=[
                pltpu.VMEM((q_rows, HS), jnp.float32),
                pltpu.VMEM((q_rows, HS), jnp.float32),
                pltpu.VMEM((q_rows, HS), jnp.float32),
            ],
        ),
        compiler_params=pltpu.CompilerParams(
            dimension_semantics=("arbitrary", "arbitrary", "arbitrary")
        ),
        cost_estimate=pl.CostEstimate(
            flops=2 * 2 * tok_rows * key_rows * width * 3 // 4,
            transcendentals=tok_rows * key_rows * heads * 3 // 4,
            bytes_accessed=2 * tok_rows * width + 2 * 2 * key_rows * width + 6 * 4 * tok_rows * width,
        ),
    )(*operands)


def cached_attention(meta, queries, received, acc, m, l):
    tok_rows, width = queries.shape
    heads = width // HS
    groups, _, per_dev, block_len, _ = received.shape

    def kv_map(index):
        def index_map(h, c, meta):
            last = (meta[1] + groups * block_len - 1) // (groups * block_len) - 1
            return (0, index, jnp.minimum(c, last), 0, h)

        return index_map

    kv_block = (groups, None, None, block_len, HS)
    state_spec = pl.BlockSpec((tok_rows, HS), lambda h, c, meta: (0, h))
    keys_total = groups * per_dev * block_len
    return pl.pallas_call(
        functools.partial(
            cached_kernel, groups=groups, block_len=block_len
        ),
        out_shape=jax.ShapeDtypeStruct((tok_rows, width), jnp.bfloat16),
        grid_spec=pltpu.PrefetchScalarGridSpec(
            num_scalar_prefetch=1,
            grid=(heads, per_dev),
            in_specs=[
                pl.BlockSpec((tok_rows, HS), lambda h, c, meta: (0, h)),
                pl.BlockSpec(kv_block, kv_map(0)),
                pl.BlockSpec(kv_block, kv_map(1)),
                state_spec,
                state_spec,
                state_spec,
            ],
            out_specs=pl.BlockSpec((tok_rows, HS), lambda h, c, meta: (0, h)),
            scratch_shapes=[
                pltpu.VMEM((tok_rows, HS), jnp.float32),
                pltpu.VMEM((tok_rows, HS), jnp.float32),
                pltpu.VMEM((tok_rows, HS), jnp.float32),
            ],
        ),
        compiler_params=pltpu.CompilerParams(dimension_semantics=("arbitrary", "arbitrary")),
        cost_estimate=pl.CostEstimate(
            flops=2 * 2 * tok_rows * keys_total * width // 2,
            transcendentals=tok_rows * keys_total * heads // 2,
            bytes_accessed=2 * keys_total * width + 2 * tok_rows * width * 2 + 3 * 4 * tok_rows * width,
        ),
    )(meta, queries, received, received, acc, m, l)


def body(states, qkv_weight, norm_gains, kv_cache, cached_len, old_table, new_table):
    tok_rows = states.shape[0]
    half_rows = tok_rows // 2
    local_width = qkv_weight.shape[2]
    local_heads = local_width // HS
    pair = lax.axis_size("bp")
    groups = lax.axis_size("bx") * pair
    slot_count = kv_cache.shape[1]
    block_len = kv_cache.shape[2]
    per_dev = old_table.shape[1] // groups
    request = lax.axis_index("bx")
    member = lax.axis_index("bp")
    my_index = request * pair + member
    late_block = 2 * pair - 1 - member
    targets = jnp.arange(groups, dtype=jnp.int32)
    kv_ids = jnp.arange(2, dtype=jnp.int32)
    kv_flat = kv_cache.reshape(2 * slot_count, block_len, local_width)

    first_dev = old_table[:, 0] // slot_count
    target_req = targets // pair
    c_index = jnp.arange(per_dev, dtype=jnp.int32)
    block_index = ((my_index - first_dev[target_req]) % groups)[:, None] + groups * c_index[None, :]
    slot_index = (
        old_table[target_req[:, None], jnp.clip(block_index, 0, old_table.shape[1] - 1)]
        - my_index * slot_count
    )
    slot_index = jnp.clip(slot_index, 0, slot_count - 1)
    out_ids = kv_ids[None, :, None] * slot_count + slot_index[:, None, :]
    outgoing = jnp.take(kv_flat, out_ids.reshape(-1), axis=0, mode="clip").reshape(
        groups, 2, per_dev, block_len, local_width
    )
    received = lax.all_to_all(
        outgoing, ("bx", "bp"), split_axis=0, concat_axis=0, tiled=True
    )

    projected = jnp.einsum(
        "tc,jcw->tjw",
        lax.all_gather(states, "head", axis=1, tiled=True),
        qkv_weight,
        preferred_element_type=jnp.float32,
    )
    queries = projected[:, 0]
    key_new = projected[:, 1]
    value_new = projected[:, 2]
    query_sq, key_sq = lax.psum(
        (jnp.sum(queries * queries, axis=1), jnp.sum(key_new * key_new, axis=1)), "head"
    )
    gains = norm_gains.astype(jnp.float32)
    queries = queries * lax.rsqrt(query_sq / D + norm_eps)[:, None] * gains[0]
    key_new = key_new * lax.rsqrt(key_sq / D + norm_eps)[:, None] * gains[1]
    half_ids = jnp.arange(half_rows, dtype=jnp.int32)
    token_offset = jnp.concatenate(
        [member * half_rows + half_ids, late_block * half_rows + half_ids]
    )
    positions = cached_len[request] + token_offset
    queries = (
        rotate(queries.reshape(tok_rows, local_heads, HS), positions, HS)
        .reshape(tok_rows, local_width)
        .astype(jnp.bfloat16)
    )
    key_new = (
        rotate(key_new.reshape(tok_rows, local_heads, HS), positions, HS)
        .reshape(tok_rows, local_width)
        .astype(jnp.bfloat16)
    )
    value_new = value_new.astype(jnp.bfloat16)
    fresh_kv = jnp.stack([key_new, value_new])
    meta = jnp.stack([member, cached_len[request], first_dev[request], 0]).astype(jnp.int32)

    partner_new = lax.ppermute(fresh_kv, "bp", [(0, 1), (1, 0)])
    state = new_attention(meta, queries, fresh_kv[0], fresh_kv[1])

    blocks_dev = tok_rows // block_len
    chunk_blocks = blocks_dev // 2
    collected = jnp.where(
        member == 0,
        jnp.concatenate([fresh_kv, partner_new], axis=1),
        jnp.concatenate([partner_new, fresh_kv], axis=1),
    )
    new_blocks = 2 * blocks_dev
    collected_flat = collected.reshape(2 * new_blocks, block_len, local_width)
    chunk_place = jnp.array([0, 2, 3, 1], dtype=jnp.int32)
    new_home = new_table[:, 0] // slot_count
    pair_index = jnp.arange(2, dtype=jnp.int32)
    reqs = jnp.arange(groups // pair, dtype=jnp.int32)
    dest = reqs * pair + member
    wanted_out = 2 * ((dest - new_home[request]) % groups)[:, None] + pair_index[None, :]
    place = chunk_place[wanted_out // chunk_blocks] * chunk_blocks + wanted_out % chunk_blocks
    pick_ids = kv_ids[None, :, None] * new_blocks + place[:, None, :]
    picked = jnp.take(collected_flat, pick_ids.reshape(-1), axis=0, mode="clip").reshape(
        groups // pair, 2, 2, block_len, local_width
    )
    arrived = lax.all_to_all(picked, "bx", split_axis=0, concat_axis=0, tiled=True)
    wanted_in = 2 * ((my_index - new_home) % groups)[:, None] + pair_index[None, :]
    target_slot = (
        new_table[reqs[:, None], jnp.clip(wanted_in, 0, new_table.shape[1] - 1)]
        - my_index * slot_count
    )
    target_ids = kv_ids[None, :, None] * slot_count + target_slot[:, None, :]
    updated_cache = (
        kv_flat.at[target_ids.reshape(-1)]
        .set(arrived.reshape(-1, block_len, local_width), mode="drop")
        .reshape(kv_cache.shape)
    )

    state = partner_attention(meta, queries, partner_new[0], partner_new[1], state)
    attended = cached_attention(meta, queries, received, *state)
    return (attended, updated_cache)


def solution(mesh):
    heads, groups = mesh.devices.shape
    split = jax.sharding.Mesh(mesh.devices.reshape(heads, groups // 2, 2), ("head", "bx", "bp"))
    blk = ("bx", "bp")
    return jax.shard_map(
        body,
        mesh=split,
        in_specs=(
            P(blk, "head"),
            P(None, None, "head"),
            P(None, "head"),
            P(None, blk, None, "head"),
            P(),
            P(),
            P(),
        ),
        out_specs=(P(blk, "head"), P(None, blk, None, "head")),
        check_vma=False,
    )
```

```python
import functools

import jax
import jax.numpy as jnp
from jax import lax
from jax.experimental import pallas as pl
from jax.experimental.pallas import tpu as pltpu
from jax.sharding import PartitionSpec as P


D = 4096
HS = 128


rope_base = 500000.0
norm_eps = 1e-06
score_scale = HS ** (-0.5)
scale2 = score_scale * 1.4426950408889634


def rotate(values, positions, head_size):
    half_size = head_size // 2
    frequency = rope_base ** (-jnp.arange(half_size, dtype=jnp.float32) * 2.0 / head_size)
    angles = positions.astype(jnp.float32)[:, None] * frequency[None, :]
    cosine = jnp.cos(angles)[:, None, :]
    sine_part = jnp.sin(angles)[:, None, :]
    first_half = values[..., :half_size]
    second = values[..., half_size:]
    return jnp.concatenate(
        [first_half * cosine - second * sine_part, second * cosine + first_half * sine_part],
        axis=-1,
    )


def online_update(s, v, m_sc, l_sc, acc_sc):
    m_prev = m_sc[...]
    m_cur = jnp.max(s, axis=1, keepdims=True) * scale2
    m_next = jnp.maximum(m_prev, m_cur)
    alpha = jnp.exp2(m_prev - m_next)
    p = jnp.exp2(s * scale2 - m_next[:, :1]).astype(jnp.bfloat16)
    v_ext = jnp.concatenate([v, jnp.ones(v.shape, v.dtype)], axis=1)
    pv = jnp.dot(p, v_ext, preferred_element_type=jnp.float32)
    acc_sc[...] = acc_sc[...] * alpha + pv[:, :HS]
    l_sc[...] = l_sc[...] * alpha + pv[:, HS:]
    m_sc[...] = m_next


def scores_of(q, k):
    return lax.dot_general(q, k, (((1,), (1,)), ((), ())), preferred_element_type=jnp.float32)


def new_kernel(meta_ref, q_ref, k_ref, v_ref, *rest, partner):
    if partner:
        acc_in, m_in, l_in, acc_out, m_out, l_out, m_sc, l_sc, acc_sc = rest
    else:
        acc_out, m_out, l_out, m_sc, l_sc, acc_sc = rest
    qi = pl.program_id(1)
    kj = pl.program_id(2)
    member = meta_ref[0]
    q_chunk = jnp.where(qi == 0, member, 3 - member)
    if partner:
        k_chunk = jnp.where(kj == 0, 1 - member, 2 + member)
    else:
        k_chunk = jnp.where(kj == 0, member, 3 - member)

    @pl.when(kj == 0)
    def _():
        if partner:
            m_sc[...] = m_in[...]
            l_sc[...] = l_in[...]
            acc_sc[...] = acc_in[...]
        else:
            m_sc[...] = jnp.full(m_sc.shape, -jnp.inf, jnp.float32)
            l_sc[...] = jnp.zeros(l_sc.shape, jnp.float32)
            acc_sc[...] = jnp.zeros(acc_sc.shape, jnp.float32)

    @pl.when(k_chunk <= q_chunk)
    def _():
        s = scores_of(q_ref[...], k_ref[...])
        rows = lax.broadcasted_iota(jnp.int32, s.shape, 0)
        cols = lax.broadcasted_iota(jnp.int32, s.shape, 1)
        s = jnp.where((k_chunk < q_chunk) | (cols <= rows), s, -jnp.inf)
        online_update(s, v_ref[...], m_sc, l_sc, acc_sc)

    @pl.when(kj == pl.num_programs(2) - 1)
    def _():
        acc_out[...] = acc_sc[...]
        m_out[...] = m_sc[...]
        l_out[...] = l_sc[...]


def partner_kernel(meta_ref, q_ref, k_ref, v_ref, acc_in, m_in, l_in, acc_out, m_out, l_out):
    k_ref = k_ref.at[0]
    v_ref = v_ref.at[0]
    member = meta_ref[0]
    rows = q_ref.shape[0]
    half = rows // 2
    acc_out[...] = acc_in[...]
    m_out[...] = m_in[...]
    l_out[...] = l_in[...]

    @pl.when(member == 0)
    def _():
        s = scores_of(q_ref[pl.ds(half, half), :], k_ref[...])
        online_update(
            s, v_ref[...], m_out.at[pl.ds(half, half)], l_out.at[pl.ds(half, half)],
            acc_out.at[pl.ds(half, half)],
        )

    @pl.when(member != 0)
    def _():
        s = scores_of(q_ref[...], k_ref[pl.ds(0, half), :])
        online_update(s, v_ref[pl.ds(0, half), :], m_out, l_out, acc_out)


def partner_attention(meta, queries, partner_new, state):
    tok_rows, width = queries.shape
    heads = width // HS
    shape = jax.ShapeDtypeStruct((tok_rows, width), jnp.float32)
    spec = pl.BlockSpec((tok_rows, HS), lambda h, meta: (0, h))
    key_spec = pl.BlockSpec((1, tok_rows, HS), lambda h, meta: (0, 0, h))
    value_spec = pl.BlockSpec((1, tok_rows, HS), lambda h, meta: (1, 0, h))
    return pl.pallas_call(
        partner_kernel,
        out_shape=(shape, shape, shape),
        grid_spec=pltpu.PrefetchScalarGridSpec(
            num_scalar_prefetch=1,
            grid=(heads,),
            in_specs=[spec, key_spec, value_spec, spec, spec, spec],
            out_specs=[spec] * 3,
        ),
        compiler_params=pltpu.CompilerParams(dimension_semantics=("arbitrary",)),
        cost_estimate=pl.CostEstimate(
            flops=2 * 2 * tok_rows * tok_rows * width // 2,
            transcendentals=tok_rows * tok_rows * heads // 2,
            bytes_accessed=3 * 2 * tok_rows * width + 6 * 4 * tok_rows * width,
        ),
    )(meta, queries, partner_new, partner_new, *state)


def cached_kernel(meta_ref, q_ref, k_ref, v_ref, acc_in, m_in, l_in, o_ref, m_sc, l_sc, acc_sc,
                  *, groups, block_len):
    c = pl.program_id(1)
    length = meta_ref[1]
    first = meta_ref[2]
    tile = groups * block_len

    @pl.when(c == 0)
    def _():
        m_sc[...] = m_in[...]
        l_sc[...] = l_in[...]
        acc_sc[...] = acc_in[...]

    @pl.when((c + 1) * groups * block_len <= length)
    def _():
        k = k_ref[...].reshape(tile, HS)
        v = v_ref[...].reshape(tile, HS)
        s = scores_of(q_ref[...], k)
        online_update(s, v, m_sc, l_sc, acc_sc)

    @pl.when((c * groups * block_len < length) & ((c + 1) * groups * block_len > length))
    def _():
        k = k_ref[...].reshape(tile, HS)
        v = v_ref[...].reshape(tile, HS)
        s = scores_of(q_ref[...], k)
        cols = lax.broadcasted_iota(jnp.int32, (1, tile), 1)
        src = cols // block_len
        block = (src - first + groups) % groups + groups * c
        visible = block * block_len + cols % block_len < length
        s = jnp.where(visible, s, -jnp.inf)
        online_update(s, v, m_sc, l_sc, acc_sc)

    @pl.when(c == pl.num_programs(1) - 1)
    def _():
        o_ref[...] = (acc_sc[...] / l_sc[...]).astype(o_ref.dtype)


def new_attention(meta, queries, keys, values, state=None):
    tok_rows, width = queries.shape
    heads = width // HS
    q_rows = tok_rows // 2
    key_rows = keys.shape[0]
    k_tiles = key_rows // q_rows
    partner = state is not None
    shape = jax.ShapeDtypeStruct((tok_rows, width), jnp.float32)
    state_spec = pl.BlockSpec((q_rows, HS), lambda h, i, j, meta: (i, h))
    in_specs = [
        pl.BlockSpec((q_rows, HS), lambda h, i, j, meta: (i, h)),
        pl.BlockSpec((q_rows, HS), lambda h, i, j, meta: (j, h)),
        pl.BlockSpec((q_rows, HS), lambda h, i, j, meta: (j, h)),
    ]
    operands = [meta, queries, keys, values]
    if partner:
        in_specs += [state_spec] * 3
        operands += list(state)
    return pl.pallas_call(
        functools.partial(new_kernel, partner=partner),
        out_shape=(shape, shape, shape),
        grid_spec=pltpu.PrefetchScalarGridSpec(
            num_scalar_prefetch=1,
            grid=(heads, 2, k_tiles),
            in_specs=in_specs,
            out_specs=[state_spec, state_spec, state_spec],
            scratch_shapes=[
                pltpu.VMEM((q_rows, HS), jnp.float32),
                pltpu.VMEM((q_rows, HS), jnp.float32),
                pltpu.VMEM((q_rows, HS), jnp.float32),
            ],
        ),
        compiler_params=pltpu.CompilerParams(
            dimension_semantics=("arbitrary", "arbitrary", "arbitrary")
        ),
        cost_estimate=pl.CostEstimate(
            flops=2 * 2 * tok_rows * key_rows * width * 3 // 4,
            transcendentals=tok_rows * key_rows * heads * 3 // 4,
            bytes_accessed=2 * tok_rows * width + 2 * 2 * key_rows * width + 6 * 4 * tok_rows * width,
        ),
    )(*operands)


def cached_attention(meta, queries, received, acc, m, l):
    tok_rows, width = queries.shape
    heads = width // HS
    groups, _, per_dev, block_len, _ = received.shape

    def kv_map(index):
        def index_map(h, c, meta):
            last = (meta[1] + groups * block_len - 1) // (groups * block_len) - 1
            return (0, index, jnp.minimum(c, last), 0, h)

        return index_map

    kv_block = (groups, None, None, block_len, HS)
    state_spec = pl.BlockSpec((tok_rows, HS), lambda h, c, meta: (0, h))
    keys_total = groups * per_dev * block_len
    return pl.pallas_call(
        functools.partial(
            cached_kernel, groups=groups, block_len=block_len
        ),
        out_shape=jax.ShapeDtypeStruct((tok_rows, width), jnp.bfloat16),
        grid_spec=pltpu.PrefetchScalarGridSpec(
            num_scalar_prefetch=1,
            grid=(heads, per_dev),
            in_specs=[
                pl.BlockSpec((tok_rows, HS), lambda h, c, meta: (0, h)),
                pl.BlockSpec(kv_block, kv_map(0)),
                pl.BlockSpec(kv_block, kv_map(1)),
                state_spec,
                state_spec,
                state_spec,
            ],
            out_specs=pl.BlockSpec((tok_rows, HS), lambda h, c, meta: (0, h)),
            scratch_shapes=[
                pltpu.VMEM((tok_rows, HS), jnp.float32),
                pltpu.VMEM((tok_rows, HS), jnp.float32),
                pltpu.VMEM((tok_rows, HS), jnp.float32),
            ],
        ),
        compiler_params=pltpu.CompilerParams(dimension_semantics=("arbitrary", "arbitrary")),
        cost_estimate=pl.CostEstimate(
            flops=2 * 2 * tok_rows * keys_total * width // 2,
            transcendentals=tok_rows * keys_total * heads // 2,
            bytes_accessed=2 * keys_total * width + 2 * tok_rows * width * 2 + 3 * 4 * tok_rows * width,
        ),
    )(meta, queries, received, received, acc, m, l)


def body(states, qkv_weight, norm_gains, kv_cache, cached_len, old_table, new_table):
    tok_rows = states.shape[0]
    half_rows = tok_rows // 2
    local_width = qkv_weight.shape[2]
    local_heads = local_width // HS
    pair = lax.axis_size("bp")
    groups = lax.axis_size("bx") * pair
    slot_count = kv_cache.shape[1]
    block_len = kv_cache.shape[2]
    per_dev = old_table.shape[1] // groups
    request = lax.axis_index("bx")
    member = lax.axis_index("bp")
    my_index = request * pair + member
    late_block = 2 * pair - 1 - member
    targets = jnp.arange(groups, dtype=jnp.int32)
    kv_ids = jnp.arange(2, dtype=jnp.int32)
    kv_flat = kv_cache.reshape(2 * slot_count, block_len, local_width)

    first_dev = old_table[:, 0] // slot_count
    target_req = targets // pair
    c_index = jnp.arange(per_dev, dtype=jnp.int32)
    block_index = ((my_index - first_dev[target_req]) % groups)[:, None] + groups * c_index[None, :]
    slot_index = (
        old_table[target_req[:, None], jnp.clip(block_index, 0, old_table.shape[1] - 1)]
        - my_index * slot_count
    )
    slot_index = jnp.clip(slot_index, 0, slot_count - 1)
    out_ids = kv_ids[None, :, None] * slot_count + slot_index[:, None, :]
    outgoing = jnp.take(kv_flat, out_ids.reshape(-1), axis=0, mode="clip").reshape(
        groups, 2, per_dev, block_len, local_width
    )
    received = lax.all_to_all(
        outgoing, ("bx", "bp"), split_axis=0, concat_axis=0, tiled=True
    )

    projected = jnp.einsum(
        "tc,jcw->tjw",
        lax.all_gather(states, "head", axis=1, tiled=True),
        qkv_weight,
        preferred_element_type=jnp.float32,
    )
    queries = projected[:, 0]
    key_new = projected[:, 1]
    value_new = projected[:, 2]
    query_sq, key_sq = lax.psum(
        (jnp.sum(queries * queries, axis=1), jnp.sum(key_new * key_new, axis=1)), "head"
    )
    gains = norm_gains.astype(jnp.float32)
    queries = queries * lax.rsqrt(query_sq / D + norm_eps)[:, None] * gains[0]
    key_new = key_new * lax.rsqrt(key_sq / D + norm_eps)[:, None] * gains[1]
    half_ids = jnp.arange(half_rows, dtype=jnp.int32)
    token_offset = jnp.concatenate(
        [member * half_rows + half_ids, late_block * half_rows + half_ids]
    )
    positions = cached_len[request] + token_offset
    queries = (
        rotate(queries.reshape(tok_rows, local_heads, HS), positions, HS)
        .reshape(tok_rows, local_width)
        .astype(jnp.bfloat16)
    )
    key_new = (
        rotate(key_new.reshape(tok_rows, local_heads, HS), positions, HS)
        .reshape(tok_rows, local_width)
        .astype(jnp.bfloat16)
    )
    value_new = value_new.astype(jnp.bfloat16)
    fresh_kv = jnp.stack([key_new, value_new])
    meta = jnp.stack([member, cached_len[request], first_dev[request], 0]).astype(jnp.int32)

    partner_new = lax.ppermute(fresh_kv, "bp", [(0, 1), (1, 0)])
    state = new_attention(meta, queries, fresh_kv[0], fresh_kv[1])

    blocks_dev = tok_rows // block_len
    chunk_blocks = blocks_dev // 2
    new_home = new_table[:, 0] // slot_count
    pair_index = jnp.arange(2, dtype=jnp.int32)
    reqs = jnp.arange(groups // pair, dtype=jnp.int32)
    dest = reqs * pair + member
    wanted_out = 2 * ((dest - new_home[request]) % groups)[:, None] + pair_index[None, :]
    chunk = wanted_out // chunk_blocks
    within = wanted_out % chunk_blocks
    own_place = jnp.where(chunk == member, 0, 1) * chunk_blocks + within
    partner_place = jnp.where(chunk == 1 - member, 0, 1) * chunk_blocks + within
    is_own = (chunk == member) | (chunk == 3 - member)

    def pick(source, place):
        ids = kv_ids[None, :, None] * blocks_dev + place[:, None, :]
        return jnp.take(
            source.reshape(2 * blocks_dev, block_len, local_width), ids.reshape(-1), axis=0,
            mode="clip",
        ).reshape(groups // pair, 2, 2, block_len, local_width)

    picked = jnp.where(
        is_own[:, None, :, None, None], pick(fresh_kv, own_place), pick(partner_new, partner_place)
    )
    arrived = lax.all_to_all(picked, "bx", split_axis=0, concat_axis=0, tiled=True)
    wanted_in = 2 * ((my_index - new_home) % groups)[:, None] + pair_index[None, :]
    target_slot = (
        new_table[reqs[:, None], jnp.clip(wanted_in, 0, new_table.shape[1] - 1)]
        - my_index * slot_count
    )
    target_ids = kv_ids[None, :, None] * slot_count + target_slot[:, None, :]
    updated_cache = (
        kv_flat.at[target_ids.reshape(-1)]
        .set(arrived.reshape(-1, block_len, local_width), mode="drop")
        .reshape(kv_cache.shape)
    )

    state = partner_attention(meta, queries, partner_new, state)
    attended = cached_attention(meta, queries, received, *state)
    return (attended, updated_cache)


def solution(mesh):
    heads, groups = mesh.devices.shape
    split = jax.sharding.Mesh(mesh.devices.reshape(heads, groups // 2, 2), ("head", "bx", "bp"))
    blk = ("bx", "bp")
    return jax.shard_map(
        body,
        mesh=split,
        in_specs=(
            P(blk, "head"),
            P(None, None, "head"),
            P(None, "head"),
            P(None, blk, None, "head"),
            P(),
            P(),
            P(),
        ),
        out_specs=(P(blk, "head"), P(None, blk, None, "head")),
        check_vma=False,
    )
```

```python
import functools

import jax
import jax.numpy as jnp
from jax import lax
from jax.experimental import pallas as pl
from jax.experimental.pallas import tpu as pltpu
from jax.sharding import PartitionSpec as P


D = 4096
HS = 128


rope_base = 500000.0
norm_eps = 1e-06
score_scale = HS ** (-0.5)
scale2 = score_scale * 1.4426950408889634


def rotate(values, positions, head_size):
    half_size = head_size // 2
    frequency = rope_base ** (-jnp.arange(half_size, dtype=jnp.float32) * 2.0 / head_size)
    angles = positions.astype(jnp.float32)[:, None] * frequency[None, :]
    cosine = jnp.cos(angles)[:, None, :]
    sine_part = jnp.sin(angles)[:, None, :]
    first_half = values[..., :half_size]
    second = values[..., half_size:]
    return jnp.concatenate(
        [first_half * cosine - second * sine_part, second * cosine + first_half * sine_part],
        axis=-1,
    )


def online_update(s, v, m_sc, l_sc, acc_sc):
    m_prev = m_sc[...]
    m_cur = jnp.max(s, axis=1, keepdims=True) * scale2
    m_next = jnp.maximum(m_prev, m_cur)
    alpha = jnp.exp2(m_prev - m_next)
    p = jnp.exp2(s * scale2 - m_next[:, :1])
    l_sc[...] = alpha * l_sc[...] + jnp.sum(p, axis=1, keepdims=True)
    pv = jnp.dot(p.astype(jnp.bfloat16), v, preferred_element_type=jnp.float32)
    acc_sc[...] = acc_sc[...] * alpha + pv
    m_sc[...] = m_next


def scores_of(q, k):
    return lax.dot_general(q, k, (((1,), (1,)), ((), ())), preferred_element_type=jnp.float32)


def new_kernel(meta_ref, q_ref, k_ref, v_ref, *rest, partner):
    if partner:
        acc_in, m_in, l_in, acc_out, m_out, l_out, m_sc, l_sc, acc_sc = rest
    else:
        acc_out, m_out, l_out, m_sc, l_sc, acc_sc = rest
    qi = pl.program_id(1)
    kj = pl.program_id(2)
    member = meta_ref[0]
    q_chunk = jnp.where(qi == 0, member, 3 - member)
    if partner:
        k_chunk = jnp.where(kj == 0, 1 - member, 2 + member)
    else:
        k_chunk = jnp.where(kj == 0, member, 3 - member)

    @pl.when(kj == 0)
    def _():
        if partner:
            m_sc[...] = m_in[...]
            l_sc[...] = l_in[...]
            acc_sc[...] = acc_in[...]
        else:
            m_sc[...] = jnp.full(m_sc.shape, -jnp.inf, jnp.float32)
            l_sc[...] = jnp.zeros(l_sc.shape, jnp.float32)
            acc_sc[...] = jnp.zeros(acc_sc.shape, jnp.float32)

    @pl.when(k_chunk <= q_chunk)
    def _():
        s = scores_of(q_ref[...], k_ref[...])
        rows = lax.broadcasted_iota(jnp.int32, s.shape, 0)
        cols = lax.broadcasted_iota(jnp.int32, s.shape, 1)
        s = jnp.where((k_chunk < q_chunk) | (cols <= rows), s, -jnp.inf)
        online_update(s, v_ref[...], m_sc, l_sc, acc_sc)

    @pl.when(kj == pl.num_programs(2) - 1)
    def _():
        acc_out[...] = acc_sc[...]
        m_out[...] = m_sc[...]
        l_out[...] = l_sc[...]


def partner_kernel(meta_ref, q_ref, k_ref, v_ref, acc_in, m_in, l_in, acc_out, m_out, l_out):
    k_ref = k_ref.at[0]
    v_ref = v_ref.at[0]
    member = meta_ref[0]
    rows = q_ref.shape[0]
    half = rows // 2
    acc_out[...] = acc_in[...]
    m_out[...] = m_in[...]
    l_out[...] = l_in[...]

    @pl.when(member == 0)
    def _():
        s = scores_of(q_ref[pl.ds(half, half), :], k_ref[...])
        online_update(
            s, v_ref[...], m_out.at[pl.ds(half, half)], l_out.at[pl.ds(half, half)],
            acc_out.at[pl.ds(half, half)],
        )

    @pl.when(member != 0)
    def _():
        s = scores_of(q_ref[...], k_ref[pl.ds(0, half), :])
        online_update(s, v_ref[pl.ds(0, half), :], m_out, l_out, acc_out)


def partner_attention(meta, queries, partner_new, state):
    tok_rows, width = queries.shape
    heads = width // HS
    shape = jax.ShapeDtypeStruct((tok_rows, width), jnp.float32)
    spec = pl.BlockSpec((tok_rows, HS), lambda h, meta: (0, h))
    key_spec = pl.BlockSpec((1, tok_rows, HS), lambda h, meta: (0, 0, h))
    value_spec = pl.BlockSpec((1, tok_rows, HS), lambda h, meta: (1, 0, h))
    return pl.pallas_call(
        partner_kernel,
        out_shape=(shape, shape, shape),
        grid_spec=pltpu.PrefetchScalarGridSpec(
            num_scalar_prefetch=1,
            grid=(heads,),
            in_specs=[spec, key_spec, value_spec, spec, spec, spec],
            out_specs=[spec] * 3,
        ),
        compiler_params=pltpu.CompilerParams(dimension_semantics=("arbitrary",)),
        cost_estimate=pl.CostEstimate(
            flops=2 * 2 * tok_rows * tok_rows * width // 2,
            transcendentals=tok_rows * tok_rows * heads // 2,
            bytes_accessed=3 * 2 * tok_rows * width + 6 * 4 * tok_rows * width,
        ),
    )(meta, queries, partner_new, partner_new, *state)


def cached_kernel(meta_ref, q_ref, k_ref, v_ref, acc_in, m_in, l_in, o_ref, m_sc, l_sc, acc_sc,
                  *, groups, block_len):
    c = pl.program_id(1)
    length = meta_ref[1]
    first = meta_ref[2]
    tile = groups * block_len

    @pl.when(c == 0)
    def _():
        m_sc[...] = m_in[...]
        l_sc[...] = l_in[...]
        acc_sc[...] = acc_in[...]

    @pl.when((c + 1) * groups * block_len <= length)
    def _():
        k = k_ref[...].reshape(tile, HS)
        v = v_ref[...].reshape(tile, HS)
        s = scores_of(q_ref[...], k)
        online_update(s, v, m_sc, l_sc, acc_sc)

    @pl.when((c * groups * block_len < length) & ((c + 1) * groups * block_len > length))
    def _():
        k = k_ref[...].reshape(tile, HS)
        v = v_ref[...].reshape(tile, HS)
        s = scores_of(q_ref[...], k)
        cols = lax.broadcasted_iota(jnp.int32, (1, tile), 1)
        src = cols // block_len
        block = (src - first + groups) % groups + groups * c
        visible = block * block_len + cols % block_len < length
        s = jnp.where(visible, s, -jnp.inf)
        online_update(s, v, m_sc, l_sc, acc_sc)

    @pl.when(c == pl.num_programs(1) - 1)
    def _():
        o_ref[...] = (acc_sc[...] / l_sc[...]).astype(o_ref.dtype)


def new_attention(meta, queries, keys, values, state=None):
    tok_rows, width = queries.shape
    heads = width // HS
    q_rows = tok_rows // 2
    key_rows = keys.shape[0]
    k_tiles = key_rows // q_rows
    partner = state is not None
    shape = jax.ShapeDtypeStruct((tok_rows, width), jnp.float32)
    state_spec = pl.BlockSpec((q_rows, HS), lambda h, i, j, meta: (i, h))
    in_specs = [
        pl.BlockSpec((q_rows, HS), lambda h, i, j, meta: (i, h)),
        pl.BlockSpec((q_rows, HS), lambda h, i, j, meta: (j, h)),
        pl.BlockSpec((q_rows, HS), lambda h, i, j, meta: (j, h)),
    ]
    operands = [meta, queries, keys, values]
    if partner:
        in_specs += [state_spec] * 3
        operands += list(state)
    return pl.pallas_call(
        functools.partial(new_kernel, partner=partner),
        out_shape=(shape, shape, shape),
        grid_spec=pltpu.PrefetchScalarGridSpec(
            num_scalar_prefetch=1,
            grid=(heads, 2, k_tiles),
            in_specs=in_specs,
            out_specs=[state_spec, state_spec, state_spec],
            scratch_shapes=[
                pltpu.VMEM((q_rows, HS), jnp.float32),
                pltpu.VMEM((q_rows, HS), jnp.float32),
                pltpu.VMEM((q_rows, HS), jnp.float32),
            ],
        ),
        compiler_params=pltpu.CompilerParams(
            dimension_semantics=("arbitrary", "arbitrary", "arbitrary")
        ),
        cost_estimate=pl.CostEstimate(
            flops=2 * 2 * tok_rows * key_rows * width * 3 // 4,
            transcendentals=tok_rows * key_rows * heads * 3 // 4,
            bytes_accessed=2 * tok_rows * width + 2 * 2 * key_rows * width + 6 * 4 * tok_rows * width,
        ),
    )(*operands)


def cached_attention(meta, queries, received, acc, m, l):
    tok_rows, width = queries.shape
    heads = width // HS
    groups, _, per_dev, block_len, _ = received.shape

    def kv_map(index):
        def index_map(h, c, meta):
            last = (meta[1] + groups * block_len - 1) // (groups * block_len) - 1
            return (0, index, jnp.minimum(c, last), 0, h)

        return index_map

    kv_block = (groups, None, None, block_len, HS)
    state_spec = pl.BlockSpec((tok_rows, HS), lambda h, c, meta: (0, h))
    keys_total = groups * per_dev * block_len
    return pl.pallas_call(
        functools.partial(
            cached_kernel, groups=groups, block_len=block_len
        ),
        out_shape=jax.ShapeDtypeStruct((tok_rows, width), jnp.bfloat16),
        grid_spec=pltpu.PrefetchScalarGridSpec(
            num_scalar_prefetch=1,
            grid=(heads, per_dev),
            in_specs=[
                pl.BlockSpec((tok_rows, HS), lambda h, c, meta: (0, h)),
                pl.BlockSpec(kv_block, kv_map(0)),
                pl.BlockSpec(kv_block, kv_map(1)),
                state_spec,
                state_spec,
                state_spec,
            ],
            out_specs=pl.BlockSpec((tok_rows, HS), lambda h, c, meta: (0, h)),
            scratch_shapes=[
                pltpu.VMEM((tok_rows, HS), jnp.float32),
                pltpu.VMEM((tok_rows, HS), jnp.float32),
                pltpu.VMEM((tok_rows, HS), jnp.float32),
            ],
        ),
        compiler_params=pltpu.CompilerParams(dimension_semantics=("arbitrary", "arbitrary")),
        cost_estimate=pl.CostEstimate(
            flops=2 * 2 * tok_rows * keys_total * width // 2,
            transcendentals=tok_rows * keys_total * heads // 2,
            bytes_accessed=2 * keys_total * width + 2 * tok_rows * width * 2 + 3 * 4 * tok_rows * width,
        ),
    )(meta, queries, received, received, acc, m, l)


def body(states, qkv_weight, norm_gains, kv_cache, cached_len, old_table, new_table):
    tok_rows = states.shape[0]
    half_rows = tok_rows // 2
    local_width = qkv_weight.shape[2]
    local_heads = local_width // HS
    pair = lax.axis_size("bp")
    groups = lax.axis_size("bx") * pair
    slot_count = kv_cache.shape[1]
    block_len = kv_cache.shape[2]
    per_dev = old_table.shape[1] // groups
    request = lax.axis_index("bx")
    member = lax.axis_index("bp")
    my_index = request * pair + member
    late_block = 2 * pair - 1 - member
    targets = jnp.arange(groups, dtype=jnp.int32)
    kv_ids = jnp.arange(2, dtype=jnp.int32)
    kv_flat = kv_cache.reshape(2 * slot_count, block_len, local_width)

    first_dev = old_table[:, 0] // slot_count
    target_req = targets // pair
    c_index = jnp.arange(per_dev, dtype=jnp.int32)
    block_index = ((my_index - first_dev[target_req]) % groups)[:, None] + groups * c_index[None, :]
    slot_index = (
        old_table[target_req[:, None], jnp.clip(block_index, 0, old_table.shape[1] - 1)]
        - my_index * slot_count
    )
    slot_index = jnp.clip(slot_index, 0, slot_count - 1)
    out_ids = kv_ids[None, :, None] * slot_count + slot_index[:, None, :]
    outgoing = jnp.take(kv_flat, out_ids.reshape(-1), axis=0, mode="clip").reshape(
        groups, 2, per_dev, block_len, local_width
    )
    received = lax.all_to_all(
        outgoing, ("bx", "bp"), split_axis=0, concat_axis=0, tiled=True
    )

    projected = jnp.einsum(
        "tc,jcw->tjw",
        lax.all_gather(states, "head", axis=1, tiled=True),
        qkv_weight,
        preferred_element_type=jnp.float32,
    )
    queries = projected[:, 0]
    key_new = projected[:, 1]
    value_new = projected[:, 2]
    query_sq, key_sq = lax.psum(
        (jnp.sum(queries * queries, axis=1), jnp.sum(key_new * key_new, axis=1)), "head"
    )
    gains = norm_gains.astype(jnp.float32)
    queries = queries * lax.rsqrt(query_sq / D + norm_eps)[:, None] * gains[0]
    key_new = key_new * lax.rsqrt(key_sq / D + norm_eps)[:, None] * gains[1]
    half_ids = jnp.arange(half_rows, dtype=jnp.int32)
    token_offset = jnp.concatenate(
        [member * half_rows + half_ids, late_block * half_rows + half_ids]
    )
    positions = cached_len[request] + token_offset
    queries = (
        rotate(queries.reshape(tok_rows, local_heads, HS), positions, HS)
        .reshape(tok_rows, local_width)
        .astype(jnp.bfloat16)
    )
    key_new = (
        rotate(key_new.reshape(tok_rows, local_heads, HS), positions, HS)
        .reshape(tok_rows, local_width)
        .astype(jnp.bfloat16)
    )
    value_new = value_new.astype(jnp.bfloat16)
    fresh_kv = jnp.stack([key_new, value_new])
    meta = jnp.stack([member, cached_len[request], first_dev[request], 0]).astype(jnp.int32)

    partner_new = lax.ppermute(fresh_kv, "bp", [(0, 1), (1, 0)])
    state = new_attention(meta, queries, fresh_kv[0], fresh_kv[1])

    blocks_dev = tok_rows // block_len
    chunk_blocks = blocks_dev // 2
    new_home = new_table[:, 0] // slot_count
    pair_index = jnp.arange(2, dtype=jnp.int32)
    reqs = jnp.arange(groups // pair, dtype=jnp.int32)
    dest = reqs * pair + member
    wanted_out = 2 * ((dest - new_home[request]) % groups)[:, None] + pair_index[None, :]
    chunk = wanted_out // chunk_blocks
    within = wanted_out % chunk_blocks
    own_place = jnp.where(chunk == member, 0, 1) * chunk_blocks + within
    partner_place = jnp.where(chunk == 1 - member, 0, 1) * chunk_blocks + within
    is_own = (chunk == member) | (chunk == 3 - member)

    def pick(source, place):
        ids = kv_ids[None, :, None] * blocks_dev + place[:, None, :]
        return jnp.take(
            source.reshape(2 * blocks_dev, block_len, local_width), ids.reshape(-1), axis=0,
            mode="clip",
        ).reshape(groups // pair, 2, 2, block_len, local_width)

    picked = jnp.where(
        is_own[:, None, :, None, None], pick(fresh_kv, own_place), pick(partner_new, partner_place)
    )
    arrived = lax.all_to_all(picked, "bx", split_axis=0, concat_axis=0, tiled=True)
    wanted_in = 2 * ((my_index - new_home) % groups)[:, None] + pair_index[None, :]
    target_slot = (
        new_table[reqs[:, None], jnp.clip(wanted_in, 0, new_table.shape[1] - 1)]
        - my_index * slot_count
    )
    target_ids = kv_ids[None, :, None] * slot_count + target_slot[:, None, :]
    updated_cache = (
        kv_flat.at[target_ids.reshape(-1)]
        .set(arrived.reshape(-1, block_len, local_width), mode="drop")
        .reshape(kv_cache.shape)
    )

    state = partner_attention(meta, queries, partner_new, state)
    attended = cached_attention(meta, queries, received, *state)
    return (attended, updated_cache)


def solution(mesh):
    heads, groups = mesh.devices.shape
    split = jax.sharding.Mesh(mesh.devices.reshape(heads, groups // 2, 2), ("head", "bx", "bp"))
    blk = ("bx", "bp")
    return jax.shard_map(
        body,
        mesh=split,
        in_specs=(
            P(blk, "head"),
            P(None, None, "head"),
            P(None, "head"),
            P(None, blk, None, "head"),
            P(),
            P(),
            P(),
        ),
        out_specs=(P(blk, "head"), P(None, blk, None, "head")),
        check_vma=False,
    )
```

```python
import functools

import jax
import jax.numpy as jnp
from jax import lax
from jax.experimental import pallas as pl
from jax.experimental.pallas import tpu as pltpu
from jax.sharding import PartitionSpec as P


D = 4096
HS = 128


rope_base = 500000.0
norm_eps = 1e-06
score_scale = HS ** (-0.5)
scale2 = score_scale * 1.4426950408889634


def rotate(values, positions, head_size):
    half_size = head_size // 2
    frequency = rope_base ** (-jnp.arange(half_size, dtype=jnp.float32) * 2.0 / head_size)
    angles = positions.astype(jnp.float32)[:, None] * frequency[None, :]
    cosine = jnp.cos(angles)[:, None, :]
    sine_part = jnp.sin(angles)[:, None, :]
    first_half = values[..., :half_size]
    second = values[..., half_size:]
    return jnp.concatenate(
        [first_half * cosine - second * sine_part, second * cosine + first_half * sine_part],
        axis=-1,
    )


def online_update(s, v, m_sc, l_sc, acc_sc):
    m_prev = m_sc[...]
    m_cur = jnp.max(s, axis=1, keepdims=True) * scale2
    m_next = jnp.maximum(m_prev, m_cur)
    alpha = jnp.exp2(m_prev - m_next)
    p = jnp.exp2(s * scale2 - m_next[:, :1])
    l_sc[...] = alpha * l_sc[...] + jnp.sum(p, axis=1, keepdims=True)
    pv = jnp.dot(p.astype(jnp.bfloat16), v, preferred_element_type=jnp.float32)
    acc_sc[...] = acc_sc[...] * alpha + pv
    m_sc[...] = m_next


def scores_of(q, k):
    return lax.dot_general(q, k, (((1,), (1,)), ((), ())), preferred_element_type=jnp.float32)


def new_kernel(meta_ref, q_ref, k_ref, v_ref, *rest, partner):
    if partner:
        acc_in, m_in, l_in, acc_out, m_out, l_out, m_sc, l_sc, acc_sc = rest
    else:
        acc_out, m_out, l_out, m_sc, l_sc, acc_sc = rest
    qi = pl.program_id(1)
    kj = pl.program_id(2)
    member = meta_ref[0]
    q_chunk = jnp.where(qi == 0, member, 3 - member)
    if partner:
        k_chunk = jnp.where(kj == 0, 1 - member, 2 + member)
    else:
        k_chunk = jnp.where(kj == 0, member, 3 - member)

    @pl.when(kj == 0)
    def _():
        if partner:
            m_sc[...] = m_in[...]
            l_sc[...] = l_in[...]
            acc_sc[...] = acc_in[...]
        else:
            m_sc[...] = jnp.full(m_sc.shape, -jnp.inf, jnp.float32)
            l_sc[...] = jnp.zeros(l_sc.shape, jnp.float32)
            acc_sc[...] = jnp.zeros(acc_sc.shape, jnp.float32)

    @pl.when(k_chunk <= q_chunk)
    def _():
        s = scores_of(q_ref[...], k_ref[...])
        rows = lax.broadcasted_iota(jnp.int32, s.shape, 0)
        cols = lax.broadcasted_iota(jnp.int32, s.shape, 1)
        s = jnp.where((k_chunk < q_chunk) | (cols <= rows), s, -jnp.inf)
        online_update(s, v_ref[...], m_sc, l_sc, acc_sc)

    @pl.when(kj == pl.num_programs(2) - 1)
    def _():
        acc_out[...] = acc_sc[...]
        m_out[...] = m_sc[...]
        l_out[...] = l_sc[...]


def partner_kernel(meta_ref, q_ref, k_ref, v_ref, acc_in, m_in, l_in, acc_out, m_out, l_out):
    k_ref = k_ref.at[0]
    v_ref = v_ref.at[0]
    member = meta_ref[0]
    rows = q_ref.shape[0]
    half = rows // 2
    acc_out[...] = acc_in[...]
    m_out[...] = m_in[...]
    l_out[...] = l_in[...]

    @pl.when(member == 0)
    def _():
        s = scores_of(q_ref[pl.ds(half, half), :], k_ref[...])
        online_update(
            s, v_ref[...], m_out.at[pl.ds(half, half)], l_out.at[pl.ds(half, half)],
            acc_out.at[pl.ds(half, half)],
        )

    @pl.when(member != 0)
    def _():
        s = scores_of(q_ref[...], k_ref[pl.ds(0, half), :])
        online_update(s, v_ref[pl.ds(0, half), :], m_out, l_out, acc_out)


def partner_attention(meta, queries, partner_new, state):
    tok_rows, width = queries.shape
    heads = width // HS
    shape = jax.ShapeDtypeStruct((tok_rows, width), jnp.float32)
    spec = pl.BlockSpec((tok_rows, HS), lambda h, meta: (0, h))
    key_spec = pl.BlockSpec((1, tok_rows, HS), lambda h, meta: (0, 0, h))
    value_spec = pl.BlockSpec((1, tok_rows, HS), lambda h, meta: (1, 0, h))
    return pl.pallas_call(
        partner_kernel,
        out_shape=(shape, shape, shape),
        grid_spec=pltpu.PrefetchScalarGridSpec(
            num_scalar_prefetch=1,
            grid=(heads,),
            in_specs=[spec, key_spec, value_spec, spec, spec, spec],
            out_specs=[spec] * 3,
        ),
        compiler_params=pltpu.CompilerParams(dimension_semantics=("arbitrary",)),
        cost_estimate=pl.CostEstimate(
            flops=2 * 2 * tok_rows * tok_rows * width // 2,
            transcendentals=tok_rows * tok_rows * heads // 2,
            bytes_accessed=3 * 2 * tok_rows * width + 6 * 4 * tok_rows * width,
        ),
    )(meta, queries, partner_new, partner_new, *state)


def cached_kernel(meta_ref, q_ref, k_ref, v_ref, acc_in, m_in, l_in, o_ref, m_sc, l_sc, acc_sc,
                  *, groups, block_len, side):
    c = pl.program_id(1)
    length = meta_ref[1]
    first = meta_ref[2]
    tile = groups * block_len

    @pl.when(c == 0)
    def _():
        m_sc[...] = m_in[...]
        l_sc[...] = l_in[...]
        acc_sc[...] = acc_in[...]

    @pl.when((c + 1) * groups * block_len <= length)
    def _():
        k = k_ref[...].reshape(tile, HS)
        v = v_ref[...].reshape(tile, HS)
        s = scores_of(q_ref[...], k)
        online_update(s, v, m_sc, l_sc, acc_sc)

    @pl.when((c * groups * block_len < length) & ((c + 1) * groups * block_len > length))
    def _():
        k = k_ref[...].reshape(tile, HS)
        v = v_ref[...].reshape(tile, HS)
        s = scores_of(q_ref[...], k)
        cols = lax.broadcasted_iota(jnp.int32, (1, tile), 1)
        shift = cols // block_len
        me = meta_ref[3]
        src = ((me // side - shift // side + side) % side) * side + (
            me % side - shift % side + side
        ) % side
        block = (src - first + groups) % groups + groups * c
        visible = block * block_len + cols % block_len < length
        s = jnp.where(visible, s, -jnp.inf)
        online_update(s, v, m_sc, l_sc, acc_sc)

    @pl.when(c == pl.num_programs(1) - 1)
    def _():
        o_ref[...] = (acc_sc[...] / l_sc[...]).astype(o_ref.dtype)


def new_attention(meta, queries, keys, values, state=None):
    tok_rows, width = queries.shape
    heads = width // HS
    q_rows = tok_rows // 2
    key_rows = keys.shape[0]
    k_tiles = key_rows // q_rows
    partner = state is not None
    shape = jax.ShapeDtypeStruct((tok_rows, width), jnp.float32)
    state_spec = pl.BlockSpec((q_rows, HS), lambda h, i, j, meta: (i, h))
    in_specs = [
        pl.BlockSpec((q_rows, HS), lambda h, i, j, meta: (i, h)),
        pl.BlockSpec((q_rows, HS), lambda h, i, j, meta: (j, h)),
        pl.BlockSpec((q_rows, HS), lambda h, i, j, meta: (j, h)),
    ]
    operands = [meta, queries, keys, values]
    if partner:
        in_specs += [state_spec] * 3
        operands += list(state)
    return pl.pallas_call(
        functools.partial(new_kernel, partner=partner),
        out_shape=(shape, shape, shape),
        grid_spec=pltpu.PrefetchScalarGridSpec(
            num_scalar_prefetch=1,
            grid=(heads, 2, k_tiles),
            in_specs=in_specs,
            out_specs=[state_spec, state_spec, state_spec],
            scratch_shapes=[
                pltpu.VMEM((q_rows, HS), jnp.float32),
                pltpu.VMEM((q_rows, HS), jnp.float32),
                pltpu.VMEM((q_rows, HS), jnp.float32),
            ],
        ),
        compiler_params=pltpu.CompilerParams(
            dimension_semantics=("arbitrary", "arbitrary", "arbitrary")
        ),
        cost_estimate=pl.CostEstimate(
            flops=2 * 2 * tok_rows * key_rows * width * 3 // 4,
            transcendentals=tok_rows * key_rows * heads * 3 // 4,
            bytes_accessed=2 * tok_rows * width + 2 * 2 * key_rows * width + 6 * 4 * tok_rows * width,
        ),
    )(*operands)


def cached_attention(meta, queries, received, acc, m, l, side):
    tok_rows, width = queries.shape
    heads = width // HS
    groups, _, per_dev, block_len, _ = received.shape

    def kv_map(index):
        def index_map(h, c, meta):
            last = (meta[1] + groups * block_len - 1) // (groups * block_len) - 1
            return (0, index, jnp.minimum(c, last), 0, h)

        return index_map

    kv_block = (groups, None, None, block_len, HS)
    state_spec = pl.BlockSpec((tok_rows, HS), lambda h, c, meta: (0, h))
    keys_total = groups * per_dev * block_len
    return pl.pallas_call(
        functools.partial(
            cached_kernel, groups=groups, block_len=block_len, side=side
        ),
        out_shape=jax.ShapeDtypeStruct((tok_rows, width), jnp.bfloat16),
        grid_spec=pltpu.PrefetchScalarGridSpec(
            num_scalar_prefetch=1,
            grid=(heads, per_dev),
            in_specs=[
                pl.BlockSpec((tok_rows, HS), lambda h, c, meta: (0, h)),
                pl.BlockSpec(kv_block, kv_map(0)),
                pl.BlockSpec(kv_block, kv_map(1)),
                state_spec,
                state_spec,
                state_spec,
            ],
            out_specs=pl.BlockSpec((tok_rows, HS), lambda h, c, meta: (0, h)),
            scratch_shapes=[
                pltpu.VMEM((tok_rows, HS), jnp.float32),
                pltpu.VMEM((tok_rows, HS), jnp.float32),
                pltpu.VMEM((tok_rows, HS), jnp.float32),
            ],
        ),
        compiler_params=pltpu.CompilerParams(dimension_semantics=("arbitrary", "arbitrary")),
        cost_estimate=pl.CostEstimate(
            flops=2 * 2 * tok_rows * keys_total * width // 2,
            transcendentals=tok_rows * keys_total * heads // 2,
            bytes_accessed=2 * keys_total * width + 2 * tok_rows * width * 2 + 3 * 4 * tok_rows * width,
        ),
    )(meta, queries, received, received, acc, m, l)


def body(states, qkv_weight, norm_gains, kv_cache, cached_len, old_table, new_table):
    tok_rows = states.shape[0]
    half_rows = tok_rows // 2
    local_width = qkv_weight.shape[2]
    local_heads = local_width // HS
    pair = lax.axis_size("bp")
    groups = lax.axis_size("bx") * pair
    slot_count = kv_cache.shape[1]
    block_len = kv_cache.shape[2]
    per_dev = old_table.shape[1] // groups
    request = lax.axis_index("bx")
    member = lax.axis_index("bp")
    my_index = request * pair + member
    late_block = 2 * pair - 1 - member
    targets = jnp.arange(groups, dtype=jnp.int32)
    kv_ids = jnp.arange(2, dtype=jnp.int32)
    kv_flat = kv_cache.reshape(2 * slot_count, block_len, local_width)

    first_dev = old_table[:, 0] // slot_count
    side = 4
    shift_x = targets // side
    shift_z = targets % side
    dest_of = lambda src: ((src // side + shift_x) % side) * side + (src + shift_z) % side
    targets = dest_of(my_index)
    target_req = targets // pair
    c_index = jnp.arange(per_dev, dtype=jnp.int32)
    block_index = ((my_index - first_dev[target_req]) % groups)[:, None] + groups * c_index[None, :]
    slot_index = (
        old_table[target_req[:, None], jnp.clip(block_index, 0, old_table.shape[1] - 1)]
        - my_index * slot_count
    )
    slot_index = jnp.clip(slot_index, 0, slot_count - 1)
    out_ids = kv_ids[None, :, None] * slot_count + slot_index[:, None, :]
    outgoing = jnp.take(kv_flat, out_ids.reshape(-1), axis=0, mode="clip").reshape(
        groups, 2, per_dev, block_len, local_width
    )
    pieces = [outgoing[0]]
    for k in range(1, groups):
        route = [
            (src, ((src // side + k // side) % side) * side + (src + k % side) % side)
            for src in range(groups)
        ]
        pieces.append(lax.ppermute(outgoing[k], ("bx", "bp"), route))
    received = jnp.stack(pieces)

    projected = jnp.einsum(
        "tc,jcw->tjw",
        lax.all_gather(states, "head", axis=1, tiled=True),
        qkv_weight,
        preferred_element_type=jnp.float32,
    )
    queries = projected[:, 0]
    key_new = projected[:, 1]
    value_new = projected[:, 2]
    query_sq, key_sq = lax.psum(
        (jnp.sum(queries * queries, axis=1), jnp.sum(key_new * key_new, axis=1)), "head"
    )
    gains = norm_gains.astype(jnp.float32)
    queries = queries * lax.rsqrt(query_sq / D + norm_eps)[:, None] * gains[0]
    key_new = key_new * lax.rsqrt(key_sq / D + norm_eps)[:, None] * gains[1]
    half_ids = jnp.arange(half_rows, dtype=jnp.int32)
    token_offset = jnp.concatenate(
        [member * half_rows + half_ids, late_block * half_rows + half_ids]
    )
    positions = cached_len[request] + token_offset
    queries = (
        rotate(queries.reshape(tok_rows, local_heads, HS), positions, HS)
        .reshape(tok_rows, local_width)
        .astype(jnp.bfloat16)
    )
    key_new = (
        rotate(key_new.reshape(tok_rows, local_heads, HS), positions, HS)
        .reshape(tok_rows, local_width)
        .astype(jnp.bfloat16)
    )
    value_new = value_new.astype(jnp.bfloat16)
    fresh_kv = jnp.stack([key_new, value_new])
    meta = jnp.stack([member, cached_len[request], first_dev[request], my_index]).astype(jnp.int32)

    partner_new = lax.ppermute(fresh_kv, "bp", [(0, 1), (1, 0)])
    state = new_attention(meta, queries, fresh_kv[0], fresh_kv[1])

    blocks_dev = tok_rows // block_len
    chunk_blocks = blocks_dev // 2
    new_home = new_table[:, 0] // slot_count
    pair_index = jnp.arange(2, dtype=jnp.int32)
    reqs = jnp.arange(groups // pair, dtype=jnp.int32)
    dest = reqs * pair + member
    wanted_out = 2 * ((dest - new_home[request]) % groups)[:, None] + pair_index[None, :]
    chunk = wanted_out // chunk_blocks
    within = wanted_out % chunk_blocks
    own_place = jnp.where(chunk == member, 0, 1) * chunk_blocks + within
    partner_place = jnp.where(chunk == 1 - member, 0, 1) * chunk_blocks + within
    is_own = (chunk == member) | (chunk == 3 - member)

    def pick(source, place):
        ids = kv_ids[None, :, None] * blocks_dev + place[:, None, :]
        return jnp.take(
            source.reshape(2 * blocks_dev, block_len, local_width), ids.reshape(-1), axis=0,
            mode="clip",
        ).reshape(groups // pair, 2, 2, block_len, local_width)

    picked = jnp.where(
        is_own[:, None, :, None, None], pick(fresh_kv, own_place), pick(partner_new, partner_place)
    )
    arrived = lax.all_to_all(picked, "bx", split_axis=0, concat_axis=0, tiled=True)
    wanted_in = 2 * ((my_index - new_home) % groups)[:, None] + pair_index[None, :]
    target_slot = (
        new_table[reqs[:, None], jnp.clip(wanted_in, 0, new_table.shape[1] - 1)]
        - my_index * slot_count
    )
    target_ids = kv_ids[None, :, None] * slot_count + target_slot[:, None, :]
    updated_cache = (
        kv_flat.at[target_ids.reshape(-1)]
        .set(arrived.reshape(-1, block_len, local_width), mode="drop")
        .reshape(kv_cache.shape)
    )

    state = partner_attention(meta, queries, partner_new, state)
    attended = cached_attention(meta, queries, received, *state, side)
    return (attended, updated_cache)


def solution(mesh):
    heads, groups = mesh.devices.shape
    split = jax.sharding.Mesh(mesh.devices.reshape(heads, groups // 2, 2), ("head", "bx", "bp"))
    blk = ("bx", "bp")
    return jax.shard_map(
        body,
        mesh=split,
        in_specs=(
            P(blk, "head"),
            P(None, None, "head"),
            P(None, "head"),
            P(None, blk, None, "head"),
            P(),
            P(),
            P(),
        ),
        out_specs=(P(blk, "head"), P(None, blk, None, "head")),
        check_vma=False,
    )
```

```python
import functools

import jax
import jax.numpy as jnp
from jax import lax
from jax.experimental import pallas as pl
from jax.experimental.pallas import tpu as pltpu
from jax.sharding import PartitionSpec as P


D = 4096
HS = 128


rope_base = 500000.0
norm_eps = 1e-06
score_scale = HS ** (-0.5)
scale2 = score_scale * 1.4426950408889634


def rotate(values, positions, head_size):
    half_size = head_size // 2
    frequency = rope_base ** (-jnp.arange(half_size, dtype=jnp.float32) * 2.0 / head_size)
    angles = positions.astype(jnp.float32)[:, None] * frequency[None, :]
    cosine = jnp.cos(angles)[:, None, :]
    sine_part = jnp.sin(angles)[:, None, :]
    first_half = values[..., :half_size]
    second = values[..., half_size:]
    return jnp.concatenate(
        [first_half * cosine - second * sine_part, second * cosine + first_half * sine_part],
        axis=-1,
    )


def online_update(s, v, m_sc, l_sc, acc_sc):
    m_prev = m_sc[...]
    m_cur = jnp.max(s, axis=1, keepdims=True) * scale2
    m_next = jnp.maximum(m_prev, m_cur)
    alpha = jnp.exp2(m_prev - m_next)
    p = jnp.exp2(s * scale2 - m_next[:, :1])
    l_sc[...] = alpha * l_sc[...] + jnp.sum(p, axis=1, keepdims=True)
    pv = jnp.dot(p.astype(jnp.bfloat16), v, preferred_element_type=jnp.float32)
    acc_sc[...] = acc_sc[...] * alpha + pv
    m_sc[...] = m_next


def scores_of(q, k):
    return lax.dot_general(q, k, (((1,), (1,)), ((), ())), preferred_element_type=jnp.float32)


def new_kernel(meta_ref, q_ref, k_ref, v_ref, *rest, partner):
    if partner:
        acc_in, m_in, l_in, acc_out, m_out, l_out, m_sc, l_sc, acc_sc = rest
    else:
        acc_out, m_out, l_out, m_sc, l_sc, acc_sc = rest
    qi = pl.program_id(1)
    kj = pl.program_id(2)
    member = meta_ref[0]
    q_chunk = jnp.where(qi == 0, member, 3 - member)
    if partner:
        k_chunk = jnp.where(kj == 0, 1 - member, 2 + member)
    else:
        k_chunk = jnp.where(kj == 0, member, 3 - member)

    @pl.when(kj == 0)
    def _():
        if partner:
            m_sc[...] = m_in[...]
            l_sc[...] = l_in[...]
            acc_sc[...] = acc_in[...]
        else:
            m_sc[...] = jnp.full(m_sc.shape, -jnp.inf, jnp.float32)
            l_sc[...] = jnp.zeros(l_sc.shape, jnp.float32)
            acc_sc[...] = jnp.zeros(acc_sc.shape, jnp.float32)

    @pl.when(k_chunk <= q_chunk)
    def _():
        s = scores_of(q_ref[...], k_ref[...])
        rows = lax.broadcasted_iota(jnp.int32, s.shape, 0)
        cols = lax.broadcasted_iota(jnp.int32, s.shape, 1)
        s = jnp.where((k_chunk < q_chunk) | (cols <= rows), s, -jnp.inf)
        online_update(s, v_ref[...], m_sc, l_sc, acc_sc)

    @pl.when(kj == pl.num_programs(2) - 1)
    def _():
        acc_out[...] = acc_sc[...]
        m_out[...] = m_sc[...]
        l_out[...] = l_sc[...]


def partner_kernel(meta_ref, q_ref, k_ref, v_ref, acc_in, m_in, l_in, acc_out, m_out, l_out):
    k_ref = k_ref.at[0]
    v_ref = v_ref.at[0]
    member = meta_ref[0]
    rows = q_ref.shape[0]
    half = rows // 2
    acc_out[...] = acc_in[...]
    m_out[...] = m_in[...]
    l_out[...] = l_in[...]

    @pl.when(member == 0)
    def _():
        s = scores_of(q_ref[pl.ds(half, half), :], k_ref[...])
        online_update(
            s, v_ref[...], m_out.at[pl.ds(half, half)], l_out.at[pl.ds(half, half)],
            acc_out.at[pl.ds(half, half)],
        )

    @pl.when(member != 0)
    def _():
        s = scores_of(q_ref[...], k_ref[pl.ds(0, half), :])
        online_update(s, v_ref[pl.ds(0, half), :], m_out, l_out, acc_out)


def partner_attention(meta, queries, partner_new, state):
    tok_rows, width = queries.shape
    heads = width // HS
    shape = jax.ShapeDtypeStruct((tok_rows, width), jnp.float32)
    spec = pl.BlockSpec((tok_rows, HS), lambda h, meta: (0, h))
    key_spec = pl.BlockSpec((1, tok_rows, HS), lambda h, meta: (0, 0, h))
    value_spec = pl.BlockSpec((1, tok_rows, HS), lambda h, meta: (1, 0, h))
    return pl.pallas_call(
        partner_kernel,
        out_shape=(shape, shape, shape),
        grid_spec=pltpu.PrefetchScalarGridSpec(
            num_scalar_prefetch=1,
            grid=(heads,),
            in_specs=[spec, key_spec, value_spec, spec, spec, spec],
            out_specs=[spec] * 3,
        ),
        compiler_params=pltpu.CompilerParams(dimension_semantics=("arbitrary",)),
        cost_estimate=pl.CostEstimate(
            flops=2 * 2 * tok_rows * tok_rows * width // 2,
            transcendentals=tok_rows * tok_rows * heads // 2,
            bytes_accessed=3 * 2 * tok_rows * width + 6 * 4 * tok_rows * width,
        ),
    )(meta, queries, partner_new, partner_new, *state)


def cached_kernel(meta_ref, q_ref, k_ref, v_ref, acc_in, m_in, l_in, o_ref, m_sc, l_sc, acc_sc,
                  *, groups, block_len):
    c = pl.program_id(1)
    length = meta_ref[1]
    first = meta_ref[2]
    tile = groups * block_len

    @pl.when(c == 0)
    def _():
        m_sc[...] = m_in[...]
        l_sc[...] = l_in[...]
        acc_sc[...] = acc_in[...]

    @pl.when((c + 1) * groups * block_len <= length)
    def _():
        k = k_ref[...].reshape(tile, HS)
        v = v_ref[...].reshape(tile, HS)
        s = scores_of(q_ref[...], k)
        online_update(s, v, m_sc, l_sc, acc_sc)

    @pl.when((c * groups * block_len < length) & ((c + 1) * groups * block_len > length))
    def _():
        k = k_ref[...].reshape(tile, HS)
        v = v_ref[...].reshape(tile, HS)
        s = scores_of(q_ref[...], k)
        cols = lax.broadcasted_iota(jnp.int32, (1, tile), 1)
        src = cols // block_len
        block = (src - first + groups) % groups + groups * c
        visible = block * block_len + cols % block_len < length
        s = jnp.where(visible, s, -jnp.inf)
        online_update(s, v, m_sc, l_sc, acc_sc)

    @pl.when(c == pl.num_programs(1) - 1)
    def _():
        o_ref[...] = (acc_sc[...] / l_sc[...]).astype(o_ref.dtype)


def new_attention(meta, queries, keys, values, state=None):
    tok_rows, width = queries.shape
    heads = width // HS
    q_rows = tok_rows // 2
    key_rows = keys.shape[0]
    k_tiles = key_rows // q_rows
    partner = state is not None
    shape = jax.ShapeDtypeStruct((tok_rows, width), jnp.float32)
    state_spec = pl.BlockSpec((q_rows, HS), lambda h, i, j, meta: (i, h))
    in_specs = [
        pl.BlockSpec((q_rows, HS), lambda h, i, j, meta: (i, h)),
        pl.BlockSpec((q_rows, HS), lambda h, i, j, meta: (j, h)),
        pl.BlockSpec((q_rows, HS), lambda h, i, j, meta: (j, h)),
    ]
    operands = [meta, queries, keys, values]
    if partner:
        in_specs += [state_spec] * 3
        operands += list(state)
    return pl.pallas_call(
        functools.partial(new_kernel, partner=partner),
        out_shape=(shape, shape, shape),
        grid_spec=pltpu.PrefetchScalarGridSpec(
            num_scalar_prefetch=1,
            grid=(heads, 2, k_tiles),
            in_specs=in_specs,
            out_specs=[state_spec, state_spec, state_spec],
            scratch_shapes=[
                pltpu.VMEM((q_rows, HS), jnp.float32),
                pltpu.VMEM((q_rows, HS), jnp.float32),
                pltpu.VMEM((q_rows, HS), jnp.float32),
            ],
        ),
        compiler_params=pltpu.CompilerParams(
            dimension_semantics=("arbitrary", "arbitrary", "arbitrary")
        ),
        cost_estimate=pl.CostEstimate(
            flops=2 * 2 * tok_rows * key_rows * width * 3 // 4,
            transcendentals=tok_rows * key_rows * heads * 3 // 4,
            bytes_accessed=2 * tok_rows * width + 2 * 2 * key_rows * width + 6 * 4 * tok_rows * width,
        ),
    )(*operands)


def cached_attention(meta, queries, received, acc, m, l):
    tok_rows, width = queries.shape
    heads = width // HS
    groups, _, per_dev, block_len, _ = received.shape

    def kv_map(index):
        def index_map(h, c, meta):
            last = (meta[1] + groups * block_len - 1) // (groups * block_len) - 1
            return (0, index, jnp.minimum(c, last), 0, h)

        return index_map

    kv_block = (groups, None, None, block_len, HS)
    state_spec = pl.BlockSpec((tok_rows, HS), lambda h, c, meta: (0, h))
    keys_total = groups * per_dev * block_len
    return pl.pallas_call(
        functools.partial(
            cached_kernel, groups=groups, block_len=block_len
        ),
        out_shape=jax.ShapeDtypeStruct((tok_rows, width), jnp.bfloat16),
        grid_spec=pltpu.PrefetchScalarGridSpec(
            num_scalar_prefetch=1,
            grid=(heads, per_dev),
            in_specs=[
                pl.BlockSpec((tok_rows, HS), lambda h, c, meta: (0, h)),
                pl.BlockSpec(kv_block, kv_map(0)),
                pl.BlockSpec(kv_block, kv_map(1)),
                state_spec,
                state_spec,
                state_spec,
            ],
            out_specs=pl.BlockSpec((tok_rows, HS), lambda h, c, meta: (0, h)),
            scratch_shapes=[
                pltpu.VMEM((tok_rows, HS), jnp.float32),
                pltpu.VMEM((tok_rows, HS), jnp.float32),
                pltpu.VMEM((tok_rows, HS), jnp.float32),
            ],
        ),
        compiler_params=pltpu.CompilerParams(dimension_semantics=("arbitrary", "arbitrary")),
        cost_estimate=pl.CostEstimate(
            flops=2 * 2 * tok_rows * keys_total * width // 2,
            transcendentals=tok_rows * keys_total * heads // 2,
            bytes_accessed=2 * keys_total * width + 2 * tok_rows * width * 2 + 3 * 4 * tok_rows * width,
        ),
    )(meta, queries, received, received, acc, m, l)


def copy_kernel(src_ref, dst_ref):
    dst_ref[...] = src_ref[...]


def cache_copy(cache):
    kinds, slots, rows, width = cache.shape
    step = 8
    spec = pl.BlockSpec((1, step, rows, width), lambda k, i: (k, i, 0, 0))
    return pl.pallas_call(
        copy_kernel,
        out_shape=jax.ShapeDtypeStruct(cache.shape, cache.dtype),
        grid=(kinds, slots // step),
        in_specs=[spec],
        out_specs=spec,
        cost_estimate=pl.CostEstimate(flops=0, transcendentals=0, bytes_accessed=2 * cache.size * 2),
    )(cache)


def body(states, qkv_weight, norm_gains, kv_cache, cached_len, old_table, new_table):
    tok_rows = states.shape[0]
    half_rows = tok_rows // 2
    local_width = qkv_weight.shape[2]
    local_heads = local_width // HS
    pair = lax.axis_size("bp")
    groups = lax.axis_size("bx") * pair
    slot_count = kv_cache.shape[1]
    block_len = kv_cache.shape[2]
    per_dev = old_table.shape[1] // groups
    request = lax.axis_index("bx")
    member = lax.axis_index("bp")
    my_index = request * pair + member
    late_block = 2 * pair - 1 - member
    targets = jnp.arange(groups, dtype=jnp.int32)
    kv_ids = jnp.arange(2, dtype=jnp.int32)
    kv_flat = kv_cache.reshape(2 * slot_count, block_len, local_width)

    first_dev = old_table[:, 0] // slot_count
    target_req = targets // pair
    c_index = jnp.arange(per_dev, dtype=jnp.int32)
    block_index = ((my_index - first_dev[target_req]) % groups)[:, None] + groups * c_index[None, :]
    slot_index = (
        old_table[target_req[:, None], jnp.clip(block_index, 0, old_table.shape[1] - 1)]
        - my_index * slot_count
    )
    slot_index = jnp.clip(slot_index, 0, slot_count - 1)
    out_ids = kv_ids[None, :, None] * slot_count + slot_index[:, None, :]
    outgoing = jnp.take(kv_flat, out_ids.reshape(-1), axis=0, mode="clip").reshape(
        groups, 2, per_dev, block_len, local_width
    )
    received = lax.all_to_all(
        outgoing, ("bx", "bp"), split_axis=0, concat_axis=0, tiled=True
    )

    projected = jnp.einsum(
        "tc,jcw->tjw",
        lax.all_gather(states, "head", axis=1, tiled=True),
        qkv_weight,
        preferred_element_type=jnp.float32,
    )
    queries = projected[:, 0]
    key_new = projected[:, 1]
    value_new = projected[:, 2]
    query_sq, key_sq = lax.psum(
        (jnp.sum(queries * queries, axis=1), jnp.sum(key_new * key_new, axis=1)), "head"
    )
    gains = norm_gains.astype(jnp.float32)
    queries = queries * lax.rsqrt(query_sq / D + norm_eps)[:, None] * gains[0]
    key_new = key_new * lax.rsqrt(key_sq / D + norm_eps)[:, None] * gains[1]
    half_ids = jnp.arange(half_rows, dtype=jnp.int32)
    token_offset = jnp.concatenate(
        [member * half_rows + half_ids, late_block * half_rows + half_ids]
    )
    positions = cached_len[request] + token_offset
    queries = (
        rotate(queries.reshape(tok_rows, local_heads, HS), positions, HS)
        .reshape(tok_rows, local_width)
        .astype(jnp.bfloat16)
    )
    key_new = (
        rotate(key_new.reshape(tok_rows, local_heads, HS), positions, HS)
        .reshape(tok_rows, local_width)
        .astype(jnp.bfloat16)
    )
    value_new = value_new.astype(jnp.bfloat16)
    fresh_kv = jnp.stack([key_new, value_new])
    meta = jnp.stack([member, cached_len[request], first_dev[request], 0]).astype(jnp.int32)

    partner_new = lax.ppermute(fresh_kv, "bp", [(0, 1), (1, 0)])
    state = new_attention(meta, queries, fresh_kv[0], fresh_kv[1])

    blocks_dev = tok_rows // block_len
    chunk_blocks = blocks_dev // 2
    new_home = new_table[:, 0] // slot_count
    pair_index = jnp.arange(2, dtype=jnp.int32)
    reqs = jnp.arange(groups // pair, dtype=jnp.int32)
    dest = reqs * pair + member
    wanted_out = 2 * ((dest - new_home[request]) % groups)[:, None] + pair_index[None, :]
    chunk = wanted_out // chunk_blocks
    within = wanted_out % chunk_blocks
    own_place = jnp.where(chunk == member, 0, 1) * chunk_blocks + within
    partner_place = jnp.where(chunk == 1 - member, 0, 1) * chunk_blocks + within
    is_own = (chunk == member) | (chunk == 3 - member)

    def pick(source, place):
        ids = kv_ids[None, :, None] * blocks_dev + place[:, None, :]
        return jnp.take(
            source.reshape(2 * blocks_dev, block_len, local_width), ids.reshape(-1), axis=0,
            mode="clip",
        ).reshape(groups // pair, 2, 2, block_len, local_width)

    picked = jnp.where(
        is_own[:, None, :, None, None], pick(fresh_kv, own_place), pick(partner_new, partner_place)
    )
    arrived = lax.all_to_all(picked, "bx", split_axis=0, concat_axis=0, tiled=True)
    wanted_in = 2 * ((my_index - new_home) % groups)[:, None] + pair_index[None, :]
    target_slot = (
        new_table[reqs[:, None], jnp.clip(wanted_in, 0, new_table.shape[1] - 1)]
        - my_index * slot_count
    )
    target_ids = kv_ids[None, :, None] * slot_count + target_slot[:, None, :]
    base = cache_copy(kv_cache).reshape(kv_flat.shape)
    updated_cache = (
        base.at[target_ids.reshape(-1)]
        .set(arrived.reshape(-1, block_len, local_width), mode="drop")
        .reshape(kv_cache.shape)
    )

    state = partner_attention(meta, queries, partner_new, state)
    attended = cached_attention(meta, queries, received, *state)
    return (attended, updated_cache)


def solution(mesh):
    heads, groups = mesh.devices.shape
    split = jax.sharding.Mesh(mesh.devices.reshape(heads, groups // 2, 2), ("head", "bx", "bp"))
    blk = ("bx", "bp")
    return jax.shard_map(
        body,
        mesh=split,
        in_specs=(
            P(blk, "head"),
            P(None, None, "head"),
            P(None, "head"),
            P(None, blk, None, "head"),
            P(),
            P(),
            P(),
        ),
        out_specs=(P(blk, "head"), P(None, blk, None, "head")),
        check_vma=False,
    )
```

```python
import functools

import jax
import jax.numpy as jnp
from jax import lax
from jax.experimental import pallas as pl
from jax.experimental.pallas import tpu as pltpu
from jax.sharding import PartitionSpec as P


D = 4096
HS = 128


rope_base = 500000.0
norm_eps = 1e-06
score_scale = HS ** (-0.5)
scale2 = score_scale * 1.4426950408889634


def rotate(values, positions, head_size):
    half_size = head_size // 2
    frequency = rope_base ** (-jnp.arange(half_size, dtype=jnp.float32) * 2.0 / head_size)
    angles = positions.astype(jnp.float32)[:, None] * frequency[None, :]
    cosine = jnp.cos(angles)[:, None, :]
    sine_part = jnp.sin(angles)[:, None, :]
    first_half = values[..., :half_size]
    second = values[..., half_size:]
    return jnp.concatenate(
        [first_half * cosine - second * sine_part, second * cosine + first_half * sine_part],
        axis=-1,
    )


def online_update(s, v, m_sc, l_sc, acc_sc):
    m_prev = m_sc[...]
    m_cur = jnp.max(s, axis=1, keepdims=True) * scale2
    m_next = jnp.maximum(m_prev, m_cur)
    alpha = jnp.exp2(m_prev - m_next)
    p = jnp.exp2(s * scale2 - m_next[:, :1])
    l_sc[...] = alpha * l_sc[...] + jnp.sum(p, axis=1, keepdims=True)
    pv = jnp.dot(p.astype(jnp.bfloat16), v, preferred_element_type=jnp.float32)
    acc_sc[...] = acc_sc[...] * alpha + pv
    m_sc[...] = m_next


def scores_of(q, k):
    return lax.dot_general(q, k, (((1,), (1,)), ((), ())), preferred_element_type=jnp.float32)


def new_kernel(meta_ref, q_ref, k_ref, v_ref, *rest, partner):
    if partner:
        acc_in, m_in, l_in, acc_out, m_out, l_out, m_sc, l_sc, acc_sc = rest
    else:
        acc_out, m_out, l_out, m_sc, l_sc, acc_sc = rest
    qi = pl.program_id(1)
    kj = pl.program_id(2)
    member = meta_ref[0]
    q_chunk = jnp.where(qi == 0, member, 3 - member)
    if partner:
        k_chunk = jnp.where(kj == 0, 1 - member, 2 + member)
    else:
        k_chunk = jnp.where(kj == 0, member, 3 - member)

    @pl.when(kj == 0)
    def _():
        if partner:
            m_sc[...] = m_in[...]
            l_sc[...] = l_in[...]
            acc_sc[...] = acc_in[...]
        else:
            m_sc[...] = jnp.full(m_sc.shape, -jnp.inf, jnp.float32)
            l_sc[...] = jnp.zeros(l_sc.shape, jnp.float32)
            acc_sc[...] = jnp.zeros(acc_sc.shape, jnp.float32)

    @pl.when(k_chunk <= q_chunk)
    def _():
        s = scores_of(q_ref[...], k_ref[...])
        rows = lax.broadcasted_iota(jnp.int32, s.shape, 0)
        cols = lax.broadcasted_iota(jnp.int32, s.shape, 1)
        s = jnp.where((k_chunk < q_chunk) | (cols <= rows), s, -jnp.inf)
        online_update(s, v_ref[...], m_sc, l_sc, acc_sc)

    @pl.when(kj == pl.num_programs(2) - 1)
    def _():
        acc_out[...] = acc_sc[...]
        m_out[...] = m_sc[...]
        l_out[...] = l_sc[...]


def cached_kernel(meta_ref, q_ref, pk_ref, pv_ref, k_ref, v_ref, acc_in, m_in, l_in, o_ref,
                  m_sc, l_sc, acc_sc, *, groups, block_len):
    c = pl.program_id(1)
    length = meta_ref[1]
    first = meta_ref[2]
    tile = groups * block_len
    member = meta_ref[0]
    half = q_ref.shape[0] // 2

    @pl.when(c == 0)
    def _():
        m_sc[...] = m_in[...]
        l_sc[...] = l_in[...]
        acc_sc[...] = acc_in[...]

    @pl.when((c == 0) & (member == 0))
    def _():
        s = scores_of(q_ref[pl.ds(half, half), :], pk_ref[0])
        online_update(
            s, pv_ref[0], m_sc.at[pl.ds(half, half)], l_sc.at[pl.ds(half, half)],
            acc_sc.at[pl.ds(half, half)],
        )

    @pl.when((c == 0) & (member != 0))
    def _():
        s = scores_of(q_ref[...], pk_ref[0, pl.ds(0, half), :])
        online_update(s, pv_ref[0, pl.ds(0, half), :], m_sc, l_sc, acc_sc)

    @pl.when((c + 1) * groups * block_len <= length)
    def _():
        k = k_ref[...].reshape(tile, HS)
        v = v_ref[...].reshape(tile, HS)
        s = scores_of(q_ref[...], k)
        online_update(s, v, m_sc, l_sc, acc_sc)

    @pl.when((c * groups * block_len < length) & ((c + 1) * groups * block_len > length))
    def _():
        k = k_ref[...].reshape(tile, HS)
        v = v_ref[...].reshape(tile, HS)
        s = scores_of(q_ref[...], k)
        cols = lax.broadcasted_iota(jnp.int32, (1, tile), 1)
        src = cols // block_len
        block = (src - first + groups) % groups + groups * c
        visible = block * block_len + cols % block_len < length
        s = jnp.where(visible, s, -jnp.inf)
        online_update(s, v, m_sc, l_sc, acc_sc)

    @pl.when(c == pl.num_programs(1) - 1)
    def _():
        o_ref[...] = (acc_sc[...] / l_sc[...]).astype(o_ref.dtype)


def new_attention(meta, queries, keys, values, state=None):
    tok_rows, width = queries.shape
    heads = width // HS
    q_rows = tok_rows // 2
    key_rows = keys.shape[0]
    k_tiles = key_rows // q_rows
    partner = state is not None
    shape = jax.ShapeDtypeStruct((tok_rows, width), jnp.float32)
    state_spec = pl.BlockSpec((q_rows, HS), lambda h, i, j, meta: (i, h))
    in_specs = [
        pl.BlockSpec((q_rows, HS), lambda h, i, j, meta: (i, h)),
        pl.BlockSpec((q_rows, HS), lambda h, i, j, meta: (j, h)),
        pl.BlockSpec((q_rows, HS), lambda h, i, j, meta: (j, h)),
    ]
    operands = [meta, queries, keys, values]
    if partner:
        in_specs += [state_spec] * 3
        operands += list(state)
    return pl.pallas_call(
        functools.partial(new_kernel, partner=partner),
        out_shape=(shape, shape, shape),
        grid_spec=pltpu.PrefetchScalarGridSpec(
            num_scalar_prefetch=1,
            grid=(heads, 2, k_tiles),
            in_specs=in_specs,
            out_specs=[state_spec, state_spec, state_spec],
            scratch_shapes=[
                pltpu.VMEM((q_rows, HS), jnp.float32),
                pltpu.VMEM((q_rows, HS), jnp.float32),
                pltpu.VMEM((q_rows, HS), jnp.float32),
            ],
        ),
        compiler_params=pltpu.CompilerParams(
            dimension_semantics=("arbitrary", "arbitrary", "arbitrary")
        ),
        cost_estimate=pl.CostEstimate(
            flops=2 * 2 * tok_rows * key_rows * width * 3 // 4,
            transcendentals=tok_rows * key_rows * heads * 3 // 4,
            bytes_accessed=2 * tok_rows * width + 2 * 2 * key_rows * width + 6 * 4 * tok_rows * width,
        ),
    )(*operands)


def cached_attention(meta, queries, partner_new, received, acc, m, l):
    tok_rows, width = queries.shape
    heads = width // HS
    groups, _, per_dev, block_len, _ = received.shape

    def kv_map(index):
        def index_map(h, c, meta):
            last = (meta[1] + groups * block_len - 1) // (groups * block_len) - 1
            return (0, index, jnp.minimum(c, last), 0, h)

        return index_map

    kv_block = (groups, None, None, block_len, HS)
    state_spec = pl.BlockSpec((tok_rows, HS), lambda h, c, meta: (0, h))
    keys_total = groups * per_dev * block_len
    return pl.pallas_call(
        functools.partial(
            cached_kernel, groups=groups, block_len=block_len
        ),
        out_shape=jax.ShapeDtypeStruct((tok_rows, width), jnp.bfloat16),
        grid_spec=pltpu.PrefetchScalarGridSpec(
            num_scalar_prefetch=1,
            grid=(heads, per_dev),
            in_specs=[
                pl.BlockSpec((tok_rows, HS), lambda h, c, meta: (0, h)),
                pl.BlockSpec((1, tok_rows, HS), lambda h, c, meta: (0, 0, h)),
                pl.BlockSpec((1, tok_rows, HS), lambda h, c, meta: (1, 0, h)),
                pl.BlockSpec(kv_block, kv_map(0)),
                pl.BlockSpec(kv_block, kv_map(1)),
                state_spec,
                state_spec,
                state_spec,
            ],
            out_specs=pl.BlockSpec((tok_rows, HS), lambda h, c, meta: (0, h)),
            scratch_shapes=[
                pltpu.VMEM((tok_rows, HS), jnp.float32),
                pltpu.VMEM((tok_rows, HS), jnp.float32),
                pltpu.VMEM((tok_rows, HS), jnp.float32),
            ],
        ),
        compiler_params=pltpu.CompilerParams(dimension_semantics=("arbitrary", "arbitrary")),
        cost_estimate=pl.CostEstimate(
            flops=2 * 2 * tok_rows * keys_total * width // 2,
            transcendentals=tok_rows * keys_total * heads // 2,
            bytes_accessed=2 * keys_total * width + 2 * tok_rows * width * 2 + 3 * 4 * tok_rows * width,
        ),
    )(meta, queries, partner_new, partner_new, received, received, acc, m, l)


def copy_kernel(src_ref, dst_ref):
    dst_ref[...] = src_ref[...]


def cache_copy(cache):
    kinds, slots, rows, width = cache.shape
    step = 8
    spec = pl.BlockSpec((1, step, rows, width), lambda k, i: (k, i, 0, 0))
    return pl.pallas_call(
        copy_kernel,
        out_shape=jax.ShapeDtypeStruct(cache.shape, cache.dtype),
        grid=(kinds, slots // step),
        in_specs=[spec],
        out_specs=spec,
        cost_estimate=pl.CostEstimate(flops=0, transcendentals=0, bytes_accessed=2 * cache.size * 2),
    )(cache)


def body(states, qkv_weight, norm_gains, kv_cache, cached_len, old_table, new_table):
    tok_rows = states.shape[0]
    half_rows = tok_rows // 2
    local_width = qkv_weight.shape[2]
    local_heads = local_width // HS
    pair = lax.axis_size("bp")
    groups = lax.axis_size("bx") * pair
    slot_count = kv_cache.shape[1]
    block_len = kv_cache.shape[2]
    per_dev = old_table.shape[1] // groups
    request = lax.axis_index("bx")
    member = lax.axis_index("bp")
    my_index = request * pair + member
    late_block = 2 * pair - 1 - member
    targets = jnp.arange(groups, dtype=jnp.int32)
    kv_ids = jnp.arange(2, dtype=jnp.int32)
    kv_flat = kv_cache.reshape(2 * slot_count, block_len, local_width)

    first_dev = old_table[:, 0] // slot_count
    target_req = targets // pair
    c_index = jnp.arange(per_dev, dtype=jnp.int32)
    block_index = ((my_index - first_dev[target_req]) % groups)[:, None] + groups * c_index[None, :]
    slot_index = (
        old_table[target_req[:, None], jnp.clip(block_index, 0, old_table.shape[1] - 1)]
        - my_index * slot_count
    )
    slot_index = jnp.clip(slot_index, 0, slot_count - 1)
    out_ids = kv_ids[None, :, None] * slot_count + slot_index[:, None, :]
    outgoing = jnp.take(kv_flat, out_ids.reshape(-1), axis=0, mode="clip").reshape(
        groups, 2, per_dev, block_len, local_width
    )
    received = lax.all_to_all(
        outgoing, ("bx", "bp"), split_axis=0, concat_axis=0, tiled=True
    )

    projected = jnp.einsum(
        "tc,jcw->tjw",
        lax.all_gather(states, "head", axis=1, tiled=True),
        qkv_weight,
        preferred_element_type=jnp.float32,
    )
    queries = projected[:, 0]
    key_new = projected[:, 1]
    value_new = projected[:, 2]
    query_sq, key_sq = lax.psum(
        (jnp.sum(queries * queries, axis=1), jnp.sum(key_new * key_new, axis=1)), "head"
    )
    gains = norm_gains.astype(jnp.float32)
    queries = queries * lax.rsqrt(query_sq / D + norm_eps)[:, None] * gains[0]
    key_new = key_new * lax.rsqrt(key_sq / D + norm_eps)[:, None] * gains[1]
    half_ids = jnp.arange(half_rows, dtype=jnp.int32)
    token_offset = jnp.concatenate(
        [member * half_rows + half_ids, late_block * half_rows + half_ids]
    )
    positions = cached_len[request] + token_offset
    queries = (
        rotate(queries.reshape(tok_rows, local_heads, HS), positions, HS)
        .reshape(tok_rows, local_width)
        .astype(jnp.bfloat16)
    )
    key_new = (
        rotate(key_new.reshape(tok_rows, local_heads, HS), positions, HS)
        .reshape(tok_rows, local_width)
        .astype(jnp.bfloat16)
    )
    value_new = value_new.astype(jnp.bfloat16)
    fresh_kv = jnp.stack([key_new, value_new])
    meta = jnp.stack([member, cached_len[request], first_dev[request], 0]).astype(jnp.int32)

    partner_new = lax.ppermute(fresh_kv, "bp", [(0, 1), (1, 0)])
    state = new_attention(meta, queries, fresh_kv[0], fresh_kv[1])

    blocks_dev = tok_rows // block_len
    chunk_blocks = blocks_dev // 2
    new_home = new_table[:, 0] // slot_count
    pair_index = jnp.arange(2, dtype=jnp.int32)
    reqs = jnp.arange(groups // pair, dtype=jnp.int32)
    dest = reqs * pair + member
    wanted_out = 2 * ((dest - new_home[request]) % groups)[:, None] + pair_index[None, :]
    chunk = wanted_out // chunk_blocks
    within = wanted_out % chunk_blocks
    own_place = jnp.where(chunk == member, 0, 1) * chunk_blocks + within
    partner_place = jnp.where(chunk == 1 - member, 0, 1) * chunk_blocks + within
    is_own = (chunk == member) | (chunk == 3 - member)

    def pick(source, place):
        ids = kv_ids[None, :, None] * blocks_dev + place[:, None, :]
        return jnp.take(
            source.reshape(2 * blocks_dev, block_len, local_width), ids.reshape(-1), axis=0,
            mode="clip",
        ).reshape(groups // pair, 2, 2, block_len, local_width)

    picked = jnp.where(
        is_own[:, None, :, None, None], pick(fresh_kv, own_place), pick(partner_new, partner_place)
    )
    arrived = lax.all_to_all(picked, "bx", split_axis=0, concat_axis=0, tiled=True)
    wanted_in = 2 * ((my_index - new_home) % groups)[:, None] + pair_index[None, :]
    target_slot = (
        new_table[reqs[:, None], jnp.clip(wanted_in, 0, new_table.shape[1] - 1)]
        - my_index * slot_count
    )
    target_ids = kv_ids[None, :, None] * slot_count + target_slot[:, None, :]
    base = cache_copy(kv_cache).reshape(kv_flat.shape)
    updated_cache = (
        base.at[target_ids.reshape(-1)]
        .set(arrived.reshape(-1, block_len, local_width), mode="drop")
        .reshape(kv_cache.shape)
    )

    attended = cached_attention(meta, queries, partner_new, received, *state)
    return (attended, updated_cache)


def solution(mesh):
    heads, groups = mesh.devices.shape
    split = jax.sharding.Mesh(mesh.devices.reshape(heads, groups // 2, 2), ("head", "bx", "bp"))
    blk = ("bx", "bp")
    return jax.shard_map(
        body,
        mesh=split,
        in_specs=(
            P(blk, "head"),
            P(None, None, "head"),
            P(None, "head"),
            P(None, blk, None, "head"),
            P(),
            P(),
            P(),
        ),
        out_specs=(P(blk, "head"), P(None, blk, None, "head")),
        check_vma=False,
    )
```

```python
import functools

import jax
import jax.numpy as jnp
from jax import lax
from jax.experimental import pallas as pl
from jax.experimental.pallas import tpu as pltpu
from jax.sharding import PartitionSpec as P


D = 4096
HS = 128


rope_base = 500000.0
norm_eps = 1e-06
score_scale = HS ** (-0.5)
scale2 = score_scale * 1.4426950408889634


def rotate(values, positions, head_size):
    half_size = head_size // 2
    frequency = rope_base ** (-jnp.arange(half_size, dtype=jnp.float32) * 2.0 / head_size)
    angles = positions.astype(jnp.float32)[:, None] * frequency[None, :]
    cosine = jnp.cos(angles)[:, None, :]
    sine_part = jnp.sin(angles)[:, None, :]
    first_half = values[..., :half_size]
    second = values[..., half_size:]
    return jnp.concatenate(
        [first_half * cosine - second * sine_part, second * cosine + first_half * sine_part],
        axis=-1,
    )


def online_update(s, v, m_sc, l_sc, acc_sc):
    m_prev = m_sc[...]
    m_cur = jnp.max(s, axis=1, keepdims=True) * scale2
    m_next = jnp.maximum(m_prev, m_cur)
    alpha = jnp.exp2(m_prev - m_next)
    p = jnp.exp2(s * scale2 - m_next[:, :1])
    l_sc[...] = alpha * l_sc[...] + jnp.sum(p, axis=1, keepdims=True)
    pv = jnp.dot(p.astype(jnp.bfloat16), v, preferred_element_type=jnp.float32)
    acc_sc[...] = acc_sc[...] * alpha + pv
    m_sc[...] = m_next


def scores_of(q, k):
    return lax.dot_general(q, k, (((1,), (1,)), ((), ())), preferred_element_type=jnp.float32)


def new_kernel(meta_ref, q_ref, k_ref, v_ref, *rest, partner):
    if partner:
        acc_in, m_in, l_in, acc_out, m_out, l_out, m_sc, l_sc, acc_sc = rest
    else:
        acc_out, m_out, l_out, m_sc, l_sc, acc_sc = rest
    qi = pl.program_id(1)
    kj = pl.program_id(2)
    member = meta_ref[0]
    q_chunk = jnp.where(qi == 0, member, 3 - member)
    if partner:
        k_chunk = jnp.where(kj == 0, 1 - member, 2 + member)
    else:
        k_chunk = jnp.where(kj == 0, member, 3 - member)

    @pl.when(kj == 0)
    def _():
        if partner:
            m_sc[...] = m_in[...]
            l_sc[...] = l_in[...]
            acc_sc[...] = acc_in[...]
        else:
            m_sc[...] = jnp.full(m_sc.shape, -jnp.inf, jnp.float32)
            l_sc[...] = jnp.zeros(l_sc.shape, jnp.float32)
            acc_sc[...] = jnp.zeros(acc_sc.shape, jnp.float32)

    @pl.when(k_chunk <= q_chunk)
    def _():
        s = scores_of(q_ref[...], k_ref[...])
        rows = lax.broadcasted_iota(jnp.int32, s.shape, 0)
        cols = lax.broadcasted_iota(jnp.int32, s.shape, 1)
        s = jnp.where((k_chunk < q_chunk) | (cols <= rows), s, -jnp.inf)
        online_update(s, v_ref[...], m_sc, l_sc, acc_sc)

    @pl.when(kj == pl.num_programs(2) - 1)
    def _():
        acc_out[...] = acc_sc[...]
        m_out[...] = m_sc[...]
        l_out[...] = l_sc[...]


def cached_kernel(meta_ref, q_ref, pk_ref, pv_ref, k_ref, v_ref, acc_in, m_in, l_in, o_ref,
                  m_sc, l_sc, acc_sc, *, groups, block_len):
    c = pl.program_id(1)
    length = meta_ref[1]
    first = meta_ref[2]
    tile = groups * block_len
    member = meta_ref[0]
    half = q_ref.shape[0] // 2

    @pl.when(c == 0)
    def _():
        m_sc[...] = m_in[...]
        l_sc[...] = l_in[...]
        acc_sc[...] = acc_in[...]

    @pl.when((c == 0) & (member == 0))
    def _():
        s = scores_of(q_ref[pl.ds(half, half), :], pk_ref[0])
        online_update(
            s, pv_ref[0], m_sc.at[pl.ds(half, half)], l_sc.at[pl.ds(half, half)],
            acc_sc.at[pl.ds(half, half)],
        )

    @pl.when((c == 0) & (member != 0))
    def _():
        s = scores_of(q_ref[...], pk_ref[0, pl.ds(0, half), :])
        online_update(s, pv_ref[0, pl.ds(0, half), :], m_sc, l_sc, acc_sc)

    @pl.when((c + 1) * groups * block_len <= length)
    def _():
        k = k_ref[...].reshape(tile, HS)
        v = v_ref[...].reshape(tile, HS)
        s = scores_of(q_ref[...], k)
        online_update(s, v, m_sc, l_sc, acc_sc)

    @pl.when((c * groups * block_len < length) & ((c + 1) * groups * block_len > length))
    def _():
        k = k_ref[...].reshape(tile, HS)
        v = v_ref[...].reshape(tile, HS)
        s = scores_of(q_ref[...], k)
        cols = lax.broadcasted_iota(jnp.int32, (1, tile), 1)
        src = cols // block_len
        block = (src - first + groups) % groups + groups * c
        visible = block * block_len + cols % block_len < length
        s = jnp.where(visible, s, -jnp.inf)
        online_update(s, v, m_sc, l_sc, acc_sc)

    @pl.when(c == pl.num_programs(1) - 1)
    def _():
        o_ref[...] = (acc_sc[...] / l_sc[...]).astype(o_ref.dtype)


def new_attention(meta, queries, keys, values, state=None):
    tok_rows, width = queries.shape
    heads = width // HS
    q_rows = tok_rows // 2
    key_rows = keys.shape[0]
    k_tiles = key_rows // q_rows
    partner = state is not None
    shape = jax.ShapeDtypeStruct((tok_rows, width), jnp.float32)
    state_spec = pl.BlockSpec((q_rows, HS), lambda h, i, j, meta: (i, h))
    in_specs = [
        pl.BlockSpec((q_rows, HS), lambda h, i, j, meta: (i, h)),
        pl.BlockSpec((q_rows, HS), lambda h, i, j, meta: (j, h)),
        pl.BlockSpec((q_rows, HS), lambda h, i, j, meta: (j, h)),
    ]
    operands = [meta, queries, keys, values]
    if partner:
        in_specs += [state_spec] * 3
        operands += list(state)
    return pl.pallas_call(
        functools.partial(new_kernel, partner=partner),
        out_shape=(shape, shape, shape),
        grid_spec=pltpu.PrefetchScalarGridSpec(
            num_scalar_prefetch=1,
            grid=(heads, 2, k_tiles),
            in_specs=in_specs,
            out_specs=[state_spec, state_spec, state_spec],
            scratch_shapes=[
                pltpu.VMEM((q_rows, HS), jnp.float32),
                pltpu.VMEM((q_rows, HS), jnp.float32),
                pltpu.VMEM((q_rows, HS), jnp.float32),
            ],
        ),
        compiler_params=pltpu.CompilerParams(
            dimension_semantics=("arbitrary", "arbitrary", "arbitrary")
        ),
        cost_estimate=pl.CostEstimate(
            flops=2 * 2 * tok_rows * key_rows * width * 3 // 4,
            transcendentals=tok_rows * key_rows * heads * 3 // 4,
            bytes_accessed=2 * tok_rows * width + 2 * 2 * key_rows * width + 6 * 4 * tok_rows * width,
        ),
    )(*operands)


def cached_attention(meta, queries, partner_new, received, acc, m, l):
    tok_rows, width = queries.shape
    heads = width // HS
    groups, _, per_dev, block_len, _ = received.shape

    def kv_map(index):
        def index_map(h, c, meta):
            last = (meta[1] + groups * block_len - 1) // (groups * block_len) - 1
            return (0, index, jnp.minimum(c, last), 0, h)

        return index_map

    kv_block = (groups, None, None, block_len, HS)
    state_spec = pl.BlockSpec((tok_rows, HS), lambda h, c, meta: (0, h))
    keys_total = groups * per_dev * block_len
    return pl.pallas_call(
        functools.partial(
            cached_kernel, groups=groups, block_len=block_len
        ),
        out_shape=jax.ShapeDtypeStruct((tok_rows, width), jnp.bfloat16),
        grid_spec=pltpu.PrefetchScalarGridSpec(
            num_scalar_prefetch=1,
            grid=(heads, per_dev),
            in_specs=[
                pl.BlockSpec((tok_rows, HS), lambda h, c, meta: (0, h)),
                pl.BlockSpec((1, tok_rows, HS), lambda h, c, meta: (0, 0, h)),
                pl.BlockSpec((1, tok_rows, HS), lambda h, c, meta: (1, 0, h)),
                pl.BlockSpec(kv_block, kv_map(0)),
                pl.BlockSpec(kv_block, kv_map(1)),
                state_spec,
                state_spec,
                state_spec,
            ],
            out_specs=pl.BlockSpec((tok_rows, HS), lambda h, c, meta: (0, h)),
            scratch_shapes=[
                pltpu.VMEM((tok_rows, HS), jnp.float32),
                pltpu.VMEM((tok_rows, HS), jnp.float32),
                pltpu.VMEM((tok_rows, HS), jnp.float32),
            ],
        ),
        compiler_params=pltpu.CompilerParams(dimension_semantics=("arbitrary", "arbitrary")),
        cost_estimate=pl.CostEstimate(
            flops=2 * 2 * tok_rows * keys_total * width // 2,
            transcendentals=tok_rows * keys_total * heads // 2,
            bytes_accessed=2 * keys_total * width + 2 * tok_rows * width * 2 + 3 * 4 * tok_rows * width,
        ),
    )(meta, queries, partner_new, partner_new, received, received, acc, m, l)


def copy_kernel(src_ref, dst_ref):
    dst_ref[...] = src_ref[...]


def cache_copy(cache):
    kinds, slots, rows, width = cache.shape
    step = 8
    spec = pl.BlockSpec((1, step, rows, width), lambda k, i: (k, i, 0, 0))
    return pl.pallas_call(
        copy_kernel,
        out_shape=jax.ShapeDtypeStruct(cache.shape, cache.dtype),
        grid=(kinds, slots // step),
        in_specs=[spec],
        out_specs=spec,
        cost_estimate=pl.CostEstimate(flops=0, transcendentals=0, bytes_accessed=2 * cache.size * 2),
    )(cache)


def place_kernel(ids_ref, blocks_ref, base_ref, out_ref, sems):
    del base_ref
    count = blocks_ref.shape[0]
    copies = [
        pltpu.make_async_copy(blocks_ref.at[i], out_ref.at[ids_ref[i]], sems.at[i])
        for i in range(count)
    ]
    for copy in copies:
        copy.start()
    for copy in copies:
        copy.wait()


def place_blocks(ids, blocks, base):
    count = blocks.shape[0]
    return pl.pallas_call(
        place_kernel,
        out_shape=jax.ShapeDtypeStruct(base.shape, base.dtype),
        grid_spec=pltpu.PrefetchScalarGridSpec(
            num_scalar_prefetch=1,
            grid=(),
            in_specs=[pl.BlockSpec(memory_space=pl.ANY), pl.BlockSpec(memory_space=pl.ANY)],
            out_specs=pl.BlockSpec(memory_space=pl.ANY),
            scratch_shapes=[pltpu.SemaphoreType.DMA((count,))],
        ),
        input_output_aliases={2: 0},
    )(ids, blocks, base)


def body(states, qkv_weight, norm_gains, kv_cache, cached_len, old_table, new_table):
    tok_rows = states.shape[0]
    half_rows = tok_rows // 2
    local_width = qkv_weight.shape[2]
    local_heads = local_width // HS
    pair = lax.axis_size("bp")
    groups = lax.axis_size("bx") * pair
    slot_count = kv_cache.shape[1]
    block_len = kv_cache.shape[2]
    per_dev = old_table.shape[1] // groups
    request = lax.axis_index("bx")
    member = lax.axis_index("bp")
    my_index = request * pair + member
    late_block = 2 * pair - 1 - member
    targets = jnp.arange(groups, dtype=jnp.int32)
    kv_ids = jnp.arange(2, dtype=jnp.int32)
    kv_flat = kv_cache.reshape(2 * slot_count, block_len, local_width)

    first_dev = old_table[:, 0] // slot_count
    target_req = targets // pair
    c_index = jnp.arange(per_dev, dtype=jnp.int32)
    block_index = ((my_index - first_dev[target_req]) % groups)[:, None] + groups * c_index[None, :]
    slot_index = (
        old_table[target_req[:, None], jnp.clip(block_index, 0, old_table.shape[1] - 1)]
        - my_index * slot_count
    )
    slot_index = jnp.clip(slot_index, 0, slot_count - 1)
    out_ids = kv_ids[None, :, None] * slot_count + slot_index[:, None, :]
    outgoing = jnp.take(kv_flat, out_ids.reshape(-1), axis=0, mode="clip").reshape(
        groups, 2, per_dev, block_len, local_width
    )
    received = lax.all_to_all(
        outgoing, ("bx", "bp"), split_axis=0, concat_axis=0, tiled=True
    )

    projected = jnp.einsum(
        "tc,jcw->tjw",
        lax.all_gather(states, "head", axis=1, tiled=True),
        qkv_weight,
        preferred_element_type=jnp.float32,
    )
    queries = projected[:, 0]
    key_new = projected[:, 1]
    value_new = projected[:, 2]
    query_sq, key_sq = lax.psum(
        (jnp.sum(queries * queries, axis=1), jnp.sum(key_new * key_new, axis=1)), "head"
    )
    gains = norm_gains.astype(jnp.float32)
    queries = queries * lax.rsqrt(query_sq / D + norm_eps)[:, None] * gains[0]
    key_new = key_new * lax.rsqrt(key_sq / D + norm_eps)[:, None] * gains[1]
    half_ids = jnp.arange(half_rows, dtype=jnp.int32)
    token_offset = jnp.concatenate(
        [member * half_rows + half_ids, late_block * half_rows + half_ids]
    )
    positions = cached_len[request] + token_offset
    queries = (
        rotate(queries.reshape(tok_rows, local_heads, HS), positions, HS)
        .reshape(tok_rows, local_width)
        .astype(jnp.bfloat16)
    )
    key_new = (
        rotate(key_new.reshape(tok_rows, local_heads, HS), positions, HS)
        .reshape(tok_rows, local_width)
        .astype(jnp.bfloat16)
    )
    value_new = value_new.astype(jnp.bfloat16)
    fresh_kv = jnp.stack([key_new, value_new])
    meta = jnp.stack([member, cached_len[request], first_dev[request], 0]).astype(jnp.int32)

    partner_new = lax.ppermute(fresh_kv, "bp", [(0, 1), (1, 0)])
    state = new_attention(meta, queries, fresh_kv[0], fresh_kv[1])

    blocks_dev = tok_rows // block_len
    chunk_blocks = blocks_dev // 2
    new_home = new_table[:, 0] // slot_count
    pair_index = jnp.arange(2, dtype=jnp.int32)
    reqs = jnp.arange(groups // pair, dtype=jnp.int32)
    dest = reqs * pair + member
    wanted_out = 2 * ((dest - new_home[request]) % groups)[:, None] + pair_index[None, :]
    chunk = wanted_out // chunk_blocks
    within = wanted_out % chunk_blocks
    own_place = jnp.where(chunk == member, 0, 1) * chunk_blocks + within
    partner_place = jnp.where(chunk == 1 - member, 0, 1) * chunk_blocks + within
    is_own = (chunk == member) | (chunk == 3 - member)

    def pick(source, place):
        ids = kv_ids[None, :, None] * blocks_dev + place[:, None, :]
        return jnp.take(
            source.reshape(2 * blocks_dev, block_len, local_width), ids.reshape(-1), axis=0,
            mode="clip",
        ).reshape(groups // pair, 2, 2, block_len, local_width)

    picked = jnp.where(
        is_own[:, None, :, None, None], pick(fresh_kv, own_place), pick(partner_new, partner_place)
    )
    arrived = lax.all_to_all(picked, "bx", split_axis=0, concat_axis=0, tiled=True)
    wanted_in = 2 * ((my_index - new_home) % groups)[:, None] + pair_index[None, :]
    target_slot = (
        new_table[reqs[:, None], jnp.clip(wanted_in, 0, new_table.shape[1] - 1)]
        - my_index * slot_count
    )
    target_ids = kv_ids[None, :, None] * slot_count + target_slot[:, None, :]
    base = cache_copy(kv_cache).reshape(kv_flat.shape)
    updated_cache = place_blocks(
        target_ids.reshape(-1), arrived.reshape(-1, block_len, local_width), base
    ).reshape(kv_cache.shape)

    attended = cached_attention(meta, queries, partner_new, received, *state)
    return (attended, updated_cache)


def solution(mesh):
    heads, groups = mesh.devices.shape
    split = jax.sharding.Mesh(mesh.devices.reshape(heads, groups // 2, 2), ("head", "bx", "bp"))
    blk = ("bx", "bp")
    return jax.shard_map(
        body,
        mesh=split,
        in_specs=(
            P(blk, "head"),
            P(None, None, "head"),
            P(None, "head"),
            P(None, blk, None, "head"),
            P(),
            P(),
            P(),
        ),
        out_specs=(P(blk, "head"), P(None, blk, None, "head")),
        check_vma=False,
    )
```
